32 devices in a mesh: tm: 8 (over y, x, core), space: 4 (over z).
Axes of the slice: x: 2, y: 2, z: 4, core: 2. Of those that a mesh axis runs over, the one named last changes fastest.
Arguments:
- starts: float32 [8, 32, 128, 128], P('tm', 'space'), may hold values from -6 to 6
- diffusivity: float32 [32, 128, 128], P('space'), may hold values from 0.04 to 0.2
- velocity: float32 [2, 32, 128, 128], P(None, 'space'), may hold values from -0.1 to 0.1
- obstacle: int32 [32, 128, 128], P('space'), may hold values from 0 to 1, as said below
- substep_scale: float32 [12], replicated, may hold values from 0.5 to 1
- neighbors: int32 [32, 4], P('space'), may hold values from 0 to 32, as said below
- coarse_x: float32 [32, 64, 64], P('space'), may hold values from -1 to 1
- coarse_y: float32 [32, 128, 128], P('space'), may hold values from -1 to 1
Outputs:
- slice_ends: float32 [8, 32, 128, 128], P('tm', 'space')
- increment: float32 [8, 32, 128, 128], P('tm', 'space')
The draws below stay inside these ranges and needn't reach their ends.
Inputs may be any that keep to these rules, and one draw needn't show every extreme that they name: `neighbors`: tiles form a grid of 4 by 8; each entry names the tile beside a tile in the given direction, or 32 on the grid's edge. The tiles 8 * k to 8 * (k + 1) - 1 fill grid row k, in any order within it, so a neighbour's number differs from the tile's block k by at most one block. `obstacle`: each tile holds one tube, a disc of radius 128 // 8 to 32 cells.
All inputs are finite; a program needn't handle non-finite values.
Results may differ from the reference program's by a relative error of at most 0.0002.
Values sent between devices are 32-bit elements; how exact they have to be, the bound alone decides.
No kernel may reach another device: no remote copies, remote signals or barrier semaphores. Data moves between devices by JAX's collectives and lax.ppermute only.
A program may use at most 128 MiB of HBM per device.

```python
import math
import jax
import jax.numpy as jnp
from jax import lax

TILES_DEV = 8
TILE = 128
TGY = 8
SUB = 12
CX = 64
SLICES = 8
TILES = 32


def coarse_inverse(key, matrix_order):
    key_rate, key_mix = jax.random.split(key)
    low_rate = 0.2
    high_rate = 20.0
    rates = jnp.exp(jax.random.uniform(key_rate, (TILES, matrix_order), jnp.float32, math.log(low_rate), math.log(high_rate)))
    damping = 1.0 - 0.15 / math.sqrt(matrix_order)
    diagonal_part = jnp.exp(-rates / SLICES) * damping
    mixing = jax.random.uniform(key_mix, (TILES, matrix_order, matrix_order), jnp.float32, -1.0, 1.0)
    mixing = 0.15 * (mixing + jnp.swapaxes(mixing, 1, 2)) / (2.0 * matrix_order)
    identity_mask = jnp.eye(matrix_order, dtype=jnp.float32)
    return mixing * (1.0 - identity_mask) + identity_mask * diagonal_part[:, :, None]


def draw_coarse_x(key, part):
    return coarse_inverse(jax.random.fold_in(key, 1), CX)


def draw_coarse_y(key, part):
    return coarse_inverse(jax.random.fold_in(key, 2), TILE)


def draw_obstacle(key, part):
    key_first, key_second, key_radius = jax.random.split(jax.random.fold_in(key, 3), 3)
    centre_x = jax.random.randint(key_first, (TILES, 1, 1), TILE // 4, 3 * TILE // 4)
    centre_y = jax.random.randint(key_second, (TILES, 1, 1), TILE // 4, 3 * TILE // 4)
    radius = jax.random.randint(key_radius, (TILES, 1, 1), TILE // 8, TILE // 4 + 1)
    row_index = jnp.arange(TILE, dtype=jnp.int32)[None, :, None]
    col_index = jnp.arange(TILE, dtype=jnp.int32)[None, None, :]
    distance = (row_index - centre_x) ** 2 + (col_index - centre_y) ** 2
    return (distance <= radius * radius).astype(jnp.int32)


def draw_neighbors(key, part):
    block_count = TILES // TILES_DEV
    block_keys = jax.random.split(jax.random.fold_in(key, 4), block_count)
    within = jax.vmap(lambda block_key: jax.random.permutation(block_key, TILES_DEV))(block_keys).astype(jnp.int32)
    block_base = (jnp.arange(block_count, dtype=jnp.int32) * TILES_DEV)[:, None]
    ordering = (within + block_base).reshape(TILES).astype(jnp.int32)
    placing = jnp.zeros((TILES,), jnp.int32).at[ordering].set(jnp.arange(TILES, dtype=jnp.int32))
    grid_rows = TILES // TGY
    grid_x = placing // TGY
    grid_y = placing % TGY

    def lookup(target_x, target_y, usable):
        flat_place = jnp.clip(target_x * TGY + target_y, 0, TILES - 1)
        return jnp.where(usable, ordering[flat_place], TILES).astype(jnp.int32)
    west_tile = lookup(grid_x - 1, grid_y, grid_x > 0)
    east_tile = lookup(grid_x + 1, grid_y, grid_x < grid_rows - 1)
    south_tile = lookup(grid_x, grid_y - 1, grid_y > 0)
    north_tile = lookup(grid_x, grid_y + 1, grid_y < TGY - 1)
    return jnp.stack([west_tile, east_tile, south_tile, north_tile], axis=1)


def block_levels(rng, dims, shards, least, top_value):
    factor_of = 1.0
    for axis_at, shards_of in shards:
        heights = jax.random.uniform(jax.random.fold_in(jax.random.fold_in(rng, 6), axis_at), (shards_of,), jnp.float32, least / len(shards), top_value / len(shards))
        factor_of = factor_of * jnp.repeat(jnp.exp(heights), dims[axis_at] // shards_of).reshape((-1,) + (1,) * (len(dims) - 1 - axis_at))
    return factor_of


def noise(stream_key, dims, width, bound, cuts=(), kind=jnp.bfloat16):
    values = jax.random.normal(stream_key, dims, jnp.float32) * width
    if len(cuts) > 0:
        values = block_levels(stream_key, dims, cuts, -0.22, 0.18) * values
    return jnp.clip(values, min=-bound, max=bound).astype(kind)


def setup_inputs(seed: int = 0) -> dict:
    keys = jax.random.split(jax.random.key(seed), 9)
    starts = noise(keys[0], (SLICES, TILES, TILE, TILE), 1.0, 6.0, ((0, 8), (1, 4)), jnp.float32)
    diffusivity = jnp.clip(jnp.exp(math.log(0.2) - 1.609438 * jax.random.uniform(keys[1], (TILES, TILE, TILE), jnp.float32) ** block_levels(keys[1], (TILES, TILE, TILE), ((0, 4),), -0.2, 0.2)), 0.04, 0.2)
    velocity = jnp.clip(jax.random.uniform(keys[2], (2, TILES, TILE, TILE), jnp.float32, -0.1, 0.1) * block_levels(keys[2], (2, TILES, TILE, TILE), ((1, 4),), -0.4, 0.0), -0.1, 0.1)
    obstacle = draw_obstacle(jax.random.fold_in(keys[8], 71), 0)
    substep_scale = jnp.clip(jnp.exp(jax.random.uniform(keys[4], (SUB,), jnp.float32, math.log(0.5), math.log(1.0))), 0.5, 1.0)
    neighbors = draw_neighbors(jax.random.fold_in(keys[8], 71), 0)
    coarse_x = draw_coarse_x(jax.random.fold_in(keys[8], 71), 0)
    coarse_y = draw_coarse_y(jax.random.fold_in(keys[8], 71), 0)
    return dict(starts=starts, diffusivity=diffusivity, velocity=velocity, obstacle=obstacle, substep_scale=substep_scale, neighbors=neighbors, coarse_x=coarse_x, coarse_y=coarse_y)


exact_precision = lax.Precision.HIGHEST


def restrict(values):
    return 0.5 * (values[..., 0::2, :] + values[..., 1::2, :])


def prolong(coarse_values):
    return jnp.repeat(coarse_values, 2, axis=-2)


def apply_coarse(coarse_values, matrix_x, matrix_y):
    mixed_x = jnp.einsum("tij,...tjk->...tik", matrix_x, coarse_values, precision=exact_precision)
    return jnp.einsum("...tik,tlk->...til", mixed_x, matrix_y, precision=exact_precision)


def fine_propagate(start_state, diffusivity, speed_x, speed_y, open_cells, substep_scale, neighbors):
    def advance(current, strength):
        own_faces = jnp.stack([current[:, 0, :], current[:, -1, :], current[:, :, 0], current[:, :, -1]], axis=1)
        padded_faces = jnp.concatenate([own_faces, jnp.zeros_like(own_faces[:1])], axis=0)
        west_face = padded_faces[neighbors[:, 0], 1]
        east_face = padded_faces[neighbors[:, 1], 0]
        south_face = padded_faces[neighbors[:, 2], 3]
        north_face = padded_faces[neighbors[:, 3], 2]
        from_west = jnp.concatenate([west_face[:, None, :], current[:, :-1, :]], axis=1)
        from_east = jnp.concatenate([current[:, 1:, :], east_face[:, None, :]], axis=1)
        from_south = jnp.concatenate([south_face[:, :, None], current[:, :, :-1]], axis=2)
        from_north = jnp.concatenate([current[:, :, 1:], north_face[:, :, None]], axis=2)
        laplace = from_west + from_east + from_south + from_north - 4.0 * current
        transport = speed_x * (from_east - from_west) + speed_y * (from_north - from_south)
        updated = open_cells * (current + strength * diffusivity * laplace - 0.5 * transport)
        return updated, None

    final_state, unused = lax.scan(advance, start_state, substep_scale)
    return final_state


def reference(starts, diffusivity, velocity, obstacle, substep_scale, neighbors, coarse_x, coarse_y):
    open_cells = 1.0 - obstacle.astype(jnp.float32)
    fine_ends = lax.map(lambda start_state: fine_propagate(start_state, diffusivity, velocity[0], velocity[1], open_cells, substep_scale, neighbors), starts)
    correction = fine_ends - prolong(apply_coarse(restrict(starts), coarse_x, coarse_y))
    coarse_jump = restrict(correction)

    def sweep(state_now, jump):
        return apply_coarse(state_now, coarse_x, coarse_y) + jump, state_now

    last_state, coarse_states = lax.scan(sweep, restrict(starts[0]), coarse_jump)
    slice_ends = prolong(apply_coarse(coarse_states, coarse_x, coarse_y)) + correction
    next_starts = jnp.concatenate([starts[:1], slice_ends[:-1]], axis=0)
    return slice_ends, next_starts - starts
```

```python
import jax
import jax.numpy as jnp
from jax import lax
from jax.experimental import pallas as pl
from jax.experimental.pallas import tpu as pltpu
from jax.sharding import PartitionSpec as P

SUB = 12
HALO = 16


exact_precision = lax.Precision.HIGHEST


def spread(value, axis, source):
    kept = jnp.where(lax.axis_index(axis) == source, value, 0).astype(value.dtype)
    return lax.psum(kept, axis)


def passed_along(block, axis, distance):
    devices = range(lax.axis_size(axis))
    route = [(i - distance, i) for i in devices if i - distance in devices]
    return lax.ppermute(block, axis, route)


def restrict(values):
    return 0.5 * (values[..., 0::2, :] + values[..., 1::2, :])


def prolong(coarse_values):
    return jnp.repeat(coarse_values, 2, axis=-2)


def apply_coarse(coarse_values, matrix_x, matrix_y):
    mixed_x = jnp.einsum("tij,...tjk->...tik", matrix_x, coarse_values, precision=exact_precision)
    return jnp.einsum("...tik,tlk->...til", mixed_x, matrix_y, precision=exact_precision)


def fine_kernel(south_ref, north_ref, south_ok_ref, north_ok_ref, scale_ref,
                u_ref, fields_ref, west_ref, east_ref, out_ref, state_ref, field_ref):
    tiles = u_ref.shape[0]
    rows = u_ref.shape[1]
    total = rows + 2 * HALO
    for i in range(tiles):
        state_ref[0, i, pl.ds(0, HALO), :] = west_ref[0, i]
        state_ref[0, i, pl.ds(HALO, rows), :] = u_ref[i]
        state_ref[0, i, pl.ds(HALO + rows, HALO), :] = east_ref[0, i]
        for f in range(4):
            field_ref[f, i, pl.ds(0, HALO), :] = west_ref[f + 1, i]
            field_ref[f, i, pl.ds(HALO, rows), :] = fields_ref[f, i]
            field_ref[f, i, pl.ds(HALO + rows, HALO), :] = east_ref[f + 1, i]

    lanes = u_ref.shape[2]
    lane = lax.broadcasted_iota(jnp.int32, (total, lanes), 1)
    first_lane = lane == 0
    last_lane = lane == lanes - 1

    def substep(s, carry):
        src = s % 2
        dst = 1 - src
        strength = scale_ref[s]
        for i in range(tiles):
            current = state_ref[src, i]
            south_tile = state_ref[src, south_ref[i]]
            north_tile = state_ref[src, north_ref[i]]
            south_edge = jnp.where(south_ok_ref[i] > 0, pltpu.roll(south_tile, 1, 1), 0.0)
            north_edge = jnp.where(north_ok_ref[i] > 0, pltpu.roll(north_tile, lanes - 1, 1), 0.0)
            from_west = pltpu.roll(current, 1, 0)
            from_east = pltpu.roll(current, total - 1, 0)
            from_south = jnp.where(first_lane, south_edge, pltpu.roll(current, 1, 1))
            from_north = jnp.where(last_lane, north_edge, pltpu.roll(current, lanes - 1, 1))
            diffusivity = field_ref[0, i]
            speed_x = field_ref[1, i]
            speed_y = field_ref[2, i]
            open_cells = field_ref[3, i]
            laplace = from_west + from_east + from_south + from_north - 4.0 * current
            transport = speed_x * (from_east - from_west) + speed_y * (from_north - from_south)
            state_ref[dst, i] = open_cells * (
                current + strength * diffusivity * laplace - 0.5 * transport
            )
        return carry

    lax.fori_loop(0, SUB, substep, 0)
    last = SUB % 2
    for i in range(tiles):
        out_ref[i] = state_ref[last, i, pl.ds(HALO, rows), :]


def fine_propagate(u, fields, west, east, south, north, south_ok, north_ok, scale):
    tiles, rows, lanes = u.shape
    total = rows + 2 * HALO
    vmem = pltpu.MemorySpace.VMEM
    smem = pltpu.MemorySpace.SMEM
    return pl.pallas_call(
        fine_kernel,
        out_shape=jax.ShapeDtypeStruct(u.shape, u.dtype),
        in_specs=[pl.BlockSpec(memory_space=smem)] * 5 + [pl.BlockSpec(memory_space=vmem)] * 4,
        out_specs=pl.BlockSpec(memory_space=vmem),
        scratch_shapes=[
            pltpu.VMEM((2, tiles, total, lanes), jnp.float32),
            pltpu.VMEM((4, tiles, total, lanes), jnp.float32),
        ],
        compiler_params=pltpu.CompilerParams(vmem_limit_bytes=48 * 1024 * 1024),
    )(south, north, south_ok, north_ok, scale, u, fields, west, east)


def on_device(
    starts, diffusivity, velocity, obstacle, substep_scale, neighbors, coarse_x, coarse_y
):
    slice_count = starts.shape[0]
    tile_count = starts.shape[1]
    rows = starts.shape[2]
    all_tiles = tile_count * lax.axis_size("space")
    block_base = lax.axis_index("space") * tile_count
    open_cells = 1.0 - obstacle.astype(jnp.float32)

    fields = jnp.stack([diffusivity, velocity[0], velocity[1], open_cells], axis=0)
    layers = jnp.concatenate([starts, fields], axis=0)
    space_count = lax.axis_size("space")
    forward = [(i, i + 1) for i in range(space_count - 1)]
    backward = [(i + 1, i) for i in range(space_count - 1)]
    from_prev = lax.ppermute(layers[:, :, rows - HALO:, :], "space", forward)
    from_next = lax.ppermute(layers[:, :, :HALO, :], "space", backward)
    zero_tile = jnp.zeros_like(from_prev[:, :1])
    from_prev = jnp.concatenate([from_prev, zero_tile], axis=1)
    from_next = jnp.concatenate([from_next, zero_tile], axis=1)
    west_nb = neighbors[:, 0]
    east_nb = neighbors[:, 1]
    west_index = jnp.where(west_nb == all_tiles, tile_count, west_nb - (block_base - tile_count))
    east_index = jnp.where(east_nb == all_tiles, tile_count, east_nb - (block_base + tile_count))
    west_index = jnp.clip(west_index, 0, tile_count)
    east_index = jnp.clip(east_index, 0, tile_count)
    west = jnp.take(from_prev, west_index, axis=1)
    east = jnp.take(from_next, east_index, axis=1)

    south_nb = neighbors[:, 2]
    north_nb = neighbors[:, 3]
    south_ok = (south_nb != all_tiles).astype(jnp.int32)
    north_ok = (north_nb != all_tiles).astype(jnp.int32)
    south = jnp.clip(south_nb - block_base, 0, tile_count - 1) * south_ok
    north = jnp.clip(north_nb - block_base, 0, tile_count - 1) * north_ok

    fine_ends = jnp.stack(
        [
            fine_propagate(
                starts[n],
                fields,
                jnp.concatenate([west[n : n + 1], west[slice_count:]], axis=0),
                jnp.concatenate([east[n : n + 1], east[slice_count:]], axis=0),
                south,
                north,
                south_ok,
                north_ok,
                substep_scale,
            )
            for n in range(slice_count)
        ],
        axis=0,
    )
    correction = fine_ends - prolong(apply_coarse(restrict(starts), coarse_x, coarse_y))
    coarse_jump = restrict(correction)
    first_coarse = spread(restrict(starts[0]), "tm", 0)
    every_jump = lax.all_gather(coarse_jump, "tm", axis=0, tiled=True)

    def sweep(state_now, jump):
        return (apply_coarse(state_now, coarse_x, coarse_y) + jump, state_now)

    last_state, history = lax.scan(sweep, first_coarse, every_jump)
    own_coarse = lax.dynamic_slice_in_dim(
        history, lax.axis_index("tm") * slice_count, slice_count, 0
    )
    slice_ends = prolong(apply_coarse(own_coarse, coarse_x, coarse_y)) + correction
    previous = passed_along(slice_ends[-1], "tm", 1)
    first_step = jnp.where(
        lax.axis_index("tm") == 0, jnp.zeros_like(previous), previous - starts[0]
    )
    increment = jnp.concatenate([first_step[None], slice_ends[:-1] - starts[1:]], axis=0)
    return (slice_ends, increment)


def solution(mesh):
    placed = (
        P("tm", "space", None, None),
        P("space", None, None),
        P(None, "space", None, None),
        P("space", None, None),
        P(),
        P("space", None),
        P("space", None, None),
        P("space", None, None),
    )
    return jax.shard_map(
        on_device,
        mesh=mesh,
        in_specs=placed,
        out_specs=(P("tm", "space", None, None), P("tm", "space", None, None)),
        check_vma=False,
    )
```

```python
import jax
import jax.numpy as jnp
from jax import lax
from jax.experimental import pallas as pl
from jax.experimental.pallas import tpu as pltpu
from jax.sharding import PartitionSpec as P

SUB = 12
HALO = 16


exact_precision = lax.Precision.HIGHEST


def spread(value, axis, source):
    kept = jnp.where(lax.axis_index(axis) == source, value, 0).astype(value.dtype)
    return lax.psum(kept, axis)


def passed_along(block, axis, distance):
    devices = range(lax.axis_size(axis))
    route = [(i - distance, i) for i in devices if i - distance in devices]
    return lax.ppermute(block, axis, route)


def restrict(values):
    return 0.5 * (values[..., 0::2, :] + values[..., 1::2, :])


def prolong(coarse_values):
    return jnp.repeat(coarse_values, 2, axis=-2)


def apply_coarse(coarse_values, matrix_x, matrix_y):
    mixed_x = jnp.einsum("tij,...tjk->...tik", matrix_x, coarse_values, precision=exact_precision)
    return jnp.einsum("...tik,tlk->...til", mixed_x, matrix_y, precision=exact_precision)


def fine_kernel(south_ref, north_ref, south_ok_ref, north_ok_ref, scale_ref,
                u_ref, fields_ref, west_ref, east_ref, out_ref, state_ref, field_ref):
    tiles = u_ref.shape[0]
    rows = u_ref.shape[1]
    total = rows + 2 * HALO
    for i in range(tiles):
        state_ref[0, i, pl.ds(0, HALO), :] = west_ref[0, i]
        state_ref[0, i, pl.ds(HALO, rows), :] = u_ref[i]
        state_ref[0, i, pl.ds(HALO + rows, HALO), :] = east_ref[0, i]
        for f in range(4):
            field_ref[f, i, pl.ds(0, HALO), :] = west_ref[f + 1, i]
            field_ref[f, i, pl.ds(HALO, rows), :] = fields_ref[f, i]
            field_ref[f, i, pl.ds(HALO + rows, HALO), :] = east_ref[f + 1, i]

    lanes = u_ref.shape[2]
    lane = lax.broadcasted_iota(jnp.int32, (total, lanes), 1)
    first_lane = lane == 0
    last_lane = lane == lanes - 1

    def substep(s, carry):
        src = s % 2
        dst = 1 - src
        strength = scale_ref[s]
        for i in range(tiles):
            current = state_ref[src, i]
            south_tile = state_ref[src, south_ref[i]]
            north_tile = state_ref[src, north_ref[i]]
            south_edge = jnp.where(south_ok_ref[i] > 0, pltpu.roll(south_tile, 1, 1), 0.0)
            north_edge = jnp.where(north_ok_ref[i] > 0, pltpu.roll(north_tile, lanes - 1, 1), 0.0)
            from_west = pltpu.roll(current, 1, 0)
            from_east = pltpu.roll(current, total - 1, 0)
            from_south = jnp.where(first_lane, south_edge, pltpu.roll(current, 1, 1))
            from_north = jnp.where(last_lane, north_edge, pltpu.roll(current, lanes - 1, 1))
            diffusivity = field_ref[0, i]
            speed_x = field_ref[1, i]
            speed_y = field_ref[2, i]
            open_cells = field_ref[3, i]
            laplace = from_west + from_east + from_south + from_north - 4.0 * current
            transport = speed_x * (from_east - from_west) + speed_y * (from_north - from_south)
            state_ref[dst, i] = open_cells * (
                current + strength * diffusivity * laplace - 0.5 * transport
            )
        return carry

    lax.fori_loop(0, SUB, substep, 0)
    last = SUB % 2
    for i in range(tiles):
        out_ref[i] = state_ref[last, i, pl.ds(HALO, rows), :]


def fine_propagate(u, fields, west, east, south, north, south_ok, north_ok, scale):
    tiles, rows, lanes = u.shape
    total = rows + 2 * HALO
    vmem = pltpu.MemorySpace.VMEM
    smem = pltpu.MemorySpace.SMEM
    return pl.pallas_call(
        fine_kernel,
        out_shape=jax.ShapeDtypeStruct(u.shape, u.dtype),
        in_specs=[pl.BlockSpec(memory_space=smem)] * 5 + [pl.BlockSpec(memory_space=vmem)] * 4,
        out_specs=pl.BlockSpec(memory_space=vmem),
        scratch_shapes=[
            pltpu.VMEM((2, tiles, total, lanes), jnp.float32),
            pltpu.VMEM((4, tiles, total, lanes), jnp.float32),
        ],
        compiler_params=pltpu.CompilerParams(vmem_limit_bytes=48 * 1024 * 1024),
    )(south, north, south_ok, north_ok, scale, u, fields, west, east)


def on_device(
    starts, diffusivity, velocity, obstacle, substep_scale, neighbors, coarse_x, coarse_y
):
    slice_count = starts.shape[0]
    tile_count = starts.shape[1]
    rows = starts.shape[2]
    all_tiles = tile_count * lax.axis_size("space")
    block_base = lax.axis_index("space") * tile_count
    open_cells = 1.0 - obstacle.astype(jnp.float32)

    fields = jnp.stack([diffusivity, velocity[0], velocity[1], open_cells], axis=0)
    layers = jnp.concatenate([starts, fields], axis=0)
    space_count = lax.axis_size("space")
    forward = [(i, i + 1) for i in range(space_count - 1)]
    backward = [(i + 1, i) for i in range(space_count - 1)]
    from_prev = lax.ppermute(layers[:, :, rows - HALO:, :], "space", forward)
    from_next = lax.ppermute(layers[:, :, :HALO, :], "space", backward)
    zero_tile = jnp.zeros_like(from_prev[:, :1])
    from_prev = jnp.concatenate([from_prev, zero_tile], axis=1)
    from_next = jnp.concatenate([from_next, zero_tile], axis=1)
    west_nb = neighbors[:, 0]
    east_nb = neighbors[:, 1]
    west_index = jnp.where(west_nb == all_tiles, tile_count, west_nb - (block_base - tile_count))
    east_index = jnp.where(east_nb == all_tiles, tile_count, east_nb - (block_base + tile_count))
    west_index = jnp.clip(west_index, 0, tile_count)
    east_index = jnp.clip(east_index, 0, tile_count)
    west = jnp.take(from_prev, west_index, axis=1)
    east = jnp.take(from_next, east_index, axis=1)

    south_nb = neighbors[:, 2]
    north_nb = neighbors[:, 3]
    south_ok = (south_nb != all_tiles).astype(jnp.int32)
    north_ok = (north_nb != all_tiles).astype(jnp.int32)
    south = jnp.clip(south_nb - block_base, 0, tile_count - 1) * south_ok
    north = jnp.clip(north_nb - block_base, 0, tile_count - 1) * north_ok

    fine_ends = jnp.stack(
        [
            fine_propagate(
                starts[n],
                fields,
                jnp.concatenate([west[n : n + 1], west[slice_count:]], axis=0),
                jnp.concatenate([east[n : n + 1], east[slice_count:]], axis=0),
                south,
                north,
                south_ok,
                north_ok,
                substep_scale,
            )
            for n in range(slice_count)
        ],
        axis=0,
    )
    correction = fine_ends - prolong(apply_coarse(restrict(starts), coarse_x, coarse_y))
    coarse_jump = restrict(correction)
    tm_index = lax.axis_index("tm")
    tm_count = lax.axis_size("tm")
    shifted_jump = jnp.concatenate(
        [passed_along(coarse_jump[-1:], "tm", 1), coarse_jump[:-1]], axis=0
    )
    first_coarse = restrict(starts[:1])
    head = jnp.where(tm_index == 0, first_coarse, shifted_jump[:1])
    local = jnp.concatenate([head, shifted_jump[1:]], axis=0)

    states = [local[0]]
    for n in range(1, slice_count):
        states.append(apply_coarse(states[-1], coarse_x, coarse_y) + local[n])
    states = jnp.stack(states, axis=0)

    power_x = coarse_x
    power_y = coarse_y
    for n in range(1, slice_count):
        power_x = jnp.einsum("tij,tjk->tik", power_x, coarse_x, precision=exact_precision)
        power_y = jnp.einsum("tij,tjk->tik", power_y, coarse_y, precision=exact_precision)
    total = states[-1]
    distance = 1
    while distance < tm_count:
        received = passed_along(total, "tm", distance)
        total = total + jnp.where(
            tm_index >= distance, apply_coarse(received, power_x, power_y), 0.0
        )
        distance *= 2
        if distance < tm_count:
            power_x = jnp.einsum("tij,tjk->tik", power_x, power_x, precision=exact_precision)
            power_y = jnp.einsum("tij,tjk->tik", power_y, power_y, precision=exact_precision)
    if slice_count == 1:
        own_coarse = total[None]
    else:
        earlier = jnp.where(tm_index > 0, passed_along(total, "tm", 1), 0.0)
        own_coarse = []
        for n in range(slice_count):
            earlier = apply_coarse(earlier, coarse_x, coarse_y)
            own_coarse.append(states[n] + earlier)
        own_coarse = jnp.stack(own_coarse, axis=0)
    slice_ends = prolong(apply_coarse(own_coarse, coarse_x, coarse_y)) + correction
    previous = passed_along(slice_ends[-1], "tm", 1)
    first_step = jnp.where(
        lax.axis_index("tm") == 0, jnp.zeros_like(previous), previous - starts[0]
    )
    increment = jnp.concatenate([first_step[None], slice_ends[:-1] - starts[1:]], axis=0)
    return (slice_ends, increment)


def solution(mesh):
    placed = (
        P("tm", "space", None, None),
        P("space", None, None),
        P(None, "space", None, None),
        P("space", None, None),
        P(),
        P("space", None),
        P("space", None, None),
        P("space", None, None),
    )
    return jax.shard_map(
        on_device,
        mesh=mesh,
        in_specs=placed,
        out_specs=(P("tm", "space", None, None), P("tm", "space", None, None)),
        check_vma=False,
    )
```

```python
import functools

import jax
import jax.numpy as jnp
from jax import lax
from jax.experimental import pallas as pl
from jax.experimental.pallas import tpu as pltpu
from jax.sharding import PartitionSpec as P

SUB = 12
HALO = 16


exact_precision = lax.Precision.HIGHEST


def spread(value, axis, source):
    kept = jnp.where(lax.axis_index(axis) == source, value, 0).astype(value.dtype)
    return lax.psum(kept, axis)


def passed_along(block, axis, distance):
    devices = range(lax.axis_size(axis))
    route = [(i - distance, i) for i in devices if i - distance in devices]
    return lax.ppermute(block, axis, route)


def restrict(values):
    return 0.5 * (values[..., 0::2, :] + values[..., 1::2, :])


def prolong(coarse_values):
    return jnp.repeat(coarse_values, 2, axis=-2)


def apply_coarse(coarse_values, matrix_x, matrix_y):
    mixed_x = jnp.einsum("tij,...tjk->...tik", matrix_x, coarse_values, precision=exact_precision)
    return jnp.einsum("...tik,tlk->...til", mixed_x, matrix_y, precision=exact_precision)


def fine_kernel(slice_at, south_ref, north_ref, south_ok_ref, north_ok_ref, west_at_ref, east_at_ref,
                west_ok_ref, east_ok_ref, scale_ref, u_ref, fields_ref, prev_ref, next_ref,
                out_ref, state_ref, field_ref):
    tiles = u_ref.shape[0]
    rows = u_ref.shape[1]
    total = rows + 2 * HALO
    layers = prev_ref.shape[0]
    for i in range(tiles):
        west_at = west_at_ref[i]
        east_at = east_at_ref[i]
        west_ok = west_ok_ref[i] > 0
        east_ok = east_ok_ref[i] > 0
        state_ref[0, i, pl.ds(0, HALO), :] = jnp.where(west_ok, prev_ref[slice_at, west_at], 0.0)
        state_ref[0, i, pl.ds(HALO, rows), :] = u_ref[i]
        state_ref[0, i, pl.ds(HALO + rows, HALO), :] = jnp.where(
            east_ok, next_ref[slice_at, east_at], 0.0
        )
        for f in range(4):
            field_at = layers - 4 + f
            field_ref[f, i, pl.ds(0, HALO), :] = jnp.where(
                west_ok, prev_ref[field_at, west_at], 0.0
            )
            field_ref[f, i, pl.ds(HALO, rows), :] = fields_ref[f, i]
            field_ref[f, i, pl.ds(HALO + rows, HALO), :] = jnp.where(
                east_ok, next_ref[field_at, east_at], 0.0
            )

    lanes = u_ref.shape[2]
    lane = lax.broadcasted_iota(jnp.int32, (total, lanes), 1)
    first_lane = lane == 0
    last_lane = lane == lanes - 1

    def substep(s, carry):
        src = s % 2
        dst = 1 - src
        strength = scale_ref[s]
        for i in range(tiles):
            current = state_ref[src, i]
            south_tile = state_ref[src, south_ref[i]]
            north_tile = state_ref[src, north_ref[i]]
            south_edge = jnp.where(south_ok_ref[i] > 0, pltpu.roll(south_tile, 1, 1), 0.0)
            north_edge = jnp.where(north_ok_ref[i] > 0, pltpu.roll(north_tile, lanes - 1, 1), 0.0)
            from_west = pltpu.roll(current, 1, 0)
            from_east = pltpu.roll(current, total - 1, 0)
            from_south = jnp.where(first_lane, south_edge, pltpu.roll(current, 1, 1))
            from_north = jnp.where(last_lane, north_edge, pltpu.roll(current, lanes - 1, 1))
            diffusivity = field_ref[0, i]
            speed_x = field_ref[1, i]
            speed_y = field_ref[2, i]
            open_cells = field_ref[3, i]
            laplace = from_west + from_east + from_south + from_north - 4.0 * current
            transport = speed_x * (from_east - from_west) + speed_y * (from_north - from_south)
            state_ref[dst, i] = open_cells * (
                current + strength * diffusivity * laplace - 0.5 * transport
            )
        return carry

    lax.fori_loop(0, SUB, substep, 0)
    last = SUB % 2
    for i in range(tiles):
        out_ref[i] = state_ref[last, i, pl.ds(HALO, rows), :]


def fine_propagate(slice_at, u, fields, from_prev, from_next, indices, scale):
    tiles, rows, lanes = u.shape
    total = rows + 2 * HALO
    vmem = pltpu.MemorySpace.VMEM
    smem = pltpu.MemorySpace.SMEM
    return pl.pallas_call(
        functools.partial(fine_kernel, slice_at),
        out_shape=jax.ShapeDtypeStruct(u.shape, u.dtype),
        in_specs=[pl.BlockSpec(memory_space=smem)] * 9 + [pl.BlockSpec(memory_space=vmem)] * 4,
        out_specs=pl.BlockSpec(memory_space=vmem),
        scratch_shapes=[
            pltpu.VMEM((2, tiles, total, lanes), jnp.float32),
            pltpu.VMEM((4, tiles, total, lanes), jnp.float32),
        ],
        compiler_params=pltpu.CompilerParams(vmem_limit_bytes=48 * 1024 * 1024),
    )(*indices, scale, u, fields, from_prev, from_next)


def on_device(
    starts, diffusivity, velocity, obstacle, substep_scale, neighbors, coarse_x, coarse_y
):
    slice_count = starts.shape[0]
    tile_count = starts.shape[1]
    rows = starts.shape[2]
    all_tiles = tile_count * lax.axis_size("space")
    block_base = lax.axis_index("space") * tile_count
    open_cells = 1.0 - obstacle.astype(jnp.float32)

    fields = jnp.stack([diffusivity, velocity[0], velocity[1], open_cells], axis=0)
    layers = jnp.concatenate([starts, fields], axis=0)
    space_count = lax.axis_size("space")
    forward = [(i, i + 1) for i in range(space_count - 1)]
    backward = [(i + 1, i) for i in range(space_count - 1)]
    from_prev = lax.ppermute(layers[:, :, rows - HALO:, :], "space", forward)
    from_next = lax.ppermute(layers[:, :, :HALO, :], "space", backward)
    west_nb = neighbors[:, 0]
    east_nb = neighbors[:, 1]
    west_ok = (west_nb != all_tiles).astype(jnp.int32)
    east_ok = (east_nb != all_tiles).astype(jnp.int32)
    west_at = jnp.clip(west_nb - (block_base - tile_count), 0, tile_count - 1) * west_ok
    east_at = jnp.clip(east_nb - (block_base + tile_count), 0, tile_count - 1) * east_ok

    south_nb = neighbors[:, 2]
    north_nb = neighbors[:, 3]
    south_ok = (south_nb != all_tiles).astype(jnp.int32)
    north_ok = (north_nb != all_tiles).astype(jnp.int32)
    south = jnp.clip(south_nb - block_base, 0, tile_count - 1) * south_ok
    north = jnp.clip(north_nb - block_base, 0, tile_count - 1) * north_ok
    indices = (south, north, south_ok, north_ok, west_at, east_at, west_ok, east_ok)

    fine_ends = jnp.stack(
        [
            fine_propagate(n, starts[n], fields, from_prev, from_next, indices, substep_scale)
            for n in range(slice_count)
        ],
        axis=0,
    )
    correction = fine_ends - prolong(apply_coarse(restrict(starts), coarse_x, coarse_y))
    coarse_jump = restrict(correction)
    tm_index = lax.axis_index("tm")
    tm_count = lax.axis_size("tm")
    first_coarse = restrict(starts[0])

    def prefix_over_tm(total, power_x, power_y):
        distance = 1
        while distance < tm_count:
            received = passed_along(total, "tm", distance)
            total = total + jnp.where(
                tm_index >= distance, apply_coarse(received, power_x, power_y), 0.0
            )
            distance *= 2
            if distance < tm_count:
                power_x = jnp.einsum("tij,tjk->tik", power_x, power_x, precision=exact_precision)
                power_y = jnp.einsum("tij,tjk->tik", power_y, power_y, precision=exact_precision)
        return total

    if slice_count == 1:
        seed = jnp.where(tm_index == 0, apply_coarse(first_coarse, coarse_x, coarse_y), 0.0)
        reached = prefix_over_tm(coarse_jump[0] + seed, coarse_x, coarse_y)
        coarse_applied = (reached - coarse_jump[0])[None]
    else:
        shifted_jump = jnp.concatenate(
            [passed_along(coarse_jump[-1:], "tm", 1), coarse_jump[:-1]], axis=0
        )
        head = jnp.where(tm_index == 0, first_coarse[None], shifted_jump[:1])
        local = jnp.concatenate([head, shifted_jump[1:]], axis=0)
        states = [local[0]]
        for n in range(1, slice_count):
            states.append(apply_coarse(states[-1], coarse_x, coarse_y) + local[n])
        power_x = coarse_x
        power_y = coarse_y
        for n in range(1, slice_count):
            power_x = jnp.einsum("tij,tjk->tik", power_x, coarse_x, precision=exact_precision)
            power_y = jnp.einsum("tij,tjk->tik", power_y, coarse_y, precision=exact_precision)
        total = prefix_over_tm(states[-1], power_x, power_y)
        earlier = jnp.where(tm_index > 0, passed_along(total, "tm", 1), 0.0)
        own_coarse = []
        for n in range(slice_count):
            earlier = apply_coarse(earlier, coarse_x, coarse_y)
            own_coarse.append(states[n] + earlier)
        coarse_applied = apply_coarse(jnp.stack(own_coarse, axis=0), coarse_x, coarse_y)
    slice_ends = prolong(coarse_applied) + correction
    previous = passed_along(slice_ends[-1], "tm", 1)
    first_step = jnp.where(
        lax.axis_index("tm") == 0, jnp.zeros_like(previous), previous - starts[0]
    )
    increment = jnp.concatenate([first_step[None], slice_ends[:-1] - starts[1:]], axis=0)
    return (slice_ends, increment)


def solution(mesh):
    placed = (
        P("tm", "space", None, None),
        P("space", None, None),
        P(None, "space", None, None),
        P("space", None, None),
        P(),
        P("space", None),
        P("space", None, None),
        P("space", None, None),
    )
    return jax.shard_map(
        on_device,
        mesh=mesh,
        in_specs=placed,
        out_specs=(P("tm", "space", None, None), P("tm", "space", None, None)),
        check_vma=False,
    )
```

```python
import functools

import jax
import jax.numpy as jnp
from jax import lax
from jax.experimental import pallas as pl
from jax.experimental.pallas import tpu as pltpu
from jax.sharding import PartitionSpec as P

SUB = 12
HALO = 16


exact_precision = lax.Precision.HIGHEST


def spread(value, axis, source):
    kept = jnp.where(lax.axis_index(axis) == source, value, 0).astype(value.dtype)
    return lax.psum(kept, axis)


def passed_along(block, axis, distance):
    devices = range(lax.axis_size(axis))
    route = [(i - distance, i) for i in devices if i - distance in devices]
    return lax.ppermute(block, axis, route)


def restrict(values):
    return 0.5 * (values[..., 0::2, :] + values[..., 1::2, :])


def prolong(coarse_values):
    return jnp.repeat(coarse_values, 2, axis=-2)


def apply_coarse(coarse_values, matrix_x, matrix_y):
    mixed_x = jnp.einsum("tij,...tjk->...tik", matrix_x, coarse_values, precision=exact_precision)
    return jnp.einsum("...tik,tlk->...til", mixed_x, matrix_y, precision=exact_precision)


def fine_kernel(slice_at, south_ref, north_ref, south_ok_ref, north_ok_ref, west_at_ref, east_at_ref,
                west_ok_ref, east_ok_ref, scale_ref, u_ref, fields_ref, prev_ref, next_ref,
                out_ref, state_ref, field_ref):
    tiles = u_ref.shape[0]
    rows = u_ref.shape[1]
    total = rows + 2 * HALO
    layers = prev_ref.shape[0]
    for i in range(tiles):
        west_at = west_at_ref[i]
        east_at = east_at_ref[i]
        west_ok = west_ok_ref[i] > 0
        east_ok = east_ok_ref[i] > 0
        state_ref[0, i, pl.ds(0, HALO), :] = jnp.where(west_ok, prev_ref[slice_at, west_at], 0.0)
        state_ref[0, i, pl.ds(HALO, rows), :] = u_ref[i]
        state_ref[0, i, pl.ds(HALO + rows, HALO), :] = jnp.where(
            east_ok, next_ref[slice_at, east_at], 0.0
        )
        for f in range(4):
            field_at = layers - 4 + f
            field_ref[f, i, pl.ds(0, HALO), :] = jnp.where(
                west_ok, prev_ref[field_at, west_at], 0.0
            )
            field_ref[f, i, pl.ds(HALO, rows), :] = fields_ref[f, i]
            field_ref[f, i, pl.ds(HALO + rows, HALO), :] = jnp.where(
                east_ok, next_ref[field_at, east_at], 0.0
            )

    lanes = u_ref.shape[2]
    lane = lax.broadcasted_iota(jnp.int32, (total, lanes), 1)
    first_lane = lane == 0
    last_lane = lane == lanes - 1

    def substep(s, carry):
        src = s % 2
        dst = 1 - src
        strength = scale_ref[s]
        for i in range(tiles):
            current = state_ref[src, i]
            south_tile = state_ref[src, south_ref[i]]
            north_tile = state_ref[src, north_ref[i]]
            south_edge = jnp.where(south_ok_ref[i] > 0, pltpu.roll(south_tile, 1, 1), 0.0)
            north_edge = jnp.where(north_ok_ref[i] > 0, pltpu.roll(north_tile, lanes - 1, 1), 0.0)
            from_west = pltpu.roll(current, 1, 0)
            from_east = pltpu.roll(current, total - 1, 0)
            from_south = jnp.where(first_lane, south_edge, pltpu.roll(current, 1, 1))
            from_north = jnp.where(last_lane, north_edge, pltpu.roll(current, lanes - 1, 1))
            diffusivity = field_ref[0, i]
            speed_x = field_ref[1, i]
            speed_y = field_ref[2, i]
            open_cells = field_ref[3, i]
            laplace = from_west + from_east + from_south + from_north - 4.0 * current
            transport = speed_x * (from_east - from_west) + speed_y * (from_north - from_south)
            state_ref[dst, i] = open_cells * (
                current + strength * diffusivity * laplace - 0.5 * transport
            )
        return carry

    lax.fori_loop(0, SUB, substep, 0)
    last = SUB % 2
    for i in range(tiles):
        out_ref[i] = state_ref[last, i, pl.ds(HALO, rows), :]


def fine_propagate(slice_at, u, fields, from_prev, from_next, indices, scale):
    tiles, rows, lanes = u.shape
    total = rows + 2 * HALO
    vmem = pltpu.MemorySpace.VMEM
    smem = pltpu.MemorySpace.SMEM
    return pl.pallas_call(
        functools.partial(fine_kernel, slice_at),
        out_shape=jax.ShapeDtypeStruct(u.shape, u.dtype),
        in_specs=[pl.BlockSpec(memory_space=smem)] * 9 + [pl.BlockSpec(memory_space=vmem)] * 4,
        out_specs=pl.BlockSpec(memory_space=vmem),
        scratch_shapes=[
            pltpu.VMEM((2, tiles, total, lanes), jnp.float32),
            pltpu.VMEM((4, tiles, total, lanes), jnp.float32),
        ],
        compiler_params=pltpu.CompilerParams(vmem_limit_bytes=48 * 1024 * 1024),
    )(*indices, scale, u, fields, from_prev, from_next)


def on_device(
    starts, diffusivity, velocity, obstacle, substep_scale, neighbors, coarse_x, coarse_y
):
    slice_count = starts.shape[0]
    tile_count = starts.shape[1]
    rows = starts.shape[2]
    all_tiles = tile_count * lax.axis_size("space")
    block_base = lax.axis_index("space") * tile_count
    open_cells = 1.0 - obstacle.astype(jnp.float32)

    fields = jnp.stack([diffusivity, velocity[0], velocity[1], open_cells], axis=0)
    layers = jnp.concatenate([starts, fields], axis=0)
    space_count = lax.axis_size("space")
    forward = [(i, i + 1) for i in range(space_count - 1)]
    backward = [(i + 1, i) for i in range(space_count - 1)]
    from_prev = lax.ppermute(layers[:, :, rows - HALO:, :], "space", forward)
    from_next = lax.ppermute(layers[:, :, :HALO, :], "space", backward)
    west_nb = neighbors[:, 0]
    east_nb = neighbors[:, 1]
    west_ok = (west_nb != all_tiles).astype(jnp.int32)
    east_ok = (east_nb != all_tiles).astype(jnp.int32)
    west_at = jnp.clip(west_nb - (block_base - tile_count), 0, tile_count - 1) * west_ok
    east_at = jnp.clip(east_nb - (block_base + tile_count), 0, tile_count - 1) * east_ok

    south_nb = neighbors[:, 2]
    north_nb = neighbors[:, 3]
    south_ok = (south_nb != all_tiles).astype(jnp.int32)
    north_ok = (north_nb != all_tiles).astype(jnp.int32)
    south = jnp.clip(south_nb - block_base, 0, tile_count - 1) * south_ok
    north = jnp.clip(north_nb - block_base, 0, tile_count - 1) * north_ok
    indices = (south, north, south_ok, north_ok, west_at, east_at, west_ok, east_ok)

    fine_ends = jnp.stack(
        [
            fine_propagate(n, starts[n], fields, from_prev, from_next, indices, substep_scale)
            for n in range(slice_count)
        ],
        axis=0,
    )
    correction = fine_ends - prolong(apply_coarse(restrict(starts), coarse_x, coarse_y))
    coarse_jump = restrict(correction)
    tm_index = lax.axis_index("tm")
    tm_count = lax.axis_size("tm")
    first_coarse = restrict(starts[0])

    def prefix_over_tm(total, power_x, power_y):
        distances = []
        distance = 1
        while distance < tm_count:
            distances.append(distance)
            distance *= 2
        powers = {}
        for distance in distances:
            powers[distance] = (power_x, power_y)
            power_x = jnp.einsum("tij,tjk->tik", power_x, power_x, precision=exact_precision)
            power_y = jnp.einsum("tij,tjk->tik", power_y, power_y, precision=exact_precision)
        half = total.shape[0] // 2
        parts = [(slice(0, half), distances[:1] + distances[1:]),
                 (slice(half, None), distances[:1] + distances[1:][::-1])]
        values = [total[part] for part, _ in parts]
        for step in range(len(distances)):
            if step == 0:
                received = passed_along(total, "tm", distances[0])
                received = [received[part] for part, _ in parts]
            else:
                received = [passed_along(values[k], "tm", parts[k][1][step]) for k in range(2)]
            for k in range(2):
                part, order = parts[k]
                distance = order[step]
                mixed = apply_coarse(received[k], powers[distance][0][part], powers[distance][1][part])
                values[k] = values[k] + jnp.where(tm_index >= distance, mixed, 0.0)
        return jnp.concatenate(values, axis=0)

    if slice_count == 1:
        seed = jnp.where(tm_index == 0, apply_coarse(first_coarse, coarse_x, coarse_y), 0.0)
        reached = prefix_over_tm(coarse_jump[0] + seed, coarse_x, coarse_y)
        coarse_applied = (reached - coarse_jump[0])[None]
    else:
        shifted_jump = jnp.concatenate(
            [passed_along(coarse_jump[-1:], "tm", 1), coarse_jump[:-1]], axis=0
        )
        head = jnp.where(tm_index == 0, first_coarse[None], shifted_jump[:1])
        local = jnp.concatenate([head, shifted_jump[1:]], axis=0)
        states = [local[0]]
        for n in range(1, slice_count):
            states.append(apply_coarse(states[-1], coarse_x, coarse_y) + local[n])
        power_x = coarse_x
        power_y = coarse_y
        for n in range(1, slice_count):
            power_x = jnp.einsum("tij,tjk->tik", power_x, coarse_x, precision=exact_precision)
            power_y = jnp.einsum("tij,tjk->tik", power_y, coarse_y, precision=exact_precision)
        total = prefix_over_tm(states[-1], power_x, power_y)
        earlier = jnp.where(tm_index > 0, passed_along(total, "tm", 1), 0.0)
        own_coarse = []
        for n in range(slice_count):
            earlier = apply_coarse(earlier, coarse_x, coarse_y)
            own_coarse.append(states[n] + earlier)
        coarse_applied = apply_coarse(jnp.stack(own_coarse, axis=0), coarse_x, coarse_y)
    slice_ends = prolong(coarse_applied) + correction
    previous = passed_along(slice_ends[-1], "tm", 1)
    first_step = jnp.where(
        lax.axis_index("tm") == 0, jnp.zeros_like(previous), previous - starts[0]
    )
    increment = jnp.concatenate([first_step[None], slice_ends[:-1] - starts[1:]], axis=0)
    return (slice_ends, increment)


def solution(mesh):
    placed = (
        P("tm", "space", None, None),
        P("space", None, None),
        P(None, "space", None, None),
        P("space", None, None),
        P(),
        P("space", None),
        P("space", None, None),
        P("space", None, None),
    )
    return jax.shard_map(
        on_device,
        mesh=mesh,
        in_specs=placed,
        out_specs=(P("tm", "space", None, None), P("tm", "space", None, None)),
        check_vma=False,
    )
```

```python
import functools

import jax
import jax.numpy as jnp
from jax import lax
from jax.experimental import pallas as pl
from jax.experimental.pallas import tpu as pltpu
from jax.sharding import PartitionSpec as P

SUB = 12
HALO = 16


exact_precision = lax.Precision.HIGHEST


def spread(value, axis, source):
    kept = jnp.where(lax.axis_index(axis) == source, value, 0).astype(value.dtype)
    return lax.psum(kept, axis)


def passed_along(block, axis, distance):
    devices = range(lax.axis_size(axis))
    route = [(i - distance, i) for i in devices if i - distance in devices]
    return lax.ppermute(block, axis, route)


def restrict(values):
    return 0.5 * (values[..., 0::2, :] + values[..., 1::2, :])


def prolong(coarse_values):
    return jnp.repeat(coarse_values, 2, axis=-2)


def apply_coarse(coarse_values, matrix_x, matrix_y):
    mixed_x = jnp.einsum("tij,...tjk->...tik", matrix_x, coarse_values, precision=exact_precision)
    return jnp.einsum("...tik,tlk->...til", mixed_x, matrix_y, precision=exact_precision)


def fine_kernel(slice_at, south_ref, north_ref, west_at_ref, east_at_ref, west_ok_ref, east_ok_ref,
                scale_ref, u_ref, diffusivity_ref, velocity_ref, obstacle_ref, prev_ref, next_ref,
                out_ref, state_ref, field_ref):
    tiles = u_ref.shape[0]
    rows = u_ref.shape[1]
    lanes = u_ref.shape[2]
    total = rows + 2 * HALO
    layers = prev_ref.shape[0]
    for b in range(2):
        state_ref[b, tiles] = jnp.zeros((total, lanes), jnp.float32)
    for i in range(tiles):
        west_at = west_at_ref[i]
        east_at = east_at_ref[i]
        west_ok = west_ok_ref[i] > 0
        east_ok = east_ok_ref[i] > 0
        state_ref[0, i, pl.ds(0, HALO), :] = jnp.where(west_ok, prev_ref[slice_at, west_at], 0.0)
        state_ref[0, i, pl.ds(HALO, rows), :] = u_ref[i]
        state_ref[0, i, pl.ds(HALO + rows, HALO), :] = jnp.where(
            east_ok, next_ref[slice_at, east_at], 0.0
        )
        own = (
            diffusivity_ref[i],
            velocity_ref[0, i],
            velocity_ref[1, i],
            1.0 - obstacle_ref[i].astype(jnp.float32),
        )
        for f in range(4):
            field_at = layers - 4 + f
            field_ref[f, i, pl.ds(0, HALO), :] = jnp.where(
                west_ok, prev_ref[field_at, west_at], 0.0
            )
            field_ref[f, i, pl.ds(HALO, rows), :] = own[f]
            field_ref[f, i, pl.ds(HALO + rows, HALO), :] = jnp.where(
                east_ok, next_ref[field_at, east_at], 0.0
            )

    lane = lax.broadcasted_iota(jnp.int32, (total, lanes), 1)
    first_lane = lane == 0
    last_lane = lane == lanes - 1

    def substep(s, carry):
        src = s % 2
        dst = 1 - src
        strength = scale_ref[s]
        for i in range(tiles):
            current = state_ref[src, i]
            south_tile = state_ref[src, south_ref[i]]
            north_tile = state_ref[src, north_ref[i]]
            from_west = pltpu.roll(current, 1, 0)
            from_east = pltpu.roll(current, total - 1, 0)
            from_south = pltpu.roll(jnp.where(last_lane, south_tile, current), 1, 1)
            from_north = pltpu.roll(jnp.where(first_lane, north_tile, current), lanes - 1, 1)
            diffusivity = field_ref[0, i]
            speed_x = field_ref[1, i]
            speed_y = field_ref[2, i]
            open_cells = field_ref[3, i]
            laplace = from_west + from_east + from_south + from_north - 4.0 * current
            transport = speed_x * (from_east - from_west) + speed_y * (from_north - from_south)
            state_ref[dst, i] = open_cells * (
                current + strength * diffusivity * laplace - 0.5 * transport
            )
        return carry

    lax.fori_loop(0, SUB, substep, 0)
    last = SUB % 2
    for i in range(tiles):
        out_ref[i] = state_ref[last, i, pl.ds(HALO, rows), :]


def fine_propagate(slice_at, u, diffusivity, velocity, obstacle, from_prev, from_next, indices, scale):
    tiles, rows, lanes = u.shape
    total = rows + 2 * HALO
    vmem = pltpu.MemorySpace.VMEM
    smem = pltpu.MemorySpace.SMEM
    return pl.pallas_call(
        functools.partial(fine_kernel, slice_at),
        out_shape=jax.ShapeDtypeStruct(u.shape, u.dtype),
        in_specs=[pl.BlockSpec(memory_space=smem)] * 7 + [pl.BlockSpec(memory_space=vmem)] * 6,
        out_specs=pl.BlockSpec(memory_space=vmem),
        scratch_shapes=[
            pltpu.VMEM((2, tiles + 1, total, lanes), jnp.float32),
            pltpu.VMEM((4, tiles, total, lanes), jnp.float32),
        ],
        compiler_params=pltpu.CompilerParams(vmem_limit_bytes=48 * 1024 * 1024),
    )(*indices, scale, u, diffusivity, velocity, obstacle, from_prev, from_next)


def on_device(
    starts, diffusivity, velocity, obstacle, substep_scale, neighbors, coarse_x, coarse_y
):
    slice_count = starts.shape[0]
    tile_count = starts.shape[1]
    rows = starts.shape[2]
    all_tiles = tile_count * lax.axis_size("space")
    block_base = lax.axis_index("space") * tile_count
    open_cells = 1.0 - obstacle.astype(jnp.float32)

    fields = jnp.stack([diffusivity, velocity[0], velocity[1], open_cells], axis=0)
    layers = jnp.concatenate([starts, fields], axis=0)
    space_count = lax.axis_size("space")
    forward = [(i, i + 1) for i in range(space_count - 1)]
    backward = [(i + 1, i) for i in range(space_count - 1)]
    from_prev = lax.ppermute(layers[:, :, rows - HALO:, :], "space", forward)
    from_next = lax.ppermute(layers[:, :, :HALO, :], "space", backward)
    west_nb = neighbors[:, 0]
    east_nb = neighbors[:, 1]
    west_ok = (west_nb != all_tiles).astype(jnp.int32)
    east_ok = (east_nb != all_tiles).astype(jnp.int32)
    west_at = jnp.clip(west_nb - (block_base - tile_count), 0, tile_count - 1) * west_ok
    east_at = jnp.clip(east_nb - (block_base + tile_count), 0, tile_count - 1) * east_ok

    south_nb = neighbors[:, 2]
    north_nb = neighbors[:, 3]
    south_ok = (south_nb != all_tiles).astype(jnp.int32)
    north_ok = (north_nb != all_tiles).astype(jnp.int32)
    south = jnp.where(south_ok > 0, jnp.clip(south_nb - block_base, 0, tile_count - 1), tile_count)
    north = jnp.where(north_ok > 0, jnp.clip(north_nb - block_base, 0, tile_count - 1), tile_count)
    indices = (south, north, west_at, east_at, west_ok, east_ok)

    fine_ends = jnp.stack(
        [
            fine_propagate(
                n, starts[n], diffusivity, velocity, obstacle, from_prev, from_next, indices,
                substep_scale,
            )
            for n in range(slice_count)
        ],
        axis=0,
    )
    correction = fine_ends - prolong(apply_coarse(restrict(starts), coarse_x, coarse_y))
    coarse_jump = restrict(correction)
    tm_index = lax.axis_index("tm")
    tm_count = lax.axis_size("tm")
    first_coarse = restrict(starts[0])

    def prefix_over_tm(total, power_x, power_y):
        distances = []
        distance = 1
        while distance < tm_count:
            distances.append(distance)
            distance *= 2
        powers = {}
        for distance in distances:
            powers[distance] = (power_x, power_y)
            power_x = jnp.einsum("tij,tjk->tik", power_x, power_x, precision=exact_precision)
            power_y = jnp.einsum("tij,tjk->tik", power_y, power_y, precision=exact_precision)
        half = total.shape[0] // 2
        parts = [(slice(0, half), distances[:1] + distances[1:]),
                 (slice(half, None), distances[:1] + distances[1:][::-1])]
        values = [total[part] for part, _ in parts]
        for step in range(len(distances)):
            if step == 0:
                received = passed_along(total, "tm", distances[0])
                received = [received[part] for part, _ in parts]
            else:
                received = [passed_along(values[k], "tm", parts[k][1][step]) for k in range(2)]
            for k in range(2):
                part, order = parts[k]
                distance = order[step]
                mixed = apply_coarse(received[k], powers[distance][0][part], powers[distance][1][part])
                values[k] = values[k] + jnp.where(tm_index >= distance, mixed, 0.0)
        return jnp.concatenate(values, axis=0)

    if slice_count == 1:
        seed = jnp.where(tm_index == 0, apply_coarse(first_coarse, coarse_x, coarse_y), 0.0)
        reached = prefix_over_tm(coarse_jump[0] + seed, coarse_x, coarse_y)
        coarse_applied = (reached - coarse_jump[0])[None]
    else:
        shifted_jump = jnp.concatenate(
            [passed_along(coarse_jump[-1:], "tm", 1), coarse_jump[:-1]], axis=0
        )
        head = jnp.where(tm_index == 0, first_coarse[None], shifted_jump[:1])
        local = jnp.concatenate([head, shifted_jump[1:]], axis=0)
        states = [local[0]]
        for n in range(1, slice_count):
            states.append(apply_coarse(states[-1], coarse_x, coarse_y) + local[n])
        power_x = coarse_x
        power_y = coarse_y
        for n in range(1, slice_count):
            power_x = jnp.einsum("tij,tjk->tik", power_x, coarse_x, precision=exact_precision)
            power_y = jnp.einsum("tij,tjk->tik", power_y, coarse_y, precision=exact_precision)
        total = prefix_over_tm(states[-1], power_x, power_y)
        earlier = jnp.where(tm_index > 0, passed_along(total, "tm", 1), 0.0)
        own_coarse = []
        for n in range(slice_count):
            earlier = apply_coarse(earlier, coarse_x, coarse_y)
            own_coarse.append(states[n] + earlier)
        coarse_applied = apply_coarse(jnp.stack(own_coarse, axis=0), coarse_x, coarse_y)
    slice_ends = prolong(coarse_applied) + correction
    previous = passed_along(slice_ends[-1], "tm", 1)
    first_step = jnp.where(
        lax.axis_index("tm") == 0, jnp.zeros_like(previous), previous - starts[0]
    )
    increment = jnp.concatenate([first_step[None], slice_ends[:-1] - starts[1:]], axis=0)
    return (slice_ends, increment)


def solution(mesh):
    placed = (
        P("tm", "space", None, None),
        P("space", None, None),
        P(None, "space", None, None),
        P("space", None, None),
        P(),
        P("space", None),
        P("space", None, None),
        P("space", None, None),
    )
    return jax.shard_map(
        on_device,
        mesh=mesh,
        in_specs=placed,
        out_specs=(P("tm", "space", None, None), P("tm", "space", None, None)),
        check_vma=False,
    )
```

```python
import functools

import jax
import jax.numpy as jnp
from jax import lax
from jax.experimental import pallas as pl
from jax.experimental.pallas import tpu as pltpu
from jax.sharding import PartitionSpec as P

SUB = 12
HALO = 16


exact_precision = lax.Precision.HIGHEST


def spread(value, axis, source):
    kept = jnp.where(lax.axis_index(axis) == source, value, 0).astype(value.dtype)
    return lax.psum(kept, axis)


def passed_along(block, axis, distance):
    devices = range(lax.axis_size(axis))
    route = [(i - distance, i) for i in devices if i - distance in devices]
    return lax.ppermute(block, axis, route)


def restrict(values):
    return 0.5 * (values[..., 0::2, :] + values[..., 1::2, :])


def prolong(coarse_values):
    return jnp.repeat(coarse_values, 2, axis=-2)


def apply_coarse(coarse_values, matrix_x, matrix_y):
    mixed_x = jnp.einsum("tij,...tjk->...tik", matrix_x, coarse_values, precision=exact_precision)
    return jnp.einsum("...tik,tlk->...til", mixed_x, matrix_y, precision=exact_precision)


def fine_kernel(slice_at, south_ref, north_ref, west_at_ref, east_at_ref, west_ok_ref, east_ok_ref,
                scale_ref, u_ref, diffusivity_ref, velocity_ref, obstacle_ref, prev_ref, next_ref,
                out_ref, state_ref, field_ref):
    tiles = u_ref.shape[0]
    rows = u_ref.shape[1]
    lanes = u_ref.shape[2]
    total = rows + 2 * HALO
    layers = prev_ref.shape[0]
    for b in range(2):
        state_ref[b, tiles] = jnp.zeros((total, lanes), jnp.float32)
    for i in range(tiles):
        west_at = west_at_ref[i]
        east_at = east_at_ref[i]
        west_ok = west_ok_ref[i] > 0
        east_ok = east_ok_ref[i] > 0
        state_ref[0, i, pl.ds(0, HALO), :] = jnp.where(west_ok, prev_ref[slice_at, west_at], 0.0)
        state_ref[0, i, pl.ds(HALO, rows), :] = u_ref[i]
        state_ref[0, i, pl.ds(HALO + rows, HALO), :] = jnp.where(
            east_ok, next_ref[slice_at, east_at], 0.0
        )
        own = (
            diffusivity_ref[i],
            velocity_ref[0, i],
            velocity_ref[1, i],
            1.0 - obstacle_ref[i].astype(jnp.float32),
        )
        for f in range(4):
            field_at = layers - 4 + f
            field_ref[f, i, pl.ds(0, HALO), :] = jnp.where(
                west_ok, prev_ref[field_at, west_at], 0.0
            )
            field_ref[f, i, pl.ds(HALO, rows), :] = own[f]
            field_ref[f, i, pl.ds(HALO + rows, HALO), :] = jnp.where(
                east_ok, next_ref[field_at, east_at], 0.0
            )

    lane = lax.broadcasted_iota(jnp.int32, (total, lanes), 1)
    first_lane = lane == 0
    last_lane = lane == lanes - 1

    def substep(s, carry):
        src = s % 2
        dst = 1 - src
        strength = scale_ref[s]
        for i in range(tiles):
            current = state_ref[src, i]
            south_tile = state_ref[src, south_ref[i]]
            north_tile = state_ref[src, north_ref[i]]
            from_west = pltpu.roll(current, 1, 0)
            from_east = pltpu.roll(current, total - 1, 0)
            from_south = pltpu.roll(jnp.where(last_lane, south_tile, current), 1, 1)
            from_north = pltpu.roll(jnp.where(first_lane, north_tile, current), lanes - 1, 1)
            diffusivity = field_ref[0, i]
            speed_x = field_ref[1, i]
            speed_y = field_ref[2, i]
            open_cells = field_ref[3, i]
            laplace = from_west + from_east + from_south + from_north - 4.0 * current
            transport = speed_x * (from_east - from_west) + speed_y * (from_north - from_south)
            state_ref[dst, i] = open_cells * (
                current + strength * diffusivity * laplace - 0.5 * transport
            )
        return carry

    lax.fori_loop(0, SUB, substep, 0)
    last = SUB % 2
    for i in range(tiles):
        out_ref[i] = state_ref[last, i, pl.ds(HALO, rows), :]


def fine_propagate(slice_at, u, diffusivity, velocity, obstacle, from_prev, from_next, indices, scale):
    tiles, rows, lanes = u.shape
    total = rows + 2 * HALO
    vmem = pltpu.MemorySpace.VMEM
    smem = pltpu.MemorySpace.SMEM
    return pl.pallas_call(
        functools.partial(fine_kernel, slice_at),
        out_shape=jax.ShapeDtypeStruct(u.shape, u.dtype),
        in_specs=[pl.BlockSpec(memory_space=smem)] * 7 + [pl.BlockSpec(memory_space=vmem)] * 6,
        out_specs=pl.BlockSpec(memory_space=vmem),
        scratch_shapes=[
            pltpu.VMEM((2, tiles + 1, total, lanes), jnp.float32),
            pltpu.VMEM((4, tiles, total, lanes), jnp.float32),
        ],
        compiler_params=pltpu.CompilerParams(vmem_limit_bytes=48 * 1024 * 1024),
    )(*indices, scale, u, diffusivity, velocity, obstacle, from_prev, from_next)


def on_device(
    starts, diffusivity, velocity, obstacle, substep_scale, neighbors, coarse_x, coarse_y
):
    slice_count = starts.shape[0]
    tile_count = starts.shape[1]
    rows = starts.shape[2]
    all_tiles = tile_count * lax.axis_size("space")
    block_base = lax.axis_index("space") * tile_count
    open_cells = 1.0 - obstacle.astype(jnp.float32)

    fields = jnp.stack([diffusivity, velocity[0], velocity[1], open_cells], axis=0)
    layers = jnp.concatenate([starts, fields], axis=0)
    space_count = lax.axis_size("space")
    forward = [(i, i + 1) for i in range(space_count - 1)]
    backward = [(i + 1, i) for i in range(space_count - 1)]
    from_prev = lax.ppermute(layers[:, :, rows - HALO:, :], "space", forward)
    from_next = lax.ppermute(layers[:, :, :HALO, :], "space", backward)
    west_nb = neighbors[:, 0]
    east_nb = neighbors[:, 1]
    west_ok = (west_nb != all_tiles).astype(jnp.int32)
    east_ok = (east_nb != all_tiles).astype(jnp.int32)
    west_at = jnp.clip(west_nb - (block_base - tile_count), 0, tile_count - 1) * west_ok
    east_at = jnp.clip(east_nb - (block_base + tile_count), 0, tile_count - 1) * east_ok

    south_nb = neighbors[:, 2]
    north_nb = neighbors[:, 3]
    south_ok = (south_nb != all_tiles).astype(jnp.int32)
    north_ok = (north_nb != all_tiles).astype(jnp.int32)
    south = jnp.where(south_ok > 0, jnp.clip(south_nb - block_base, 0, tile_count - 1), tile_count)
    north = jnp.where(north_ok > 0, jnp.clip(north_nb - block_base, 0, tile_count - 1), tile_count)
    indices = (south, north, west_at, east_at, west_ok, east_ok)

    fine_ends = jnp.stack(
        [
            fine_propagate(
                n, starts[n], diffusivity, velocity, obstacle, from_prev, from_next, indices,
                substep_scale,
            )
            for n in range(slice_count)
        ],
        axis=0,
    )
    correction = fine_ends - prolong(apply_coarse(restrict(starts), coarse_x, coarse_y))
    coarse_jump = restrict(correction)
    earlier_correction = passed_along(correction[-1], "tm", 1)
    tm_index = lax.axis_index("tm")
    tm_count = lax.axis_size("tm")
    first_coarse = restrict(starts[0])

    def prefix_over_tm(total, power_x, power_y):
        distances = []
        distance = 1
        while distance < tm_count:
            distances.append(distance)
            distance *= 2
        powers = {}
        for distance in distances:
            powers[distance] = (power_x, power_y)
            power_x = jnp.einsum("tij,tjk->tik", power_x, power_x, precision=exact_precision)
            power_y = jnp.einsum("tij,tjk->tik", power_y, power_y, precision=exact_precision)
        half = total.shape[0] // 2
        parts = [(slice(0, half), distances[:1] + distances[1:]),
                 (slice(half, None), distances[:1] + distances[1:][::-1])]
        values = [total[part] for part, _ in parts]
        for step in range(len(distances)):
            if step == 0:
                received = passed_along(total, "tm", distances[0])
                received = [received[part] for part, _ in parts]
            else:
                received = [passed_along(values[k], "tm", parts[k][1][step]) for k in range(2)]
            for k in range(2):
                part, order = parts[k]
                distance = order[step]
                mixed = apply_coarse(received[k], powers[distance][0][part], powers[distance][1][part])
                values[k] = values[k] + jnp.where(tm_index >= distance, mixed, 0.0)
        return jnp.concatenate(values, axis=0)

    if slice_count == 1:
        seed = jnp.where(tm_index == 0, apply_coarse(first_coarse, coarse_x, coarse_y), 0.0)
        reached = prefix_over_tm(coarse_jump[0] + seed, coarse_x, coarse_y)
        coarse_applied = (reached - coarse_jump[0])[None]
    else:
        shifted_jump = jnp.concatenate(
            [passed_along(coarse_jump[-1:], "tm", 1), coarse_jump[:-1]], axis=0
        )
        head = jnp.where(tm_index == 0, first_coarse[None], shifted_jump[:1])
        local = jnp.concatenate([head, shifted_jump[1:]], axis=0)
        states = [local[0]]
        for n in range(1, slice_count):
            states.append(apply_coarse(states[-1], coarse_x, coarse_y) + local[n])
        power_x = coarse_x
        power_y = coarse_y
        for n in range(1, slice_count):
            power_x = jnp.einsum("tij,tjk->tik", power_x, coarse_x, precision=exact_precision)
            power_y = jnp.einsum("tij,tjk->tik", power_y, coarse_y, precision=exact_precision)
        total = prefix_over_tm(states[-1], power_x, power_y)
        earlier = jnp.where(tm_index > 0, passed_along(total, "tm", 1), 0.0)
        own_coarse = []
        for n in range(slice_count):
            earlier = apply_coarse(earlier, coarse_x, coarse_y)
            own_coarse.append(states[n] + earlier)
        coarse_applied = apply_coarse(jnp.stack(own_coarse, axis=0), coarse_x, coarse_y)
    slice_ends = prolong(coarse_applied) + correction
    previous = prolong(passed_along(coarse_applied[-1], "tm", 1)) + earlier_correction
    first_step = jnp.where(
        lax.axis_index("tm") == 0, jnp.zeros_like(previous), previous - starts[0]
    )
    increment = jnp.concatenate([first_step[None], slice_ends[:-1] - starts[1:]], axis=0)
    return (slice_ends, increment)


def solution(mesh):
    placed = (
        P("tm", "space", None, None),
        P("space", None, None),
        P(None, "space", None, None),
        P("space", None, None),
        P(),
        P("space", None),
        P("space", None, None),
        P("space", None, None),
    )
    return jax.shard_map(
        on_device,
        mesh=mesh,
        in_specs=placed,
        out_specs=(P("tm", "space", None, None), P("tm", "space", None, None)),
        check_vma=False,
    )
```

```python
import functools

import jax
import jax.numpy as jnp
from jax import lax
from jax.experimental import pallas as pl
from jax.experimental.pallas import tpu as pltpu
from jax.sharding import PartitionSpec as P

SUB = 12
HALO = 16


exact_precision = lax.Precision.HIGHEST


def spread(value, axis, source):
    kept = jnp.where(lax.axis_index(axis) == source, value, 0).astype(value.dtype)
    return lax.psum(kept, axis)


def passed_along(block, axis, distance):
    devices = range(lax.axis_size(axis))
    route = [(i - distance, i) for i in devices if i - distance in devices]
    return lax.ppermute(block, axis, route)


def restrict(values):
    return 0.5 * (values[..., 0::2, :] + values[..., 1::2, :])


def prolong(coarse_values):
    return jnp.repeat(coarse_values, 2, axis=-2)


def apply_coarse(coarse_values, matrix_x, matrix_y):
    mixed_x = jnp.einsum("tij,...tjk->...tik", matrix_x, coarse_values, precision=exact_precision)
    return jnp.einsum("...tik,tlk->...til", mixed_x, matrix_y, precision=exact_precision)


def fine_kernel(slice_at, south_ref, north_ref, west_at_ref, east_at_ref, west_ok_ref, east_ok_ref,
                scale_ref, u_ref, diffusivity_ref, velocity_ref, obstacle_ref, prev_ref, next_ref,
                out_ref, state_ref, field_ref):
    tiles = u_ref.shape[0]
    rows = u_ref.shape[1]
    lanes = u_ref.shape[2]
    total = rows + 2 * HALO
    layers = prev_ref.shape[0]
    for b in range(2):
        state_ref[b, tiles] = jnp.zeros((total, lanes), jnp.float32)
    for i in range(tiles):
        west_at = west_at_ref[i]
        east_at = east_at_ref[i]
        west_ok = west_ok_ref[i] > 0
        east_ok = east_ok_ref[i] > 0
        state_ref[0, i, pl.ds(0, HALO), :] = jnp.where(west_ok, prev_ref[slice_at, west_at], 0.0)
        state_ref[0, i, pl.ds(HALO, rows), :] = u_ref[i]
        state_ref[0, i, pl.ds(HALO + rows, HALO), :] = jnp.where(
            east_ok, next_ref[slice_at, east_at], 0.0
        )
        own = (
            diffusivity_ref[i],
            velocity_ref[0, i],
            velocity_ref[1, i],
            1.0 - obstacle_ref[i].astype(jnp.float32),
        )
        for f in range(4):
            field_at = layers - 4 + f
            field_ref[f, i, pl.ds(0, HALO), :] = jnp.where(
                west_ok, prev_ref[field_at, west_at], 0.0
            )
            field_ref[f, i, pl.ds(HALO, rows), :] = own[f]
            field_ref[f, i, pl.ds(HALO + rows, HALO), :] = jnp.where(
                east_ok, next_ref[field_at, east_at], 0.0
            )

    lane = lax.broadcasted_iota(jnp.int32, (total, lanes), 1)
    first_lane = lane == 0
    last_lane = lane == lanes - 1

    def substep(s, carry):
        src = s % 2
        dst = 1 - src
        strength = scale_ref[s]
        for i in range(tiles):
            current = state_ref[src, i]
            south_tile = state_ref[src, south_ref[i]]
            north_tile = state_ref[src, north_ref[i]]
            from_west = pltpu.roll(current, 1, 0)
            from_east = pltpu.roll(current, total - 1, 0)
            from_south = pltpu.roll(jnp.where(last_lane, south_tile, current), 1, 1)
            from_north = pltpu.roll(jnp.where(first_lane, north_tile, current), lanes - 1, 1)
            diffusivity = field_ref[0, i]
            speed_x = field_ref[1, i]
            speed_y = field_ref[2, i]
            open_cells = field_ref[3, i]
            laplace = from_west + from_east + from_south + from_north - 4.0 * current
            transport = speed_x * (from_east - from_west) + speed_y * (from_north - from_south)
            state_ref[dst, i] = open_cells * (
                current + strength * diffusivity * laplace - 0.5 * transport
            )
        return carry

    lax.fori_loop(0, SUB, substep, 0)
    last = SUB % 2
    for i in range(tiles):
        out_ref[i] = state_ref[last, i, pl.ds(HALO, rows), :]


def fine_propagate(slice_at, u, diffusivity, velocity, obstacle, from_prev, from_next, indices, scale):
    tiles, rows, lanes = u.shape
    total = rows + 2 * HALO
    vmem = pltpu.MemorySpace.VMEM
    smem = pltpu.MemorySpace.SMEM
    return pl.pallas_call(
        functools.partial(fine_kernel, slice_at),
        out_shape=jax.ShapeDtypeStruct(u.shape, u.dtype),
        in_specs=[pl.BlockSpec(memory_space=smem)] * 7 + [pl.BlockSpec(memory_space=vmem)] * 6,
        out_specs=pl.BlockSpec(memory_space=vmem),
        scratch_shapes=[
            pltpu.VMEM((2, tiles + 1, total, lanes), jnp.float32),
            pltpu.VMEM((4, tiles, total, lanes), jnp.float32),
        ],
        compiler_params=pltpu.CompilerParams(vmem_limit_bytes=48 * 1024 * 1024),
    )(*indices, scale, u, diffusivity, velocity, obstacle, from_prev, from_next)


def on_device(
    starts, diffusivity, velocity, obstacle, substep_scale, neighbors, coarse_x, coarse_y
):
    slice_count = starts.shape[0]
    tile_count = starts.shape[1]
    rows = starts.shape[2]
    all_tiles = tile_count * lax.axis_size("space")
    block_base = lax.axis_index("space") * tile_count

    def edge_rows(part):
        return jnp.concatenate(
            [
                starts[:, :, part, :],
                diffusivity[None, :, part, :],
                velocity[:, :, part, :],
                1.0 - obstacle[None, :, part, :].astype(jnp.float32),
            ],
            axis=0,
        )

    space_count = lax.axis_size("space")
    forward = [(i, i + 1) for i in range(space_count - 1)]
    backward = [(i + 1, i) for i in range(space_count - 1)]
    from_prev = lax.ppermute(edge_rows(slice(rows - HALO, None)), "space", forward)
    from_next = lax.ppermute(edge_rows(slice(0, HALO)), "space", backward)
    west_nb = neighbors[:, 0]
    east_nb = neighbors[:, 1]
    west_ok = (west_nb != all_tiles).astype(jnp.int32)
    east_ok = (east_nb != all_tiles).astype(jnp.int32)
    west_at = jnp.clip(west_nb - (block_base - tile_count), 0, tile_count - 1) * west_ok
    east_at = jnp.clip(east_nb - (block_base + tile_count), 0, tile_count - 1) * east_ok

    south_nb = neighbors[:, 2]
    north_nb = neighbors[:, 3]
    south_ok = (south_nb != all_tiles).astype(jnp.int32)
    north_ok = (north_nb != all_tiles).astype(jnp.int32)
    south = jnp.where(south_ok > 0, jnp.clip(south_nb - block_base, 0, tile_count - 1), tile_count)
    north = jnp.where(north_ok > 0, jnp.clip(north_nb - block_base, 0, tile_count - 1), tile_count)
    indices = (south, north, west_at, east_at, west_ok, east_ok)

    fine_ends = jnp.stack(
        [
            fine_propagate(
                n, starts[n], diffusivity, velocity, obstacle, from_prev, from_next, indices,
                substep_scale,
            )
            for n in range(slice_count)
        ],
        axis=0,
    )
    correction = fine_ends - prolong(apply_coarse(restrict(starts), coarse_x, coarse_y))
    coarse_jump = restrict(correction)
    late_x, late_y, coarse_jump = lax.optimization_barrier((coarse_x, coarse_y, coarse_jump))
    earlier_correction = passed_along(correction[-1], "tm", 1)
    tm_index = lax.axis_index("tm")
    tm_count = lax.axis_size("tm")
    first_coarse = restrict(starts[0])

    def prefix_over_tm(total, power_x, power_y):
        distances = []
        distance = 1
        while distance < tm_count:
            distances.append(distance)
            distance *= 2
        powers = {}
        for distance in distances:
            powers[distance] = (power_x, power_y)
            power_x = jnp.einsum("tij,tjk->tik", power_x, power_x, precision=exact_precision)
            power_y = jnp.einsum("tij,tjk->tik", power_y, power_y, precision=exact_precision)
        half = total.shape[0] // 2
        parts = [(slice(0, half), distances[:1] + distances[1:]),
                 (slice(half, None), distances[:1] + distances[1:][::-1])]
        values = [total[part] for part, _ in parts]
        for step in range(len(distances)):
            if step == 0:
                received = passed_along(total, "tm", distances[0])
                received = [received[part] for part, _ in parts]
            else:
                received = [passed_along(values[k], "tm", parts[k][1][step]) for k in range(2)]
            for k in range(2):
                part, order = parts[k]
                distance = order[step]
                mixed = apply_coarse(received[k], powers[distance][0][part], powers[distance][1][part])
                values[k] = values[k] + jnp.where(tm_index >= distance, mixed, 0.0)
        return jnp.concatenate(values, axis=0)

    if slice_count == 1:
        seed = jnp.where(tm_index == 0, apply_coarse(first_coarse, coarse_x, coarse_y), 0.0)
        reached = prefix_over_tm(coarse_jump[0] + seed, late_x, late_y)
        coarse_applied = (reached - coarse_jump[0])[None]
    else:
        shifted_jump = jnp.concatenate(
            [passed_along(coarse_jump[-1:], "tm", 1), coarse_jump[:-1]], axis=0
        )
        head = jnp.where(tm_index == 0, first_coarse[None], shifted_jump[:1])
        local = jnp.concatenate([head, shifted_jump[1:]], axis=0)
        states = [local[0]]
        for n in range(1, slice_count):
            states.append(apply_coarse(states[-1], coarse_x, coarse_y) + local[n])
        power_x = coarse_x
        power_y = coarse_y
        for n in range(1, slice_count):
            power_x = jnp.einsum("tij,tjk->tik", power_x, coarse_x, precision=exact_precision)
            power_y = jnp.einsum("tij,tjk->tik", power_y, coarse_y, precision=exact_precision)
        power_x, power_y, states = lax.optimization_barrier((power_x, power_y, states))
        total = prefix_over_tm(states[-1], power_x, power_y)
        earlier = jnp.where(tm_index > 0, passed_along(total, "tm", 1), 0.0)
        own_coarse = []
        for n in range(slice_count):
            earlier = apply_coarse(earlier, coarse_x, coarse_y)
            own_coarse.append(states[n] + earlier)
        coarse_applied = apply_coarse(jnp.stack(own_coarse, axis=0), coarse_x, coarse_y)
    slice_ends = prolong(coarse_applied) + correction
    previous = prolong(passed_along(coarse_applied[-1], "tm", 1)) + earlier_correction
    first_step = jnp.where(
        lax.axis_index("tm") == 0, jnp.zeros_like(previous), previous - starts[0]
    )
    increment = jnp.concatenate([first_step[None], slice_ends[:-1] - starts[1:]], axis=0)
    return (slice_ends, increment)


def solution(mesh):
    placed = (
        P("tm", "space", None, None),
        P("space", None, None),
        P(None, "space", None, None),
        P("space", None, None),
        P(),
        P("space", None),
        P("space", None, None),
        P("space", None, None),
    )
    return jax.shard_map(
        on_device,
        mesh=mesh,
        in_specs=placed,
        out_specs=(P("tm", "space", None, None), P("tm", "space", None, None)),
        check_vma=False,
    )
```

```python
import functools

import jax
import jax.numpy as jnp
from jax import lax
from jax.experimental import pallas as pl
from jax.experimental.pallas import tpu as pltpu
from jax.sharding import PartitionSpec as P

SUB = 12
HALO = 16
PAD = 8


exact_precision = lax.Precision.HIGHEST


def spread(value, axis, source):
    kept = jnp.where(lax.axis_index(axis) == source, value, 0).astype(value.dtype)
    return lax.psum(kept, axis)


def passed_along(block, axis, distance):
    devices = range(lax.axis_size(axis))
    route = [(i - distance, i) for i in devices if i - distance in devices]
    return lax.ppermute(block, axis, route)


def restrict(values):
    return 0.5 * (values[..., 0::2, :] + values[..., 1::2, :])


def prolong(coarse_values):
    return jnp.repeat(coarse_values, 2, axis=-2)


def apply_coarse(coarse_values, matrix_x, matrix_y):
    mixed_x = jnp.einsum("tij,...tjk->...tik", matrix_x, coarse_values, precision=exact_precision)
    return jnp.einsum("...tik,tlk->...til", mixed_x, matrix_y, precision=exact_precision)


def fine_kernel(slice_at, south_ref, north_ref, west_at_ref, east_at_ref, west_ok_ref, east_ok_ref,
                scale_ref, u_ref, diffusivity_ref, velocity_ref, obstacle_ref, prev_ref, next_ref,
                out_ref, state_ref, field_ref):
    tiles = u_ref.shape[0]
    rows = u_ref.shape[1]
    lanes = u_ref.shape[2]
    total = rows + 2 * HALO
    layers = prev_ref.shape[0]
    state_ref[...] = jnp.zeros(state_ref.shape, jnp.float32)
    for i in range(tiles):
        west_at = west_at_ref[i]
        east_at = east_at_ref[i]
        west_ok = west_ok_ref[i] > 0
        east_ok = east_ok_ref[i] > 0
        state_ref[0, i, pl.ds(PAD, HALO), :] = jnp.where(west_ok, prev_ref[slice_at, west_at], 0.0)
        state_ref[0, i, pl.ds(PAD + HALO, rows), :] = u_ref[i]
        state_ref[0, i, pl.ds(PAD + HALO + rows, HALO), :] = jnp.where(
            east_ok, next_ref[slice_at, east_at], 0.0
        )
        own = (
            diffusivity_ref[i],
            velocity_ref[0, i],
            velocity_ref[1, i],
            1.0 - obstacle_ref[i].astype(jnp.float32),
        )
        factor = (1.0, 0.5, 0.5, 1.0)
        for f in range(4):
            field_at = layers - 4 + f
            field_ref[f, i, pl.ds(0, HALO), :] = factor[f] * jnp.where(
                west_ok, prev_ref[field_at, west_at], 0.0
            )
            field_ref[f, i, pl.ds(HALO, rows), :] = factor[f] * own[f]
            field_ref[f, i, pl.ds(HALO + rows, HALO), :] = factor[f] * jnp.where(
                east_ok, next_ref[field_at, east_at], 0.0
            )

    lane = lax.broadcasted_iota(jnp.int32, (total, lanes), 1)
    first_lane = lane == 0
    last_lane = lane == lanes - 1

    def substep(s, carry):
        src = s % 2
        dst = 1 - src
        strength = scale_ref[s]
        for i in range(tiles):
            current = state_ref[src, i, pl.ds(PAD, total), :]
            south_tile = state_ref[src, south_ref[i], pl.ds(PAD, total), :]
            north_tile = state_ref[src, north_ref[i], pl.ds(PAD, total), :]
            from_west = state_ref[src, i, pl.ds(PAD - 1, total), :]
            from_east = state_ref[src, i, pl.ds(PAD + 1, total), :]
            from_south = pltpu.roll(jnp.where(last_lane, south_tile, current), 1, 1)
            from_north = pltpu.roll(jnp.where(first_lane, north_tile, current), lanes - 1, 1)
            diffusivity = field_ref[0, i]
            half_speed_x = field_ref[1, i]
            half_speed_y = field_ref[2, i]
            open_cells = field_ref[3, i]
            laplace = from_west + from_east + from_south + from_north - 4.0 * current
            half_transport = half_speed_x * (from_east - from_west) + half_speed_y * (
                from_north - from_south
            )
            state_ref[dst, i, pl.ds(PAD, total), :] = open_cells * (
                current + strength * diffusivity * laplace - half_transport
            )
        return carry

    lax.fori_loop(0, SUB, substep, 0)
    last = SUB % 2
    for i in range(tiles):
        out_ref[i] = state_ref[last, i, pl.ds(PAD + HALO, rows), :]


def fine_propagate(slice_at, u, diffusivity, velocity, obstacle, from_prev, from_next, indices, scale):
    tiles, rows, lanes = u.shape
    total = rows + 2 * HALO
    vmem = pltpu.MemorySpace.VMEM
    smem = pltpu.MemorySpace.SMEM
    return pl.pallas_call(
        functools.partial(fine_kernel, slice_at),
        out_shape=jax.ShapeDtypeStruct(u.shape, u.dtype),
        in_specs=[pl.BlockSpec(memory_space=smem)] * 7 + [pl.BlockSpec(memory_space=vmem)] * 6,
        out_specs=pl.BlockSpec(memory_space=vmem),
        scratch_shapes=[
            pltpu.VMEM((2, tiles + 1, total + 2 * PAD, lanes), jnp.float32),
            pltpu.VMEM((4, tiles, total, lanes), jnp.float32),
        ],
        compiler_params=pltpu.CompilerParams(vmem_limit_bytes=48 * 1024 * 1024),
    )(*indices, scale, u, diffusivity, velocity, obstacle, from_prev, from_next)


def on_device(
    starts, diffusivity, velocity, obstacle, substep_scale, neighbors, coarse_x, coarse_y
):
    slice_count = starts.shape[0]
    tile_count = starts.shape[1]
    rows = starts.shape[2]
    all_tiles = tile_count * lax.axis_size("space")
    block_base = lax.axis_index("space") * tile_count
    open_cells = 1.0 - obstacle.astype(jnp.float32)

    fields = jnp.stack([diffusivity, velocity[0], velocity[1], open_cells], axis=0)
    layers = jnp.concatenate([starts, fields], axis=0)
    space_count = lax.axis_size("space")
    forward = [(i, i + 1) for i in range(space_count - 1)]
    backward = [(i + 1, i) for i in range(space_count - 1)]
    from_prev = lax.ppermute(layers[:, :, rows - HALO:, :], "space", forward)
    from_next = lax.ppermute(layers[:, :, :HALO, :], "space", backward)
    west_nb = neighbors[:, 0]
    east_nb = neighbors[:, 1]
    west_ok = (west_nb != all_tiles).astype(jnp.int32)
    east_ok = (east_nb != all_tiles).astype(jnp.int32)
    west_at = jnp.clip(west_nb - (block_base - tile_count), 0, tile_count - 1) * west_ok
    east_at = jnp.clip(east_nb - (block_base + tile_count), 0, tile_count - 1) * east_ok

    south_nb = neighbors[:, 2]
    north_nb = neighbors[:, 3]
    south_ok = (south_nb != all_tiles).astype(jnp.int32)
    north_ok = (north_nb != all_tiles).astype(jnp.int32)
    south = jnp.where(south_ok > 0, jnp.clip(south_nb - block_base, 0, tile_count - 1), tile_count)
    north = jnp.where(north_ok > 0, jnp.clip(north_nb - block_base, 0, tile_count - 1), tile_count)
    indices = (south, north, west_at, east_at, west_ok, east_ok)

    fine_ends = jnp.stack(
        [
            fine_propagate(
                n, starts[n], diffusivity, velocity, obstacle, from_prev, from_next, indices,
                substep_scale,
            )
            for n in range(slice_count)
        ],
        axis=0,
    )
    correction = fine_ends - prolong(apply_coarse(restrict(starts), coarse_x, coarse_y))
    coarse_jump = restrict(correction)
    earlier_correction = passed_along(correction[-1], "tm", 1)
    tm_index = lax.axis_index("tm")
    tm_count = lax.axis_size("tm")
    first_coarse = restrict(starts[0])

    def prefix_over_tm(total, power_x, power_y):
        distances = []
        distance = 1
        while distance < tm_count:
            distances.append(distance)
            distance *= 2
        powers = {}
        for distance in distances:
            powers[distance] = (power_x, power_y)
            power_x = jnp.einsum("tij,tjk->tik", power_x, power_x, precision=exact_precision)
            power_y = jnp.einsum("tij,tjk->tik", power_y, power_y, precision=exact_precision)
        half = total.shape[0] // 2
        parts = [(slice(0, half), distances[:1] + distances[1:]),
                 (slice(half, None), distances[:1] + distances[1:][::-1])]
        values = [total[part] for part, _ in parts]
        for step in range(len(distances)):
            if step == 0:
                received = passed_along(total, "tm", distances[0])
                received = [received[part] for part, _ in parts]
            else:
                received = [passed_along(values[k], "tm", parts[k][1][step]) for k in range(2)]
            for k in range(2):
                part, order = parts[k]
                distance = order[step]
                mixed = apply_coarse(received[k], powers[distance][0][part], powers[distance][1][part])
                values[k] = values[k] + jnp.where(tm_index >= distance, mixed, 0.0)
        return jnp.concatenate(values, axis=0)

    if slice_count == 1:
        seed = jnp.where(tm_index == 0, apply_coarse(first_coarse, coarse_x, coarse_y), 0.0)
        reached = prefix_over_tm(coarse_jump[0] + seed, coarse_x, coarse_y)
        coarse_applied = (reached - coarse_jump[0])[None]
    else:
        shifted_jump = jnp.concatenate(
            [passed_along(coarse_jump[-1:], "tm", 1), coarse_jump[:-1]], axis=0
        )
        head = jnp.where(tm_index == 0, first_coarse[None], shifted_jump[:1])
        local = jnp.concatenate([head, shifted_jump[1:]], axis=0)
        states = [local[0]]
        for n in range(1, slice_count):
            states.append(apply_coarse(states[-1], coarse_x, coarse_y) + local[n])
        power_x = coarse_x
        power_y = coarse_y
        for n in range(1, slice_count):
            power_x = jnp.einsum("tij,tjk->tik", power_x, coarse_x, precision=exact_precision)
            power_y = jnp.einsum("tij,tjk->tik", power_y, coarse_y, precision=exact_precision)
        total = prefix_over_tm(states[-1], power_x, power_y)
        earlier = jnp.where(tm_index > 0, passed_along(total, "tm", 1), 0.0)
        own_coarse = []
        for n in range(slice_count):
            earlier = apply_coarse(earlier, coarse_x, coarse_y)
            own_coarse.append(states[n] + earlier)
        coarse_applied = apply_coarse(jnp.stack(own_coarse, axis=0), coarse_x, coarse_y)
    slice_ends = prolong(coarse_applied) + correction
    previous = prolong(passed_along(coarse_applied[-1], "tm", 1)) + earlier_correction
    first_step = jnp.where(
        lax.axis_index("tm") == 0, jnp.zeros_like(previous), previous - starts[0]
    )
    increment = jnp.concatenate([first_step[None], slice_ends[:-1] - starts[1:]], axis=0)
    return (slice_ends, increment)


def solution(mesh):
    placed = (
        P("tm", "space", None, None),
        P("space", None, None),
        P(None, "space", None, None),
        P("space", None, None),
        P(),
        P("space", None),
        P("space", None, None),
        P("space", None, None),
    )
    return jax.shard_map(
        on_device,
        mesh=mesh,
        in_specs=placed,
        out_specs=(P("tm", "space", None, None), P("tm", "space", None, None)),
        check_vma=False,
    )
```

```python
import functools

import jax
import jax.numpy as jnp
from jax import lax
from jax.experimental import pallas as pl
from jax.experimental.pallas import tpu as pltpu
from jax.sharding import PartitionSpec as P

SUB = 12
HALO = 16
PAD = 8


exact_precision = lax.Precision.HIGHEST


def spread(value, axis, source):
    kept = jnp.where(lax.axis_index(axis) == source, value, 0).astype(value.dtype)
    return lax.psum(kept, axis)


def passed_along(block, axis, distance):
    devices = range(lax.axis_size(axis))
    route = [(i - distance, i) for i in devices if i - distance in devices]
    return lax.ppermute(block, axis, route)


def restrict(values):
    return 0.5 * (values[..., 0::2, :] + values[..., 1::2, :])


def prolong(coarse_values):
    return jnp.repeat(coarse_values, 2, axis=-2)


def apply_coarse(coarse_values, matrix_x, matrix_y):
    mixed_x = jnp.einsum("tij,...tjk->...tik", matrix_x, coarse_values, precision=exact_precision)
    return jnp.einsum("...tik,tlk->...til", mixed_x, matrix_y, precision=exact_precision)


def fine_kernel(slice_at, south_ref, north_ref, west_at_ref, east_at_ref, west_ok_ref, east_ok_ref,
                scale_ref, u_ref, diffusivity_ref, velocity_ref, obstacle_ref, prev_ref, next_ref,
                out_ref, state_ref, field_ref):
    tiles = u_ref.shape[0]
    rows = u_ref.shape[1]
    lanes = u_ref.shape[2]
    total = rows + 2 * HALO
    layers = prev_ref.shape[0]
    state_ref[...] = jnp.zeros(state_ref.shape, jnp.float32)
    for i in range(tiles):
        west_at = west_at_ref[i]
        east_at = east_at_ref[i]
        west_ok = west_ok_ref[i] > 0
        east_ok = east_ok_ref[i] > 0
        state_ref[0, i, pl.ds(PAD, HALO), :] = jnp.where(west_ok, prev_ref[slice_at, west_at], 0.0)
        state_ref[0, i, pl.ds(PAD + HALO, rows), :] = u_ref[i]
        state_ref[0, i, pl.ds(PAD + HALO + rows, HALO), :] = jnp.where(
            east_ok, next_ref[slice_at, east_at], 0.0
        )
        own = (
            diffusivity_ref[i],
            velocity_ref[0, i],
            velocity_ref[1, i],
            1.0 - obstacle_ref[i].astype(jnp.float32),
        )
        factor = (1.0, 0.5, 0.5, 1.0)
        for f in range(4):
            field_at = layers - 4 + f
            field_ref[f, i, pl.ds(0, HALO), :] = factor[f] * jnp.where(
                west_ok, prev_ref[field_at, west_at], 0.0
            )
            field_ref[f, i, pl.ds(HALO, rows), :] = factor[f] * own[f]
            field_ref[f, i, pl.ds(HALO + rows, HALO), :] = factor[f] * jnp.where(
                east_ok, next_ref[field_at, east_at], 0.0
            )

    chunk = 16
    lane = lax.broadcasted_iota(jnp.int32, (chunk, lanes), 1)
    first_lane = lane == 0
    last_lane = lane == lanes - 1

    def substep(s, carry):
        src = s % 2
        dst = 1 - src
        strength = scale_ref[s]
        for i in range(tiles):
            south_at = south_ref[i]
            north_at = north_ref[i]
            for start in range(0, total, chunk):
                rows_at = pl.ds(PAD + start, chunk)
                current = state_ref[src, i, rows_at, :]
                south_tile = state_ref[src, south_at, rows_at, :]
                north_tile = state_ref[src, north_at, rows_at, :]
                from_west = state_ref[src, i, pl.ds(PAD + start - 1, chunk), :]
                from_east = state_ref[src, i, pl.ds(PAD + start + 1, chunk), :]
                from_south = pltpu.roll(jnp.where(last_lane, south_tile, current), 1, 1)
                from_north = pltpu.roll(jnp.where(first_lane, north_tile, current), lanes - 1, 1)
                diffusivity = field_ref[0, i, pl.ds(start, chunk), :]
                half_speed_x = field_ref[1, i, pl.ds(start, chunk), :]
                half_speed_y = field_ref[2, i, pl.ds(start, chunk), :]
                open_cells = field_ref[3, i, pl.ds(start, chunk), :]
                laplace = from_west + from_east + from_south + from_north - 4.0 * current
                half_transport = half_speed_x * (from_east - from_west) + half_speed_y * (
                    from_north - from_south
                )
                state_ref[dst, i, rows_at, :] = open_cells * (
                    current + strength * diffusivity * laplace - half_transport
                )
        return carry

    lax.fori_loop(0, SUB, substep, 0)
    last = SUB % 2
    for i in range(tiles):
        out_ref[i] = state_ref[last, i, pl.ds(PAD + HALO, rows), :]


def fine_propagate(slice_at, u, diffusivity, velocity, obstacle, from_prev, from_next, indices, scale):
    tiles, rows, lanes = u.shape
    total = rows + 2 * HALO
    vmem = pltpu.MemorySpace.VMEM
    smem = pltpu.MemorySpace.SMEM
    return pl.pallas_call(
        functools.partial(fine_kernel, slice_at),
        out_shape=jax.ShapeDtypeStruct(u.shape, u.dtype),
        in_specs=[pl.BlockSpec(memory_space=smem)] * 7 + [pl.BlockSpec(memory_space=vmem)] * 6,
        out_specs=pl.BlockSpec(memory_space=vmem),
        scratch_shapes=[
            pltpu.VMEM((2, tiles + 1, total + 2 * PAD, lanes), jnp.float32),
            pltpu.VMEM((4, tiles, total, lanes), jnp.float32),
        ],
        compiler_params=pltpu.CompilerParams(vmem_limit_bytes=48 * 1024 * 1024),
    )(*indices, scale, u, diffusivity, velocity, obstacle, from_prev, from_next)


def on_device(
    starts, diffusivity, velocity, obstacle, substep_scale, neighbors, coarse_x, coarse_y
):
    slice_count = starts.shape[0]
    tile_count = starts.shape[1]
    rows = starts.shape[2]
    all_tiles = tile_count * lax.axis_size("space")
    block_base = lax.axis_index("space") * tile_count
    open_cells = 1.0 - obstacle.astype(jnp.float32)

    fields = jnp.stack([diffusivity, velocity[0], velocity[1], open_cells], axis=0)
    layers = jnp.concatenate([starts, fields], axis=0)
    space_count = lax.axis_size("space")
    forward = [(i, i + 1) for i in range(space_count - 1)]
    backward = [(i + 1, i) for i in range(space_count - 1)]
    from_prev = lax.ppermute(layers[:, :, rows - HALO:, :], "space", forward)
    from_next = lax.ppermute(layers[:, :, :HALO, :], "space", backward)
    west_nb = neighbors[:, 0]
    east_nb = neighbors[:, 1]
    west_ok = (west_nb != all_tiles).astype(jnp.int32)
    east_ok = (east_nb != all_tiles).astype(jnp.int32)
    west_at = jnp.clip(west_nb - (block_base - tile_count), 0, tile_count - 1) * west_ok
    east_at = jnp.clip(east_nb - (block_base + tile_count), 0, tile_count - 1) * east_ok

    south_nb = neighbors[:, 2]
    north_nb = neighbors[:, 3]
    south_ok = (south_nb != all_tiles).astype(jnp.int32)
    north_ok = (north_nb != all_tiles).astype(jnp.int32)
    south = jnp.where(south_ok > 0, jnp.clip(south_nb - block_base, 0, tile_count - 1), tile_count)
    north = jnp.where(north_ok > 0, jnp.clip(north_nb - block_base, 0, tile_count - 1), tile_count)
    indices = (south, north, west_at, east_at, west_ok, east_ok)

    fine_ends = jnp.stack(
        [
            fine_propagate(
                n, starts[n], diffusivity, velocity, obstacle, from_prev, from_next, indices,
                substep_scale,
            )
            for n in range(slice_count)
        ],
        axis=0,
    )
    correction = fine_ends - prolong(apply_coarse(restrict(starts), coarse_x, coarse_y))
    coarse_jump = restrict(correction)
    earlier_correction = passed_along(correction[-1], "tm", 1)
    tm_index = lax.axis_index("tm")
    tm_count = lax.axis_size("tm")
    first_coarse = restrict(starts[0])

    def prefix_over_tm(total, power_x, power_y):
        distances = []
        distance = 1
        while distance < tm_count:
            distances.append(distance)
            distance *= 2
        powers = {}
        for distance in distances:
            powers[distance] = (power_x, power_y)
            power_x = jnp.einsum("tij,tjk->tik", power_x, power_x, precision=exact_precision)
            power_y = jnp.einsum("tij,tjk->tik", power_y, power_y, precision=exact_precision)
        half = total.shape[0] // 2
        parts = [(slice(0, half), distances[:1] + distances[1:]),
                 (slice(half, None), distances[:1] + distances[1:][::-1])]
        values = [total[part] for part, _ in parts]
        for step in range(len(distances)):
            if step == 0:
                received = passed_along(total, "tm", distances[0])
                received = [received[part] for part, _ in parts]
            else:
                received = [passed_along(values[k], "tm", parts[k][1][step]) for k in range(2)]
            for k in range(2):
                part, order = parts[k]
                distance = order[step]
                mixed = apply_coarse(received[k], powers[distance][0][part], powers[distance][1][part])
                values[k] = values[k] + jnp.where(tm_index >= distance, mixed, 0.0)
        return jnp.concatenate(values, axis=0)

    if slice_count == 1:
        seed = jnp.where(tm_index == 0, apply_coarse(first_coarse, coarse_x, coarse_y), 0.0)
        reached = prefix_over_tm(coarse_jump[0] + seed, coarse_x, coarse_y)
        coarse_applied = (reached - coarse_jump[0])[None]
    else:
        shifted_jump = jnp.concatenate(
            [passed_along(coarse_jump[-1:], "tm", 1), coarse_jump[:-1]], axis=0
        )
        head = jnp.where(tm_index == 0, first_coarse[None], shifted_jump[:1])
        local = jnp.concatenate([head, shifted_jump[1:]], axis=0)
        states = [local[0]]
        for n in range(1, slice_count):
            states.append(apply_coarse(states[-1], coarse_x, coarse_y) + local[n])
        power_x = coarse_x
        power_y = coarse_y
        for n in range(1, slice_count):
            power_x = jnp.einsum("tij,tjk->tik", power_x, coarse_x, precision=exact_precision)
            power_y = jnp.einsum("tij,tjk->tik", power_y, coarse_y, precision=exact_precision)
        total = prefix_over_tm(states[-1], power_x, power_y)
        earlier = jnp.where(tm_index > 0, passed_along(total, "tm", 1), 0.0)
        own_coarse = []
        for n in range(slice_count):
            earlier = apply_coarse(earlier, coarse_x, coarse_y)
            own_coarse.append(states[n] + earlier)
        coarse_applied = apply_coarse(jnp.stack(own_coarse, axis=0), coarse_x, coarse_y)
    slice_ends = prolong(coarse_applied) + correction
    previous = prolong(passed_along(coarse_applied[-1], "tm", 1)) + earlier_correction
    first_step = jnp.where(
        lax.axis_index("tm") == 0, jnp.zeros_like(previous), previous - starts[0]
    )
    increment = jnp.concatenate([first_step[None], slice_ends[:-1] - starts[1:]], axis=0)
    return (slice_ends, increment)


def solution(mesh):
    placed = (
        P("tm", "space", None, None),
        P("space", None, None),
        P(None, "space", None, None),
        P("space", None, None),
        P(),
        P("space", None),
        P("space", None, None),
        P("space", None, None),
    )
    return jax.shard_map(
        on_device,
        mesh=mesh,
        in_specs=placed,
        out_specs=(P("tm", "space", None, None), P("tm", "space", None, None)),
        check_vma=False,
    )
```

```python
import functools

import jax
import jax.numpy as jnp
from jax import lax
from jax.experimental import pallas as pl
from jax.experimental.pallas import tpu as pltpu
from jax.sharding import PartitionSpec as P

SUB = 12
HALO = 16
PAD = 8


exact_precision = lax.Precision.HIGHEST


def spread(value, axis, source):
    kept = jnp.where(lax.axis_index(axis) == source, value, 0).astype(value.dtype)
    return lax.psum(kept, axis)


def passed_along(block, axis, distance):
    devices = range(lax.axis_size(axis))
    route = [(i - distance, i) for i in devices if i - distance in devices]
    return lax.ppermute(block, axis, route)


def restrict(values):
    return 0.5 * (values[..., 0::2, :] + values[..., 1::2, :])


def prolong(coarse_values):
    return jnp.repeat(coarse_values, 2, axis=-2)


def apply_coarse(coarse_values, matrix_x, matrix_y):
    mixed_x = jnp.einsum("tij,...tjk->...tik", matrix_x, coarse_values, precision=exact_precision)
    return jnp.einsum("...tik,tlk->...til", mixed_x, matrix_y, precision=exact_precision)


def fine_kernel(slice_at, south_ref, north_ref, west_at_ref, east_at_ref, west_ok_ref, east_ok_ref,
                scale_ref, u_ref, diffusivity_ref, velocity_ref, obstacle_ref, prev_ref, next_ref,
                out_ref, state_ref, other_ref, field_ref):
    tiles = u_ref.shape[0]
    rows = u_ref.shape[1]
    lanes = u_ref.shape[2]
    total = rows + 2 * HALO
    layers = prev_ref.shape[0]
    state_ref[...] = jnp.zeros(state_ref.shape, jnp.float32)
    other_ref[...] = jnp.zeros(other_ref.shape, jnp.float32)
    for i in range(tiles):
        west_at = west_at_ref[i]
        east_at = east_at_ref[i]
        west_ok = west_ok_ref[i] > 0
        east_ok = east_ok_ref[i] > 0
        state_ref[i, pl.ds(PAD, HALO), :] = jnp.where(west_ok, prev_ref[slice_at, west_at], 0.0)
        state_ref[i, pl.ds(PAD + HALO, rows), :] = u_ref[i]
        state_ref[i, pl.ds(PAD + HALO + rows, HALO), :] = jnp.where(
            east_ok, next_ref[slice_at, east_at], 0.0
        )
        own = (
            diffusivity_ref[i],
            velocity_ref[0, i],
            velocity_ref[1, i],
            1.0 - obstacle_ref[i].astype(jnp.float32),
        )
        factor = (1.0, 0.5, 0.5, 1.0)
        for f in range(4):
            field_at = layers - 4 + f
            field_ref[f, i, pl.ds(0, HALO), :] = factor[f] * jnp.where(
                west_ok, prev_ref[field_at, west_at], 0.0
            )
            field_ref[f, i, pl.ds(HALO, rows), :] = factor[f] * own[f]
            field_ref[f, i, pl.ds(HALO + rows, HALO), :] = factor[f] * jnp.where(
                east_ok, next_ref[field_at, east_at], 0.0
            )

    chunk = 16
    lane = lax.broadcasted_iota(jnp.int32, (chunk, lanes), 1)
    first_lane = lane == 0
    last_lane = lane == lanes - 1

    def substep(strength, src_ref, dst_ref):
        for i in range(tiles):
            south_at = south_ref[i]
            north_at = north_ref[i]
            for start in range(0, total, chunk):
                rows_at = pl.ds(PAD + start, chunk)
                current = src_ref[i, rows_at, :]
                south_tile = src_ref[south_at, rows_at, :]
                north_tile = src_ref[north_at, rows_at, :]
                from_west = src_ref[i, pl.ds(PAD + start - 1, chunk), :]
                from_east = src_ref[i, pl.ds(PAD + start + 1, chunk), :]
                from_south = pltpu.roll(jnp.where(last_lane, south_tile, current), 1, 1)
                from_north = pltpu.roll(jnp.where(first_lane, north_tile, current), lanes - 1, 1)
                diffusivity = field_ref[0, i, pl.ds(start, chunk), :]
                half_speed_x = field_ref[1, i, pl.ds(start, chunk), :]
                half_speed_y = field_ref[2, i, pl.ds(start, chunk), :]
                open_cells = field_ref[3, i, pl.ds(start, chunk), :]
                laplace = from_west + from_east + from_south + from_north - 4.0 * current
                half_transport = half_speed_x * (from_east - from_west) + half_speed_y * (
                    from_north - from_south
                )
                dst_ref[i, rows_at, :] = open_cells * (
                    current + strength * diffusivity * laplace - half_transport
                )

    def substep_pair(p, carry):
        substep(scale_ref[2 * p], state_ref, other_ref)
        substep(scale_ref[2 * p + 1], other_ref, state_ref)
        return carry

    lax.fori_loop(0, SUB // 2, substep_pair, 0)
    final_ref = state_ref
    if SUB % 2:
        substep(scale_ref[SUB - 1], state_ref, other_ref)
        final_ref = other_ref
    for i in range(tiles):
        out_ref[i] = final_ref[i, pl.ds(PAD + HALO, rows), :]


def fine_propagate(slice_at, u, diffusivity, velocity, obstacle, from_prev, from_next, indices, scale):
    tiles, rows, lanes = u.shape
    total = rows + 2 * HALO
    vmem = pltpu.MemorySpace.VMEM
    smem = pltpu.MemorySpace.SMEM
    return pl.pallas_call(
        functools.partial(fine_kernel, slice_at),
        out_shape=jax.ShapeDtypeStruct(u.shape, u.dtype),
        in_specs=[pl.BlockSpec(memory_space=smem)] * 7 + [pl.BlockSpec(memory_space=vmem)] * 6,
        out_specs=pl.BlockSpec(memory_space=vmem),
        scratch_shapes=[
            pltpu.VMEM((tiles + 1, total + 2 * PAD, lanes), jnp.float32),
            pltpu.VMEM((tiles + 1, total + 2 * PAD, lanes), jnp.float32),
            pltpu.VMEM((4, tiles, total, lanes), jnp.float32),
        ],
        compiler_params=pltpu.CompilerParams(vmem_limit_bytes=48 * 1024 * 1024),
    )(*indices, scale, u, diffusivity, velocity, obstacle, from_prev, from_next)


def on_device(
    starts, diffusivity, velocity, obstacle, substep_scale, neighbors, coarse_x, coarse_y
):
    slice_count = starts.shape[0]
    tile_count = starts.shape[1]
    rows = starts.shape[2]
    all_tiles = tile_count * lax.axis_size("space")
    block_base = lax.axis_index("space") * tile_count
    open_cells = 1.0 - obstacle.astype(jnp.float32)

    fields = jnp.stack([diffusivity, velocity[0], velocity[1], open_cells], axis=0)
    layers = jnp.concatenate([starts, fields], axis=0)
    space_count = lax.axis_size("space")
    forward = [(i, i + 1) for i in range(space_count - 1)]
    backward = [(i + 1, i) for i in range(space_count - 1)]
    from_prev = lax.ppermute(layers[:, :, rows - HALO:, :], "space", forward)
    from_next = lax.ppermute(layers[:, :, :HALO, :], "space", backward)
    west_nb = neighbors[:, 0]
    east_nb = neighbors[:, 1]
    west_ok = (west_nb != all_tiles).astype(jnp.int32)
    east_ok = (east_nb != all_tiles).astype(jnp.int32)
    west_at = jnp.clip(west_nb - (block_base - tile_count), 0, tile_count - 1) * west_ok
    east_at = jnp.clip(east_nb - (block_base + tile_count), 0, tile_count - 1) * east_ok

    south_nb = neighbors[:, 2]
    north_nb = neighbors[:, 3]
    south_ok = (south_nb != all_tiles).astype(jnp.int32)
    north_ok = (north_nb != all_tiles).astype(jnp.int32)
    south = jnp.where(south_ok > 0, jnp.clip(south_nb - block_base, 0, tile_count - 1), tile_count)
    north = jnp.where(north_ok > 0, jnp.clip(north_nb - block_base, 0, tile_count - 1), tile_count)
    indices = (south, north, west_at, east_at, west_ok, east_ok)

    fine_ends = jnp.stack(
        [
            fine_propagate(
                n, starts[n], diffusivity, velocity, obstacle, from_prev, from_next, indices,
                substep_scale,
            )
            for n in range(slice_count)
        ],
        axis=0,
    )
    correction = fine_ends - prolong(apply_coarse(restrict(starts), coarse_x, coarse_y))
    coarse_jump = restrict(correction)
    earlier_correction = passed_along(correction[-1], "tm", 1)
    tm_index = lax.axis_index("tm")
    tm_count = lax.axis_size("tm")
    first_coarse = restrict(starts[0])

    def prefix_over_tm(total, power_x, power_y):
        distances = []
        distance = 1
        while distance < tm_count:
            distances.append(distance)
            distance *= 2
        powers = {}
        for distance in distances:
            powers[distance] = (power_x, power_y)
            power_x = jnp.einsum("tij,tjk->tik", power_x, power_x, precision=exact_precision)
            power_y = jnp.einsum("tij,tjk->tik", power_y, power_y, precision=exact_precision)
        half = total.shape[0] // 2
        parts = [(slice(0, half), distances[:1] + distances[1:]),
                 (slice(half, None), distances[:1] + distances[1:][::-1])]
        values = [total[part] for part, _ in parts]
        for step in range(len(distances)):
            if step == 0:
                received = passed_along(total, "tm", distances[0])
                received = [received[part] for part, _ in parts]
            else:
                received = [passed_along(values[k], "tm", parts[k][1][step]) for k in range(2)]
            for k in range(2):
                part, order = parts[k]
                distance = order[step]
                mixed = apply_coarse(received[k], powers[distance][0][part], powers[distance][1][part])
                values[k] = values[k] + jnp.where(tm_index >= distance, mixed, 0.0)
        return jnp.concatenate(values, axis=0)

    if slice_count == 1:
        seed = jnp.where(tm_index == 0, apply_coarse(first_coarse, coarse_x, coarse_y), 0.0)
        reached = prefix_over_tm(coarse_jump[0] + seed, coarse_x, coarse_y)
        coarse_applied = (reached - coarse_jump[0])[None]
    else:
        shifted_jump = jnp.concatenate(
            [passed_along(coarse_jump[-1:], "tm", 1), coarse_jump[:-1]], axis=0
        )
        head = jnp.where(tm_index == 0, first_coarse[None], shifted_jump[:1])
        local = jnp.concatenate([head, shifted_jump[1:]], axis=0)
        states = [local[0]]
        for n in range(1, slice_count):
            states.append(apply_coarse(states[-1], coarse_x, coarse_y) + local[n])
        power_x = coarse_x
        power_y = coarse_y
        for n in range(1, slice_count):
            power_x = jnp.einsum("tij,tjk->tik", power_x, coarse_x, precision=exact_precision)
            power_y = jnp.einsum("tij,tjk->tik", power_y, coarse_y, precision=exact_precision)
        total = prefix_over_tm(states[-1], power_x, power_y)
        earlier = jnp.where(tm_index > 0, passed_along(total, "tm", 1), 0.0)
        own_coarse = []
        for n in range(slice_count):
            earlier = apply_coarse(earlier, coarse_x, coarse_y)
            own_coarse.append(states[n] + earlier)
        coarse_applied = apply_coarse(jnp.stack(own_coarse, axis=0), coarse_x, coarse_y)
    slice_ends = prolong(coarse_applied) + correction
    previous = prolong(passed_along(coarse_applied[-1], "tm", 1)) + earlier_correction
    first_step = jnp.where(
        lax.axis_index("tm") == 0, jnp.zeros_like(previous), previous - starts[0]
    )
    increment = jnp.concatenate([first_step[None], slice_ends[:-1] - starts[1:]], axis=0)
    return (slice_ends, increment)


def solution(mesh):
    placed = (
        P("tm", "space", None, None),
        P("space", None, None),
        P(None, "space", None, None),
        P("space", None, None),
        P(),
        P("space", None),
        P("space", None, None),
        P("space", None, None),
    )
    return jax.shard_map(
        on_device,
        mesh=mesh,
        in_specs=placed,
        out_specs=(P("tm", "space", None, None), P("tm", "space", None, None)),
        check_vma=False,
    )
```

```python
import functools

import jax
import jax.numpy as jnp
from jax import lax
from jax.experimental import pallas as pl
from jax.experimental.pallas import tpu as pltpu
from jax.sharding import PartitionSpec as P

SUB = 12
HALO = 16
PAD = 8


exact_precision = lax.Precision.HIGHEST


def spread(value, axis, source):
    kept = jnp.where(lax.axis_index(axis) == source, value, 0).astype(value.dtype)
    return lax.psum(kept, axis)


def passed_along(block, axis, distance):
    devices = range(lax.axis_size(axis))
    route = [(i - distance, i) for i in devices if i - distance in devices]
    return lax.ppermute(block, axis, route)


def restrict(values):
    return 0.5 * (values[..., 0::2, :] + values[..., 1::2, :])


def prolong(coarse_values):
    return jnp.repeat(coarse_values, 2, axis=-2)


def apply_coarse(coarse_values, matrix_x, matrix_y):
    mixed_x = jnp.einsum("tij,...tjk->...tik", matrix_x, coarse_values, precision=exact_precision)
    return jnp.einsum("...tik,tlk->...til", mixed_x, matrix_y, precision=exact_precision)


def fine_kernel(slice_at, south_ref, north_ref, west_at_ref, east_at_ref, west_ok_ref, east_ok_ref,
                scale_ref, u_ref, diffusivity_ref, velocity_ref, obstacle_ref, prev_ref, next_ref,
                out_ref, state_ref, other_ref, field_ref):
    tiles = u_ref.shape[0]
    rows = u_ref.shape[1]
    lanes = u_ref.shape[2]
    total = rows + 2 * HALO
    layers = prev_ref.shape[0]
    for ref in (state_ref, other_ref):
        ref[tiles] = jnp.zeros(ref.shape[1:], jnp.float32)
        for i in range(tiles):
            ref[i, pl.ds(0, PAD), :] = jnp.zeros((PAD, lanes), jnp.float32)
            ref[i, pl.ds(PAD + total, PAD), :] = jnp.zeros((PAD, lanes), jnp.float32)
    for i in range(tiles):
        west_at = west_at_ref[i]
        east_at = east_at_ref[i]
        west_ok = west_ok_ref[i] > 0
        east_ok = east_ok_ref[i] > 0
        state_ref[i, pl.ds(PAD, HALO), :] = jnp.where(west_ok, prev_ref[slice_at, west_at], 0.0)
        state_ref[i, pl.ds(PAD + HALO, rows), :] = u_ref[i]
        state_ref[i, pl.ds(PAD + HALO + rows, HALO), :] = jnp.where(
            east_ok, next_ref[slice_at, east_at], 0.0
        )
        own = (
            diffusivity_ref[i],
            velocity_ref[0, i],
            velocity_ref[1, i],
            1.0 - obstacle_ref[i].astype(jnp.float32),
        )
        factor = (1.0, 0.5, 0.5, 1.0)
        for f in range(4):
            field_at = layers - 4 + f
            field_ref[f, i, pl.ds(0, HALO), :] = factor[f] * jnp.where(
                west_ok, prev_ref[field_at, west_at], 0.0
            )
            field_ref[f, i, pl.ds(HALO, rows), :] = factor[f] * own[f]
            field_ref[f, i, pl.ds(HALO + rows, HALO), :] = factor[f] * jnp.where(
                east_ok, next_ref[field_at, east_at], 0.0
            )

    chunk = 16
    lane = lax.broadcasted_iota(jnp.int32, (chunk, lanes), 1)
    first_lane = lane == 0
    last_lane = lane == lanes - 1

    def substep(strength, src_ref, dst_ref):
        for i in range(tiles):
            south_at = south_ref[i]
            north_at = north_ref[i]
            for start in range(0, total, chunk):
                rows_at = pl.ds(PAD + start, chunk)
                current = src_ref[i, rows_at, :]
                south_tile = src_ref[south_at, rows_at, :]
                north_tile = src_ref[north_at, rows_at, :]
                from_west = src_ref[i, pl.ds(PAD + start - 1, chunk), :]
                from_east = src_ref[i, pl.ds(PAD + start + 1, chunk), :]
                from_south = pltpu.roll(jnp.where(last_lane, south_tile, current), 1, 1)
                from_north = pltpu.roll(jnp.where(first_lane, north_tile, current), lanes - 1, 1)
                diffusivity = field_ref[0, i, pl.ds(start, chunk), :]
                half_speed_x = field_ref[1, i, pl.ds(start, chunk), :]
                half_speed_y = field_ref[2, i, pl.ds(start, chunk), :]
                open_cells = field_ref[3, i, pl.ds(start, chunk), :]
                laplace = from_west + from_east + from_south + from_north - 4.0 * current
                half_transport = half_speed_x * (from_east - from_west) + half_speed_y * (
                    from_north - from_south
                )
                dst_ref[i, rows_at, :] = open_cells * (
                    current + strength * diffusivity * laplace - half_transport
                )

    def substep_pair(p, carry):
        substep(scale_ref[2 * p], state_ref, other_ref)
        substep(scale_ref[2 * p + 1], other_ref, state_ref)
        return carry

    lax.fori_loop(0, SUB // 2, substep_pair, 0)
    final_ref = state_ref
    if SUB % 2:
        substep(scale_ref[SUB - 1], state_ref, other_ref)
        final_ref = other_ref
    for i in range(tiles):
        out_ref[i] = final_ref[i, pl.ds(PAD + HALO, rows), :]


def fine_propagate(slice_at, u, diffusivity, velocity, obstacle, from_prev, from_next, indices, scale):
    tiles, rows, lanes = u.shape
    total = rows + 2 * HALO
    vmem = pltpu.MemorySpace.VMEM
    smem = pltpu.MemorySpace.SMEM
    return pl.pallas_call(
        functools.partial(fine_kernel, slice_at),
        out_shape=jax.ShapeDtypeStruct(u.shape, u.dtype),
        in_specs=[pl.BlockSpec(memory_space=smem)] * 7 + [pl.BlockSpec(memory_space=vmem)] * 6,
        out_specs=pl.BlockSpec(memory_space=vmem),
        scratch_shapes=[
            pltpu.VMEM((tiles + 1, total + 2 * PAD, lanes), jnp.float32),
            pltpu.VMEM((tiles + 1, total + 2 * PAD, lanes), jnp.float32),
            pltpu.VMEM((4, tiles, total, lanes), jnp.float32),
        ],
        compiler_params=pltpu.CompilerParams(vmem_limit_bytes=48 * 1024 * 1024),
    )(*indices, scale, u, diffusivity, velocity, obstacle, from_prev, from_next)


def on_device(
    starts, diffusivity, velocity, obstacle, substep_scale, neighbors, coarse_x, coarse_y
):
    slice_count = starts.shape[0]
    tile_count = starts.shape[1]
    rows = starts.shape[2]
    all_tiles = tile_count * lax.axis_size("space")
    block_base = lax.axis_index("space") * tile_count
    open_cells = 1.0 - obstacle.astype(jnp.float32)

    fields = jnp.stack([diffusivity, velocity[0], velocity[1], open_cells], axis=0)
    layers = jnp.concatenate([starts, fields], axis=0)
    space_count = lax.axis_size("space")
    forward = [(i, i + 1) for i in range(space_count - 1)]
    backward = [(i + 1, i) for i in range(space_count - 1)]
    from_prev = lax.ppermute(layers[:, :, rows - HALO:, :], "space", forward)
    from_next = lax.ppermute(layers[:, :, :HALO, :], "space", backward)
    west_nb = neighbors[:, 0]
    east_nb = neighbors[:, 1]
    west_ok = (west_nb != all_tiles).astype(jnp.int32)
    east_ok = (east_nb != all_tiles).astype(jnp.int32)
    west_at = jnp.clip(west_nb - (block_base - tile_count), 0, tile_count - 1) * west_ok
    east_at = jnp.clip(east_nb - (block_base + tile_count), 0, tile_count - 1) * east_ok

    south_nb = neighbors[:, 2]
    north_nb = neighbors[:, 3]
    south_ok = (south_nb != all_tiles).astype(jnp.int32)
    north_ok = (north_nb != all_tiles).astype(jnp.int32)
    south = jnp.where(south_ok > 0, jnp.clip(south_nb - block_base, 0, tile_count - 1), tile_count)
    north = jnp.where(north_ok > 0, jnp.clip(north_nb - block_base, 0, tile_count - 1), tile_count)
    indices = (south, north, west_at, east_at, west_ok, east_ok)

    fine_ends = jnp.stack(
        [
            fine_propagate(
                n, starts[n], diffusivity, velocity, obstacle, from_prev, from_next, indices,
                substep_scale,
            )
            for n in range(slice_count)
        ],
        axis=0,
    )
    restricting_x = 0.5 * jnp.repeat(coarse_x, 2, axis=2)
    coarse_of_starts = apply_coarse(starts, restricting_x, coarse_y)
    correction = fine_ends - prolong(coarse_of_starts)
    coarse_jump = restrict(correction)
    earlier_correction = passed_along(correction[-1], "tm", 1)
    tm_index = lax.axis_index("tm")
    tm_count = lax.axis_size("tm")
    first_coarse = restrict(starts[0])

    def prefix_over_tm(total, power_x, power_y):
        distances = []
        distance = 1
        while distance < tm_count:
            distances.append(distance)
            distance *= 2
        powers = {}
        for distance in distances:
            powers[distance] = (power_x, power_y)
            power_x = jnp.einsum("tij,tjk->tik", power_x, power_x, precision=exact_precision)
            power_y = jnp.einsum("tij,tjk->tik", power_y, power_y, precision=exact_precision)
        half = total.shape[0] // 2
        parts = [(slice(0, half), distances[:1] + distances[1:]),
                 (slice(half, None), distances[:1] + distances[1:][::-1])]
        values = [total[part] for part, _ in parts]
        for step in range(len(distances)):
            if step == 0:
                received = passed_along(total, "tm", distances[0])
                received = [received[part] for part, _ in parts]
            else:
                received = [passed_along(values[k], "tm", parts[k][1][step]) for k in range(2)]
            for k in range(2):
                part, order = parts[k]
                distance = order[step]
                mixed = apply_coarse(received[k], powers[distance][0][part], powers[distance][1][part])
                values[k] = values[k] + jnp.where(tm_index >= distance, mixed, 0.0)
        return jnp.concatenate(values, axis=0)

    if slice_count == 1:
        seed = jnp.where(tm_index == 0, coarse_of_starts[0], 0.0)
        reached = prefix_over_tm(coarse_jump[0] + seed, coarse_x, coarse_y)
        coarse_applied = (reached - coarse_jump[0])[None]
    else:
        shifted_jump = jnp.concatenate(
            [passed_along(coarse_jump[-1:], "tm", 1), coarse_jump[:-1]], axis=0
        )
        head = jnp.where(tm_index == 0, first_coarse[None], shifted_jump[:1])
        local = jnp.concatenate([head, shifted_jump[1:]], axis=0)
        states = [local[0]]
        for n in range(1, slice_count):
            states.append(apply_coarse(states[-1], coarse_x, coarse_y) + local[n])
        power_x = coarse_x
        power_y = coarse_y
        for n in range(1, slice_count):
            power_x = jnp.einsum("tij,tjk->tik", power_x, coarse_x, precision=exact_precision)
            power_y = jnp.einsum("tij,tjk->tik", power_y, coarse_y, precision=exact_precision)
        total = prefix_over_tm(states[-1], power_x, power_y)
        earlier = jnp.where(tm_index > 0, passed_along(total, "tm", 1), 0.0)
        own_coarse = []
        for n in range(slice_count):
            earlier = apply_coarse(earlier, coarse_x, coarse_y)
            own_coarse.append(states[n] + earlier)
        coarse_applied = apply_coarse(jnp.stack(own_coarse, axis=0), coarse_x, coarse_y)
    slice_ends = prolong(coarse_applied) + correction
    previous = prolong(passed_along(coarse_applied[-1], "tm", 1)) + earlier_correction
    first_step = jnp.where(
        lax.axis_index("tm") == 0, jnp.zeros_like(previous), previous - starts[0]
    )
    increment = jnp.concatenate([first_step[None], slice_ends[:-1] - starts[1:]], axis=0)
    return (slice_ends, increment)


def solution(mesh):
    placed = (
        P("tm", "space", None, None),
        P("space", None, None),
        P(None, "space", None, None),
        P("space", None, None),
        P(),
        P("space", None),
        P("space", None, None),
        P("space", None, None),
    )
    return jax.shard_map(
        on_device,
        mesh=mesh,
        in_specs=placed,
        out_specs=(P("tm", "space", None, None), P("tm", "space", None, None)),
        check_vma=False,
    )
```

```python
import functools

import jax
import jax.numpy as jnp
from jax import lax
from jax.experimental import pallas as pl
from jax.experimental.pallas import tpu as pltpu
from jax.sharding import PartitionSpec as P

SUB = 12
HALO = 16
PAD = 8


exact_precision = lax.Precision.HIGHEST


def spread(value, axis, source):
    kept = jnp.where(lax.axis_index(axis) == source, value, 0).astype(value.dtype)
    return lax.psum(kept, axis)


def passed_along(block, axis, distance):
    devices = range(lax.axis_size(axis))
    route = [(i - distance, i) for i in devices if i - distance in devices]
    return lax.ppermute(block, axis, route)


def restrict(values):
    return 0.5 * (values[..., 0::2, :] + values[..., 1::2, :])


def prolong(coarse_values):
    return jnp.repeat(coarse_values, 2, axis=-2)


def apply_coarse(coarse_values, matrix_x, matrix_y):
    mixed_x = jnp.einsum("tij,...tjk->...tik", matrix_x, coarse_values, precision=exact_precision)
    return jnp.einsum("...tik,tlk->...til", mixed_x, matrix_y, precision=exact_precision)


def fine_kernel(slice_at, south_ref, north_ref, west_at_ref, east_at_ref, west_ok_ref, east_ok_ref,
                scale_ref, u_ref, diffusivity_ref, velocity_ref, obstacle_ref, prev_ref, next_ref,
                out_ref, state_ref, other_ref, field_ref):
    tiles = u_ref.shape[0]
    rows = u_ref.shape[1]
    lanes = u_ref.shape[2]
    total = rows + 2 * HALO
    layers = prev_ref.shape[0]
    for ref in (state_ref, other_ref):
        ref[tiles] = jnp.zeros(ref.shape[1:], jnp.float32)
        for i in range(tiles):
            ref[i, pl.ds(0, PAD), :] = jnp.zeros((PAD, lanes), jnp.float32)
            ref[i, pl.ds(PAD + total, PAD), :] = jnp.zeros((PAD, lanes), jnp.float32)
    for i in range(tiles):
        west_at = west_at_ref[i]
        east_at = east_at_ref[i]
        west_ok = west_ok_ref[i] > 0
        east_ok = east_ok_ref[i] > 0
        state_ref[i, pl.ds(PAD, HALO), :] = jnp.where(west_ok, prev_ref[slice_at, west_at], 0.0)
        state_ref[i, pl.ds(PAD + HALO, rows), :] = u_ref[i]
        state_ref[i, pl.ds(PAD + HALO + rows, HALO), :] = jnp.where(
            east_ok, next_ref[slice_at, east_at], 0.0
        )
        own = (
            diffusivity_ref[i],
            velocity_ref[0, i],
            velocity_ref[1, i],
            1.0 - obstacle_ref[i].astype(jnp.float32),
        )
        factor = (1.0, 0.5, 0.5, 1.0)
        for f in range(4):
            field_at = layers - 4 + f
            field_ref[f, i, pl.ds(0, HALO), :] = factor[f] * jnp.where(
                west_ok, prev_ref[field_at, west_at], 0.0
            )
            field_ref[f, i, pl.ds(HALO, rows), :] = factor[f] * own[f]
            field_ref[f, i, pl.ds(HALO + rows, HALO), :] = factor[f] * jnp.where(
                east_ok, next_ref[field_at, east_at], 0.0
            )

    chunk = 16
    lane = lax.broadcasted_iota(jnp.int32, (chunk, lanes), 1)
    first_lane = lane == 0
    last_lane = lane == lanes - 1

    def substep(strength, src_ref, dst_ref):
        for i in range(tiles):
            south_at = south_ref[i]
            north_at = north_ref[i]
            for start in range(0, total, chunk):
                rows_at = pl.ds(PAD + start, chunk)
                current = src_ref[i, rows_at, :]
                south_tile = src_ref[south_at, rows_at, :]
                north_tile = src_ref[north_at, rows_at, :]
                from_west = src_ref[i, pl.ds(PAD + start - 1, chunk), :]
                from_east = src_ref[i, pl.ds(PAD + start + 1, chunk), :]
                from_south = pltpu.roll(jnp.where(last_lane, south_tile, current), 1, 1)
                from_north = pltpu.roll(jnp.where(first_lane, north_tile, current), lanes - 1, 1)
                diffusivity = field_ref[0, i, pl.ds(start, chunk), :]
                half_speed_x = field_ref[1, i, pl.ds(start, chunk), :]
                half_speed_y = field_ref[2, i, pl.ds(start, chunk), :]
                open_cells = field_ref[3, i, pl.ds(start, chunk), :]
                laplace = from_west + from_east + from_south + from_north - 4.0 * current
                half_transport = half_speed_x * (from_east - from_west) + half_speed_y * (
                    from_north - from_south
                )
                dst_ref[i, rows_at, :] = open_cells * (
                    current + strength * diffusivity * laplace - half_transport
                )

    def substep_pair(p, carry):
        substep(scale_ref[2 * p], state_ref, other_ref)
        substep(scale_ref[2 * p + 1], other_ref, state_ref)
        return carry

    lax.fori_loop(0, SUB // 2, substep_pair, 0)
    final_ref = state_ref
    if SUB % 2:
        substep(scale_ref[SUB - 1], state_ref, other_ref)
        final_ref = other_ref
    for i in range(tiles):
        out_ref[i] = final_ref[i, pl.ds(PAD + HALO, rows), :]


def fine_propagate(slice_at, u, diffusivity, velocity, obstacle, from_prev, from_next, indices, scale):
    tiles, rows, lanes = u.shape
    total = rows + 2 * HALO
    vmem = pltpu.MemorySpace.VMEM
    smem = pltpu.MemorySpace.SMEM
    return pl.pallas_call(
        functools.partial(fine_kernel, slice_at),
        out_shape=jax.ShapeDtypeStruct(u.shape, u.dtype),
        in_specs=[pl.BlockSpec(memory_space=smem)] * 7 + [pl.BlockSpec(memory_space=vmem)] * 6,
        out_specs=pl.BlockSpec(memory_space=vmem),
        scratch_shapes=[
            pltpu.VMEM((tiles + 1, total + 2 * PAD, lanes), jnp.float32),
            pltpu.VMEM((tiles + 1, total + 2 * PAD, lanes), jnp.float32),
            pltpu.VMEM((4, tiles, total, lanes), jnp.float32),
        ],
        compiler_params=pltpu.CompilerParams(vmem_limit_bytes=48 * 1024 * 1024),
    )(*indices, scale, u, diffusivity, velocity, obstacle, from_prev, from_next)


def on_device(
    starts, diffusivity, velocity, obstacle, substep_scale, neighbors, coarse_x, coarse_y
):
    slice_count = starts.shape[0]
    tile_count = starts.shape[1]
    rows = starts.shape[2]
    all_tiles = tile_count * lax.axis_size("space")
    block_base = lax.axis_index("space") * tile_count
    open_cells = 1.0 - obstacle.astype(jnp.float32)

    fields = jnp.stack([diffusivity, velocity[0], velocity[1], open_cells], axis=0)
    layers = jnp.concatenate([starts, fields], axis=0)
    space_count = lax.axis_size("space")
    forward = [(i, i + 1) for i in range(space_count - 1)]
    backward = [(i + 1, i) for i in range(space_count - 1)]
    from_prev = lax.ppermute(layers[:, :, rows - HALO:, :], "space", forward)
    from_next = lax.ppermute(layers[:, :, :HALO, :], "space", backward)
    west_nb = neighbors[:, 0]
    east_nb = neighbors[:, 1]
    west_ok = (west_nb != all_tiles).astype(jnp.int32)
    east_ok = (east_nb != all_tiles).astype(jnp.int32)
    west_at = jnp.clip(west_nb - (block_base - tile_count), 0, tile_count - 1) * west_ok
    east_at = jnp.clip(east_nb - (block_base + tile_count), 0, tile_count - 1) * east_ok

    south_nb = neighbors[:, 2]
    north_nb = neighbors[:, 3]
    south_ok = (south_nb != all_tiles).astype(jnp.int32)
    north_ok = (north_nb != all_tiles).astype(jnp.int32)
    south = jnp.where(south_ok > 0, jnp.clip(south_nb - block_base, 0, tile_count - 1), tile_count)
    north = jnp.where(north_ok > 0, jnp.clip(north_nb - block_base, 0, tile_count - 1), tile_count)
    indices = (south, north, west_at, east_at, west_ok, east_ok)

    fine_ends = jnp.stack(
        [
            fine_propagate(
                n, starts[n], diffusivity, velocity, obstacle, from_prev, from_next, indices,
                substep_scale,
            )
            for n in range(slice_count)
        ],
        axis=0,
    )
    restricting_x = 0.5 * jnp.repeat(coarse_x, 2, axis=2)
    coarse_of_starts = apply_coarse(starts, restricting_x, coarse_y)
    correction = fine_ends - prolong(coarse_of_starts)
    coarse_jump = restrict(correction)
    tm_index = lax.axis_index("tm")
    tm_count = lax.axis_size("tm")
    first_coarse = restrict(starts[0])

    def prefix_over_tm(total, power_x, power_y, later):
        distances = []
        distance = 1
        while distance < tm_count:
            distances.append(distance)
            distance *= 2
        powers = {}
        for distance in distances:
            powers[distance] = (power_x, power_y)
            power_x = jnp.einsum("tij,tjk->tik", power_x, power_x, precision=exact_precision)
            power_y = jnp.einsum("tij,tjk->tik", power_y, power_y, precision=exact_precision)
        half = total.shape[0] // 2
        parts = [(slice(0, half), distances[:1] + distances[1:]),
                 (slice(half, None), distances[:1] + distances[1:][::-1])]
        values = [total[part] for part, _ in parts]
        for step in range(len(distances)):
            if step == 0:
                received = passed_along(total, "tm", distances[0])
                later, received = lax.optimization_barrier((later, received))
                later = passed_along(later, "tm", 1)
                received = [received[part] for part, _ in parts]
            else:
                received = [passed_along(values[k], "tm", parts[k][1][step]) for k in range(2)]
            for k in range(2):
                part, order = parts[k]
                distance = order[step]
                mixed = apply_coarse(received[k], powers[distance][0][part], powers[distance][1][part])
                values[k] = values[k] + jnp.where(tm_index >= distance, mixed, 0.0)
        return jnp.concatenate(values, axis=0), later

    if slice_count == 1:
        seed = jnp.where(tm_index == 0, coarse_of_starts[0], 0.0)
        reached, earlier_correction = prefix_over_tm(
            coarse_jump[0] + seed, coarse_x, coarse_y, correction[-1]
        )
        coarse_applied = (reached - coarse_jump[0])[None]
    else:
        shifted_jump = jnp.concatenate(
            [passed_along(coarse_jump[-1:], "tm", 1), coarse_jump[:-1]], axis=0
        )
        head = jnp.where(tm_index == 0, first_coarse[None], shifted_jump[:1])
        local = jnp.concatenate([head, shifted_jump[1:]], axis=0)
        states = [local[0]]
        for n in range(1, slice_count):
            states.append(apply_coarse(states[-1], coarse_x, coarse_y) + local[n])
        power_x = coarse_x
        power_y = coarse_y
        for n in range(1, slice_count):
            power_x = jnp.einsum("tij,tjk->tik", power_x, coarse_x, precision=exact_precision)
            power_y = jnp.einsum("tij,tjk->tik", power_y, coarse_y, precision=exact_precision)
        total, earlier_correction = prefix_over_tm(states[-1], power_x, power_y, correction[-1])
        earlier = jnp.where(tm_index > 0, passed_along(total, "tm", 1), 0.0)
        own_coarse = []
        for n in range(slice_count):
            earlier = apply_coarse(earlier, coarse_x, coarse_y)
            own_coarse.append(states[n] + earlier)
        coarse_applied = apply_coarse(jnp.stack(own_coarse, axis=0), coarse_x, coarse_y)
    slice_ends = prolong(coarse_applied) + correction
    previous = prolong(passed_along(coarse_applied[-1], "tm", 1)) + earlier_correction
    first_step = jnp.where(
        lax.axis_index("tm") == 0, jnp.zeros_like(previous), previous - starts[0]
    )
    increment = jnp.concatenate([first_step[None], slice_ends[:-1] - starts[1:]], axis=0)
    return (slice_ends, increment)


def solution(mesh):
    placed = (
        P("tm", "space", None, None),
        P("space", None, None),
        P(None, "space", None, None),
        P("space", None, None),
        P(),
        P("space", None),
        P("space", None, None),
        P("space", None, None),
    )
    return jax.shard_map(
        on_device,
        mesh=mesh,
        in_specs=placed,
        out_specs=(P("tm", "space", None, None), P("tm", "space", None, None)),
        check_vma=False,
    )
```

```python
import functools

import jax
import jax.numpy as jnp
from jax import lax
from jax.experimental import pallas as pl
from jax.experimental.pallas import tpu as pltpu
from jax.sharding import PartitionSpec as P

SUB = 12
HALO = 16
PAD = 8


exact_precision = lax.Precision.HIGHEST


def spread(value, axis, source):
    kept = jnp.where(lax.axis_index(axis) == source, value, 0).astype(value.dtype)
    return lax.psum(kept, axis)


def passed_along(block, axis, distance):
    devices = range(lax.axis_size(axis))
    route = [(i - distance, i) for i in devices if i - distance in devices]
    return lax.ppermute(block, axis, route)


def restrict(values):
    return 0.5 * (values[..., 0::2, :] + values[..., 1::2, :])


def prolong(coarse_values):
    return jnp.repeat(coarse_values, 2, axis=-2)


def apply_coarse(coarse_values, matrix_x, matrix_y):
    mixed_x = jnp.einsum("tij,...tjk->...tik", matrix_x, coarse_values, precision=exact_precision)
    return jnp.einsum("...tik,tlk->...til", mixed_x, matrix_y, precision=exact_precision)


def fine_kernel(slice_at, south_ref, north_ref, west_at_ref, east_at_ref, west_ok_ref, east_ok_ref,
                scale_ref, u_ref, diffusivity_ref, velocity_ref, obstacle_ref, prev_ref, next_ref,
                out_ref, state_ref, other_ref, field_ref):
    tiles = u_ref.shape[0]
    rows = u_ref.shape[1]
    lanes = u_ref.shape[2]
    total = rows + 2 * HALO
    layers = prev_ref.shape[1] // HALO
    for ref in (state_ref, other_ref):
        ref[tiles] = jnp.zeros(ref.shape[1:], jnp.float32)
        for i in range(tiles):
            ref[i, pl.ds(0, PAD), :] = jnp.zeros((PAD, lanes), jnp.float32)
            ref[i, pl.ds(PAD + total, PAD), :] = jnp.zeros((PAD, lanes), jnp.float32)
    for i in range(tiles):
        west_at = west_at_ref[i]
        east_at = east_at_ref[i]
        west_ok = west_ok_ref[i] > 0
        east_ok = east_ok_ref[i] > 0
        def west_layer(layer):
            return prev_ref[west_at, pl.ds(layer * HALO, HALO), :]

        def east_layer(layer):
            return next_ref[east_at, pl.ds(layer * HALO, HALO), :]

        state_ref[i, pl.ds(PAD, HALO), :] = jnp.where(west_ok, west_layer(slice_at), 0.0)
        state_ref[i, pl.ds(PAD + HALO, rows), :] = u_ref[i]
        state_ref[i, pl.ds(PAD + HALO + rows, HALO), :] = jnp.where(
            east_ok, east_layer(slice_at), 0.0
        )
        own = (
            diffusivity_ref[i],
            velocity_ref[0, i],
            velocity_ref[1, i],
            1.0 - obstacle_ref[i].astype(jnp.float32),
        )
        factor = (1.0, 0.5, 0.5, 1.0)
        for f in range(4):
            field_at = layers - 4 + f
            west_rows = west_layer(field_at)
            east_rows = east_layer(field_at)
            if f == 3:
                west_rows = 1.0 - west_rows
                east_rows = 1.0 - east_rows
            field_ref[f, i, pl.ds(0, HALO), :] = factor[f] * jnp.where(west_ok, west_rows, 0.0)
            field_ref[f, i, pl.ds(HALO, rows), :] = factor[f] * own[f]
            field_ref[f, i, pl.ds(HALO + rows, HALO), :] = factor[f] * jnp.where(
                east_ok, east_rows, 0.0
            )

    chunk = 16
    lane = lax.broadcasted_iota(jnp.int32, (chunk, lanes), 1)
    first_lane = lane == 0
    last_lane = lane == lanes - 1

    def substep(strength, src_ref, dst_ref):
        for i in range(tiles):
            south_at = south_ref[i]
            north_at = north_ref[i]
            for start in range(0, total, chunk):
                rows_at = pl.ds(PAD + start, chunk)
                current = src_ref[i, rows_at, :]
                south_tile = src_ref[south_at, rows_at, :]
                north_tile = src_ref[north_at, rows_at, :]
                from_west = src_ref[i, pl.ds(PAD + start - 1, chunk), :]
                from_east = src_ref[i, pl.ds(PAD + start + 1, chunk), :]
                from_south = pltpu.roll(jnp.where(last_lane, south_tile, current), 1, 1)
                from_north = pltpu.roll(jnp.where(first_lane, north_tile, current), lanes - 1, 1)
                diffusivity = field_ref[0, i, pl.ds(start, chunk), :]
                half_speed_x = field_ref[1, i, pl.ds(start, chunk), :]
                half_speed_y = field_ref[2, i, pl.ds(start, chunk), :]
                open_cells = field_ref[3, i, pl.ds(start, chunk), :]
                laplace = from_west + from_east + from_south + from_north - 4.0 * current
                half_transport = half_speed_x * (from_east - from_west) + half_speed_y * (
                    from_north - from_south
                )
                dst_ref[i, rows_at, :] = open_cells * (
                    current + strength * diffusivity * laplace - half_transport
                )

    def substep_pair(p, carry):
        substep(scale_ref[2 * p], state_ref, other_ref)
        substep(scale_ref[2 * p + 1], other_ref, state_ref)
        return carry

    lax.fori_loop(0, SUB // 2, substep_pair, 0)
    final_ref = state_ref
    if SUB % 2:
        substep(scale_ref[SUB - 1], state_ref, other_ref)
        final_ref = other_ref
    for i in range(tiles):
        out_ref[i] = final_ref[i, pl.ds(PAD + HALO, rows), :]


def fine_propagate(slice_at, u, diffusivity, velocity, obstacle, from_prev, from_next, indices, scale):
    tiles, rows, lanes = u.shape
    total = rows + 2 * HALO
    vmem = pltpu.MemorySpace.VMEM
    smem = pltpu.MemorySpace.SMEM
    return pl.pallas_call(
        functools.partial(fine_kernel, slice_at),
        out_shape=jax.ShapeDtypeStruct(u.shape, u.dtype),
        in_specs=[pl.BlockSpec(memory_space=smem)] * 7 + [pl.BlockSpec(memory_space=vmem)] * 6,
        out_specs=pl.BlockSpec(memory_space=vmem),
        scratch_shapes=[
            pltpu.VMEM((tiles + 1, total + 2 * PAD, lanes), jnp.float32),
            pltpu.VMEM((tiles + 1, total + 2 * PAD, lanes), jnp.float32),
            pltpu.VMEM((4, tiles, total, lanes), jnp.float32),
        ],
        compiler_params=pltpu.CompilerParams(vmem_limit_bytes=48 * 1024 * 1024),
    )(*indices, scale, u, diffusivity, velocity, obstacle, from_prev, from_next)


def on_device(
    starts, diffusivity, velocity, obstacle, substep_scale, neighbors, coarse_x, coarse_y
):
    slice_count = starts.shape[0]
    tile_count = starts.shape[1]
    rows = starts.shape[2]
    all_tiles = tile_count * lax.axis_size("space")
    block_base = lax.axis_index("space") * tile_count

    def edge_rows(part):
        pieces = [starts[n][:, part, :] for n in range(slice_count)]
        pieces += [diffusivity[:, part, :], velocity[0][:, part, :], velocity[1][:, part, :]]
        pieces.append(obstacle[:, part, :].astype(jnp.float32))
        return jnp.concatenate(pieces, axis=1)

    space_count = lax.axis_size("space")
    forward = [(i, i + 1) for i in range(space_count - 1)]
    backward = [(i + 1, i) for i in range(space_count - 1)]
    from_prev = lax.ppermute(edge_rows(slice(rows - HALO, None)), "space", forward)
    from_next = lax.ppermute(edge_rows(slice(0, HALO)), "space", backward)
    west_nb = neighbors[:, 0]
    east_nb = neighbors[:, 1]
    west_ok = (west_nb != all_tiles).astype(jnp.int32)
    east_ok = (east_nb != all_tiles).astype(jnp.int32)
    west_at = jnp.clip(west_nb - (block_base - tile_count), 0, tile_count - 1) * west_ok
    east_at = jnp.clip(east_nb - (block_base + tile_count), 0, tile_count - 1) * east_ok

    south_nb = neighbors[:, 2]
    north_nb = neighbors[:, 3]
    south_ok = (south_nb != all_tiles).astype(jnp.int32)
    north_ok = (north_nb != all_tiles).astype(jnp.int32)
    south = jnp.where(south_ok > 0, jnp.clip(south_nb - block_base, 0, tile_count - 1), tile_count)
    north = jnp.where(north_ok > 0, jnp.clip(north_nb - block_base, 0, tile_count - 1), tile_count)
    indices = (south, north, west_at, east_at, west_ok, east_ok)

    fine_ends = jnp.stack(
        [
            fine_propagate(
                n, starts[n], diffusivity, velocity, obstacle, from_prev, from_next, indices,
                substep_scale,
            )
            for n in range(slice_count)
        ],
        axis=0,
    )
    restricting_x = 0.5 * jnp.repeat(coarse_x, 2, axis=2)
    coarse_of_starts = apply_coarse(starts, restricting_x, coarse_y)
    correction = fine_ends - prolong(coarse_of_starts)
    coarse_jump = restrict(correction)
    earlier_correction = passed_along(correction[-1], "tm", 1)
    tm_index = lax.axis_index("tm")
    tm_count = lax.axis_size("tm")
    first_coarse = restrict(starts[0])

    def prefix_over_tm(total, power_x, power_y):
        distances = []
        distance = 1
        while distance < tm_count:
            distances.append(distance)
            distance *= 2
        powers = {}
        for distance in distances:
            powers[distance] = (power_x, power_y)
            power_x = jnp.einsum("tij,tjk->tik", power_x, power_x, precision=exact_precision)
            power_y = jnp.einsum("tij,tjk->tik", power_y, power_y, precision=exact_precision)
        half = total.shape[0] // 2
        parts = [(slice(0, half), distances[:1] + distances[1:]),
                 (slice(half, None), distances[:1] + distances[1:][::-1])]
        values = [total[part] for part, _ in parts]
        for step in range(len(distances)):
            if step == 0:
                received = passed_along(total, "tm", distances[0])
                received = [received[part] for part, _ in parts]
            else:
                received = [passed_along(values[k], "tm", parts[k][1][step]) for k in range(2)]
            for k in range(2):
                part, order = parts[k]
                distance = order[step]
                mixed = apply_coarse(received[k], powers[distance][0][part], powers[distance][1][part])
                values[k] = values[k] + jnp.where(tm_index >= distance, mixed, 0.0)
        return jnp.concatenate(values, axis=0)

    if slice_count == 1:
        seed = jnp.where(tm_index == 0, coarse_of_starts[0], 0.0)
        reached = prefix_over_tm(coarse_jump[0] + seed, coarse_x, coarse_y)
        coarse_applied = (reached - coarse_jump[0])[None]
    else:
        shifted_jump = jnp.concatenate(
            [passed_along(coarse_jump[-1:], "tm", 1), coarse_jump[:-1]], axis=0
        )
        head = jnp.where(tm_index == 0, first_coarse[None], shifted_jump[:1])
        local = jnp.concatenate([head, shifted_jump[1:]], axis=0)
        states = [local[0]]
        for n in range(1, slice_count):
            states.append(apply_coarse(states[-1], coarse_x, coarse_y) + local[n])
        power_x = coarse_x
        power_y = coarse_y
        for n in range(1, slice_count):
            power_x = jnp.einsum("tij,tjk->tik", power_x, coarse_x, precision=exact_precision)
            power_y = jnp.einsum("tij,tjk->tik", power_y, coarse_y, precision=exact_precision)
        total = prefix_over_tm(states[-1], power_x, power_y)
        earlier = jnp.where(tm_index > 0, passed_along(total, "tm", 1), 0.0)
        own_coarse = []
        for n in range(slice_count):
            earlier = apply_coarse(earlier, coarse_x, coarse_y)
            own_coarse.append(states[n] + earlier)
        coarse_applied = apply_coarse(jnp.stack(own_coarse, axis=0), coarse_x, coarse_y)
    slice_ends = prolong(coarse_applied) + correction
    previous = prolong(passed_along(coarse_applied[-1], "tm", 1)) + earlier_correction
    first_step = jnp.where(
        lax.axis_index("tm") == 0, jnp.zeros_like(previous), previous - starts[0]
    )
    increment = jnp.concatenate([first_step[None], slice_ends[:-1] - starts[1:]], axis=0)
    return (slice_ends, increment)


def solution(mesh):
    placed = (
        P("tm", "space", None, None),
        P("space", None, None),
        P(None, "space", None, None),
        P("space", None, None),
        P(),
        P("space", None),
        P("space", None, None),
        P("space", None, None),
    )
    return jax.shard_map(
        on_device,
        mesh=mesh,
        in_specs=placed,
        out_specs=(P("tm", "space", None, None), P("tm", "space", None, None)),
        check_vma=False,
    )
```

```python
import functools

import jax
import jax.numpy as jnp
from jax import lax
from jax.experimental import pallas as pl
from jax.experimental.pallas import tpu as pltpu
from jax.sharding import PartitionSpec as P

SUB = 12
HALO = 16
PAD = 8


exact_precision = lax.Precision.HIGHEST


def spread(value, axis, source):
    kept = jnp.where(lax.axis_index(axis) == source, value, 0).astype(value.dtype)
    return lax.psum(kept, axis)


def passed_along(block, axis, distance):
    devices = range(lax.axis_size(axis))
    route = [(i - distance, i) for i in devices if i - distance in devices]
    return lax.ppermute(block, axis, route)


def restrict(values):
    return 0.5 * (values[..., 0::2, :] + values[..., 1::2, :])


def prolong(coarse_values):
    return jnp.repeat(coarse_values, 2, axis=-2)


def apply_coarse(coarse_values, matrix_x, matrix_y):
    mixed_x = jnp.einsum("tij,...tjk->...tik", matrix_x, coarse_values, precision=exact_precision)
    return jnp.einsum("...tik,tlk->...til", mixed_x, matrix_y, precision=exact_precision)


def fine_kernel(slice_at, south_ref, north_ref, west_at_ref, east_at_ref, west_ok_ref, east_ok_ref,
                scale_ref, u_ref, diffusivity_ref, velocity_ref, obstacle_ref, prev_ref, next_ref,
                out_ref, state_ref, other_ref, field_ref):
    tiles = u_ref.shape[0]
    rows = u_ref.shape[1]
    lanes = u_ref.shape[2]
    total = rows + 2 * HALO
    layers = prev_ref.shape[0]
    for ref in (state_ref, other_ref):
        ref[tiles] = jnp.zeros(ref.shape[1:], jnp.float32)
        for i in range(tiles):
            ref[i, pl.ds(0, PAD), :] = jnp.zeros((PAD, lanes), jnp.float32)
            ref[i, pl.ds(PAD + total, PAD), :] = jnp.zeros((PAD, lanes), jnp.float32)
    for i in range(tiles):
        west_at = west_at_ref[i]
        east_at = east_at_ref[i]
        west_ok = west_ok_ref[i] > 0
        east_ok = east_ok_ref[i] > 0
        state_ref[i, pl.ds(PAD, HALO), :] = jnp.where(west_ok, prev_ref[slice_at, west_at], 0.0)
        state_ref[i, pl.ds(PAD + HALO, rows), :] = u_ref[i]
        state_ref[i, pl.ds(PAD + HALO + rows, HALO), :] = jnp.where(
            east_ok, next_ref[slice_at, east_at], 0.0
        )
        own = (
            diffusivity_ref[i],
            velocity_ref[0, i],
            velocity_ref[1, i],
            1.0 - obstacle_ref[i].astype(jnp.float32),
        )
        factor = (1.0, 0.5, 0.5, 1.0)
        for f in range(4):
            field_at = layers - 4 + f
            field_ref[f, i, pl.ds(0, HALO), :] = factor[f] * jnp.where(
                west_ok, prev_ref[field_at, west_at], 0.0
            )
            field_ref[f, i, pl.ds(HALO, rows), :] = factor[f] * own[f]
            field_ref[f, i, pl.ds(HALO + rows, HALO), :] = factor[f] * jnp.where(
                east_ok, next_ref[field_at, east_at], 0.0
            )

    chunk = 16
    lane = lax.broadcasted_iota(jnp.int32, (chunk, lanes), 1)
    first_lane = lane == 0
    last_lane = lane == lanes - 1

    def substep(strength, src_ref, dst_ref):
        for i in range(tiles):
            south_at = south_ref[i]
            north_at = north_ref[i]
            for start in range(0, total, chunk):
                rows_at = pl.ds(PAD + start, chunk)
                current = src_ref[i, rows_at, :]
                south_tile = src_ref[south_at, rows_at, :]
                north_tile = src_ref[north_at, rows_at, :]
                from_west = src_ref[i, pl.ds(PAD + start - 1, chunk), :]
                from_east = src_ref[i, pl.ds(PAD + start + 1, chunk), :]
                from_south = pltpu.roll(jnp.where(last_lane, south_tile, current), 1, 1)
                from_north = pltpu.roll(jnp.where(first_lane, north_tile, current), lanes - 1, 1)
                diffusivity = field_ref[0, i, pl.ds(start, chunk), :]
                half_speed_x = field_ref[1, i, pl.ds(start, chunk), :]
                half_speed_y = field_ref[2, i, pl.ds(start, chunk), :]
                open_cells = field_ref[3, i, pl.ds(start, chunk), :]
                laplace = from_west + from_east + from_south + from_north - 4.0 * current
                half_transport = half_speed_x * (from_east - from_west) + half_speed_y * (
                    from_north - from_south
                )
                dst_ref[i, rows_at, :] = open_cells * (
                    current + strength * diffusivity * laplace - half_transport
                )

    def substep_pair(p, carry):
        substep(scale_ref[2 * p], state_ref, other_ref)
        substep(scale_ref[2 * p + 1], other_ref, state_ref)
        return carry

    lax.fori_loop(0, SUB // 2, substep_pair, 0)
    final_ref = state_ref
    if SUB % 2:
        substep(scale_ref[SUB - 1], state_ref, other_ref)
        final_ref = other_ref
    for i in range(tiles):
        out_ref[i] = final_ref[i, pl.ds(PAD + HALO, rows), :]


def fine_propagate(slice_at, u, diffusivity, velocity, obstacle, from_prev, from_next, indices, scale):
    tiles, rows, lanes = u.shape
    total = rows + 2 * HALO
    vmem = pltpu.MemorySpace.VMEM
    smem = pltpu.MemorySpace.SMEM
    return pl.pallas_call(
        functools.partial(fine_kernel, slice_at),
        out_shape=jax.ShapeDtypeStruct(u.shape, u.dtype),
        in_specs=[pl.BlockSpec(memory_space=smem)] * 7 + [pl.BlockSpec(memory_space=vmem)] * 6,
        out_specs=pl.BlockSpec(memory_space=vmem),
        scratch_shapes=[
            pltpu.VMEM((tiles + 1, total + 2 * PAD, lanes), jnp.float32),
            pltpu.VMEM((tiles + 1, total + 2 * PAD, lanes), jnp.float32),
            pltpu.VMEM((4, tiles, total, lanes), jnp.float32),
        ],
        compiler_params=pltpu.CompilerParams(vmem_limit_bytes=48 * 1024 * 1024),
    )(*indices, scale, u, diffusivity, velocity, obstacle, from_prev, from_next)


def payload_kernel(starts_hbm, diffusivity_hbm, velocity_hbm, obstacle_hbm, low_ref, high_ref,
                   obstacle_rows, sems):
    slices = starts_hbm.shape[0]
    rows = starts_hbm.shape[2]
    copies = []
    for side, (out_ref, first) in enumerate(((low_ref, 0), (high_ref, rows - HALO))):
        part = pl.ds(first, HALO)
        sources = [starts_hbm.at[n, :, part, :] for n in range(slices)]
        sources += [
            diffusivity_hbm.at[:, part, :],
            velocity_hbm.at[0, :, part, :],
            velocity_hbm.at[1, :, part, :],
        ]
        for k, source in enumerate(sources):
            copies.append(pltpu.make_async_copy(source, out_ref.at[k], sems.at[side, k]))
        copies.append(
            pltpu.make_async_copy(
                obstacle_hbm.at[:, part, :], obstacle_rows.at[side], sems.at[side, len(sources)]
            )
        )
    for copy in copies:
        copy.start()
    for copy in copies:
        copy.wait()
    for side, out_ref in enumerate((low_ref, high_ref)):
        out_ref[slices + 3] = 1.0 - obstacle_rows[side].astype(jnp.float32)


def edge_payload(starts, diffusivity, velocity, obstacle):
    slices, tiles, rows, lanes = starts.shape
    shape = jax.ShapeDtypeStruct((slices + 4, tiles, HALO, lanes), jnp.float32)
    vmem = pltpu.MemorySpace.VMEM
    return pl.pallas_call(
        payload_kernel,
        out_shape=(shape, shape),
        in_specs=[pl.BlockSpec(memory_space=pl.ANY)] * 4,
        out_specs=(pl.BlockSpec(memory_space=vmem), pl.BlockSpec(memory_space=vmem)),
        scratch_shapes=[
            pltpu.VMEM((2, tiles, HALO, lanes), jnp.int32),
            pltpu.SemaphoreType.DMA((2, slices + 4)),
        ],
    )(starts, diffusivity, velocity, obstacle)


def on_device(
    starts, diffusivity, velocity, obstacle, substep_scale, neighbors, coarse_x, coarse_y
):
    slice_count = starts.shape[0]
    tile_count = starts.shape[1]
    rows = starts.shape[2]
    all_tiles = tile_count * lax.axis_size("space")
    block_base = lax.axis_index("space") * tile_count

    low_rows, high_rows = edge_payload(starts, diffusivity, velocity, obstacle)
    space_count = lax.axis_size("space")
    forward = [(i, i + 1) for i in range(space_count - 1)]
    backward = [(i + 1, i) for i in range(space_count - 1)]
    from_prev = lax.ppermute(high_rows, "space", forward)
    from_next = lax.ppermute(low_rows, "space", backward)
    west_nb = neighbors[:, 0]
    east_nb = neighbors[:, 1]
    west_ok = (west_nb != all_tiles).astype(jnp.int32)
    east_ok = (east_nb != all_tiles).astype(jnp.int32)
    west_at = jnp.clip(west_nb - (block_base - tile_count), 0, tile_count - 1) * west_ok
    east_at = jnp.clip(east_nb - (block_base + tile_count), 0, tile_count - 1) * east_ok

    south_nb = neighbors[:, 2]
    north_nb = neighbors[:, 3]
    south_ok = (south_nb != all_tiles).astype(jnp.int32)
    north_ok = (north_nb != all_tiles).astype(jnp.int32)
    south = jnp.where(south_ok > 0, jnp.clip(south_nb - block_base, 0, tile_count - 1), tile_count)
    north = jnp.where(north_ok > 0, jnp.clip(north_nb - block_base, 0, tile_count - 1), tile_count)
    indices = (south, north, west_at, east_at, west_ok, east_ok)

    fine_ends = jnp.stack(
        [
            fine_propagate(
                n, starts[n], diffusivity, velocity, obstacle, from_prev, from_next, indices,
                substep_scale,
            )
            for n in range(slice_count)
        ],
        axis=0,
    )
    restricting_x = 0.5 * jnp.repeat(coarse_x, 2, axis=2)
    coarse_of_starts = apply_coarse(starts, restricting_x, coarse_y)
    correction = fine_ends - prolong(coarse_of_starts)
    coarse_jump = restrict(correction)
    earlier_correction = passed_along(correction[-1], "tm", 1)
    tm_index = lax.axis_index("tm")
    tm_count = lax.axis_size("tm")
    first_coarse = restrict(starts[0])

    def prefix_over_tm(total, power_x, power_y):
        distances = []
        distance = 1
        while distance < tm_count:
            distances.append(distance)
            distance *= 2
        powers = {}
        for distance in distances:
            powers[distance] = (power_x, power_y)
            power_x = jnp.einsum("tij,tjk->tik", power_x, power_x, precision=exact_precision)
            power_y = jnp.einsum("tij,tjk->tik", power_y, power_y, precision=exact_precision)
        half = total.shape[0] // 2
        parts = [(slice(0, half), distances[:1] + distances[1:]),
                 (slice(half, None), distances[:1] + distances[1:][::-1])]
        values = [total[part] for part, _ in parts]
        for step in range(len(distances)):
            if step == 0:
                received = passed_along(total, "tm", distances[0])
                received = [received[part] for part, _ in parts]
            else:
                received = [passed_along(values[k], "tm", parts[k][1][step]) for k in range(2)]
            for k in range(2):
                part, order = parts[k]
                distance = order[step]
                mixed = apply_coarse(received[k], powers[distance][0][part], powers[distance][1][part])
                values[k] = values[k] + jnp.where(tm_index >= distance, mixed, 0.0)
        return jnp.concatenate(values, axis=0)

    if slice_count == 1:
        seed = jnp.where(tm_index == 0, coarse_of_starts[0], 0.0)
        reached = prefix_over_tm(coarse_jump[0] + seed, coarse_x, coarse_y)
        coarse_applied = (reached - coarse_jump[0])[None]
    else:
        shifted_jump = jnp.concatenate(
            [passed_along(coarse_jump[-1:], "tm", 1), coarse_jump[:-1]], axis=0
        )
        head = jnp.where(tm_index == 0, first_coarse[None], shifted_jump[:1])
        local = jnp.concatenate([head, shifted_jump[1:]], axis=0)
        states = [local[0]]
        for n in range(1, slice_count):
            states.append(apply_coarse(states[-1], coarse_x, coarse_y) + local[n])
        power_x = coarse_x
        power_y = coarse_y
        for n in range(1, slice_count):
            power_x = jnp.einsum("tij,tjk->tik", power_x, coarse_x, precision=exact_precision)
            power_y = jnp.einsum("tij,tjk->tik", power_y, coarse_y, precision=exact_precision)
        total = prefix_over_tm(states[-1], power_x, power_y)
        earlier = jnp.where(tm_index > 0, passed_along(total, "tm", 1), 0.0)
        own_coarse = []
        for n in range(slice_count):
            earlier = apply_coarse(earlier, coarse_x, coarse_y)
            own_coarse.append(states[n] + earlier)
        coarse_applied = apply_coarse(jnp.stack(own_coarse, axis=0), coarse_x, coarse_y)
    slice_ends = prolong(coarse_applied) + correction
    previous = prolong(passed_along(coarse_applied[-1], "tm", 1)) + earlier_correction
    first_step = jnp.where(
        lax.axis_index("tm") == 0, jnp.zeros_like(previous), previous - starts[0]
    )
    increment = jnp.concatenate([first_step[None], slice_ends[:-1] - starts[1:]], axis=0)
    return (slice_ends, increment)


def solution(mesh):
    placed = (
        P("tm", "space", None, None),
        P("space", None, None),
        P(None, "space", None, None),
        P("space", None, None),
        P(),
        P("space", None),
        P("space", None, None),
        P("space", None, None),
    )
    return jax.shard_map(
        on_device,
        mesh=mesh,
        in_specs=placed,
        out_specs=(P("tm", "space", None, None), P("tm", "space", None, None)),
        check_vma=False,
    )
```

```python
import functools

import jax
import jax.numpy as jnp
from jax import lax
from jax.experimental import pallas as pl
from jax.experimental.pallas import tpu as pltpu
from jax.sharding import PartitionSpec as P

SUB = 12
HALO = 16
PAD = 8


exact_precision = lax.Precision.HIGHEST


def spread(value, axis, source):
    kept = jnp.where(lax.axis_index(axis) == source, value, 0).astype(value.dtype)
    return lax.psum(kept, axis)


def passed_along(block, axis, distance):
    devices = range(lax.axis_size(axis))
    route = [(i - distance, i) for i in devices if i - distance in devices]
    return lax.ppermute(block, axis, route)


def restrict(values):
    return 0.5 * (values[..., 0::2, :] + values[..., 1::2, :])


def prolong(coarse_values):
    return jnp.repeat(coarse_values, 2, axis=-2)


def apply_coarse(coarse_values, matrix_x, matrix_y):
    mixed_x = jnp.einsum("tij,...tjk->...tik", matrix_x, coarse_values, precision=exact_precision)
    return jnp.einsum("...tik,tlk->...til", mixed_x, matrix_y, precision=exact_precision)


def fine_kernel(slice_at, south_ref, north_ref, west_at_ref, east_at_ref, west_ok_ref, east_ok_ref,
                scale_ref, u_ref, diffusivity_ref, velocity_ref, obstacle_ref, prev_ref, next_ref,
                out_ref, state_ref, other_ref, field_ref):
    tiles = u_ref.shape[0]
    rows = u_ref.shape[1]
    lanes = u_ref.shape[2]
    total = rows + 2 * HALO
    layers = prev_ref.shape[0]
    for ref in (state_ref, other_ref):
        ref[tiles] = jnp.zeros(ref.shape[1:], jnp.float32)
        for i in range(tiles):
            ref[i, pl.ds(0, PAD), :] = jnp.zeros((PAD, lanes), jnp.float32)
            ref[i, pl.ds(PAD + total, PAD), :] = jnp.zeros((PAD, lanes), jnp.float32)
    for i in range(tiles):
        west_at = west_at_ref[i]
        east_at = east_at_ref[i]
        west_ok = west_ok_ref[i] > 0
        east_ok = east_ok_ref[i] > 0
        state_ref[i, pl.ds(PAD, HALO), :] = jnp.where(west_ok, prev_ref[slice_at, west_at], 0.0)
        state_ref[i, pl.ds(PAD + HALO, rows), :] = u_ref[i]
        state_ref[i, pl.ds(PAD + HALO + rows, HALO), :] = jnp.where(
            east_ok, next_ref[slice_at, east_at], 0.0
        )
        own = (
            diffusivity_ref[i],
            velocity_ref[0, i],
            velocity_ref[1, i],
            1.0 - obstacle_ref[i].astype(jnp.float32),
        )
        factor = (1.0, 0.5, 0.5, 1.0)
        for f in range(4):
            field_at = layers - 4 + f
            field_ref[f, i, pl.ds(0, HALO), :] = factor[f] * jnp.where(
                west_ok, prev_ref[field_at, west_at], 0.0
            )
            field_ref[f, i, pl.ds(HALO, rows), :] = factor[f] * own[f]
            field_ref[f, i, pl.ds(HALO + rows, HALO), :] = factor[f] * jnp.where(
                east_ok, next_ref[field_at, east_at], 0.0
            )

    chunk = 16
    lane = lax.broadcasted_iota(jnp.int32, (chunk, lanes), 1)
    first_lane = lane == 0
    last_lane = lane == lanes - 1

    def substep(strength, src_ref, dst_ref):
        for i in range(tiles):
            south_at = south_ref[i]
            north_at = north_ref[i]
            for start in range(0, total, chunk):
                rows_at = pl.ds(PAD + start, chunk)
                current = src_ref[i, rows_at, :]
                south_tile = src_ref[south_at, rows_at, :]
                north_tile = src_ref[north_at, rows_at, :]
                from_west = src_ref[i, pl.ds(PAD + start - 1, chunk), :]
                from_east = src_ref[i, pl.ds(PAD + start + 1, chunk), :]
                from_south = pltpu.roll(jnp.where(last_lane, south_tile, current), 1, 1)
                from_north = pltpu.roll(jnp.where(first_lane, north_tile, current), lanes - 1, 1)
                diffusivity = field_ref[0, i, pl.ds(start, chunk), :]
                half_speed_x = field_ref[1, i, pl.ds(start, chunk), :]
                half_speed_y = field_ref[2, i, pl.ds(start, chunk), :]
                open_cells = field_ref[3, i, pl.ds(start, chunk), :]
                laplace = from_west + from_east + from_south + from_north - 4.0 * current
                half_transport = half_speed_x * (from_east - from_west) + half_speed_y * (
                    from_north - from_south
                )
                dst_ref[i, rows_at, :] = open_cells * (
                    current + strength * diffusivity * laplace - half_transport
                )

    def substep_pair(p, carry):
        substep(scale_ref[2 * p], state_ref, other_ref)
        substep(scale_ref[2 * p + 1], other_ref, state_ref)
        return carry

    lax.fori_loop(0, SUB // 2, substep_pair, 0)
    final_ref = state_ref
    if SUB % 2:
        substep(scale_ref[SUB - 1], state_ref, other_ref)
        final_ref = other_ref
    for i in range(tiles):
        out_ref[i] = final_ref[i, pl.ds(PAD + HALO, rows), :]


def fine_propagate(slice_at, u, diffusivity, velocity, obstacle, from_prev, from_next, indices, scale):
    tiles, rows, lanes = u.shape
    total = rows + 2 * HALO
    vmem = pltpu.MemorySpace.VMEM
    smem = pltpu.MemorySpace.SMEM
    return pl.pallas_call(
        functools.partial(fine_kernel, slice_at),
        out_shape=jax.ShapeDtypeStruct(u.shape, u.dtype),
        in_specs=[pl.BlockSpec(memory_space=smem)] * 7 + [pl.BlockSpec(memory_space=vmem)] * 6,
        out_specs=pl.BlockSpec(memory_space=vmem),
        scratch_shapes=[
            pltpu.VMEM((tiles + 1, total + 2 * PAD, lanes), jnp.float32),
            pltpu.VMEM((tiles + 1, total + 2 * PAD, lanes), jnp.float32),
            pltpu.VMEM((4, tiles, total, lanes), jnp.float32),
        ],
        compiler_params=pltpu.CompilerParams(vmem_limit_bytes=48 * 1024 * 1024),
    )(*indices, scale, u, diffusivity, velocity, obstacle, from_prev, from_next)


def payload_kernel(starts_hbm, diffusivity_hbm, velocity_hbm, obstacle_hbm, low_ref, high_ref,
                   obstacle_rows, sems):
    slices = starts_hbm.shape[0]
    rows = starts_hbm.shape[2]
    copies = []
    for side, (out_ref, first) in enumerate(((low_ref, 0), (high_ref, rows - HALO))):
        part = pl.ds(first, HALO)
        sources = [starts_hbm.at[n, :, part, :] for n in range(slices)]
        sources += [
            diffusivity_hbm.at[:, part, :],
            velocity_hbm.at[0, :, part, :],
            velocity_hbm.at[1, :, part, :],
        ]
        for k, source in enumerate(sources):
            copies.append(pltpu.make_async_copy(source, out_ref.at[k], sems.at[side, k]))
        copies.append(
            pltpu.make_async_copy(
                obstacle_hbm.at[:, part, :], obstacle_rows.at[side], sems.at[side, len(sources)]
            )
        )
    for copy in copies:
        copy.start()
    for copy in copies:
        copy.wait()
    for side, out_ref in enumerate((low_ref, high_ref)):
        out_ref[slices + 3] = 1.0 - obstacle_rows[side].astype(jnp.float32)


def edge_payload(starts, diffusivity, velocity, obstacle):
    slices, tiles, rows, lanes = starts.shape
    shape = jax.ShapeDtypeStruct((slices + 4, tiles, HALO, lanes), jnp.float32)
    vmem = pltpu.MemorySpace.VMEM
    return pl.pallas_call(
        payload_kernel,
        out_shape=(shape, shape),
        in_specs=[pl.BlockSpec(memory_space=pl.ANY)] * 4,
        out_specs=(pl.BlockSpec(memory_space=vmem), pl.BlockSpec(memory_space=vmem)),
        scratch_shapes=[
            pltpu.VMEM((2, tiles, HALO, lanes), jnp.int32),
            pltpu.SemaphoreType.DMA((2, slices + 4)),
        ],
    )(starts, diffusivity, velocity, obstacle)


def on_device(
    starts, diffusivity, velocity, obstacle, substep_scale, neighbors, coarse_x, coarse_y
):
    slice_count = starts.shape[0]
    tile_count = starts.shape[1]
    rows = starts.shape[2]
    all_tiles = tile_count * lax.axis_size("space")
    block_base = lax.axis_index("space") * tile_count

    low_rows, high_rows = edge_payload(starts, diffusivity, velocity, obstacle)
    space_count = lax.axis_size("space")
    forward = [(i, i + 1) for i in range(space_count - 1)]
    backward = [(i + 1, i) for i in range(space_count - 1)]
    from_prev = lax.ppermute(high_rows, "space", forward)
    from_next = lax.ppermute(low_rows, "space", backward)
    west_nb = neighbors[:, 0]
    east_nb = neighbors[:, 1]
    west_ok = (west_nb != all_tiles).astype(jnp.int32)
    east_ok = (east_nb != all_tiles).astype(jnp.int32)
    west_at = jnp.clip(west_nb - (block_base - tile_count), 0, tile_count - 1) * west_ok
    east_at = jnp.clip(east_nb - (block_base + tile_count), 0, tile_count - 1) * east_ok

    south_nb = neighbors[:, 2]
    north_nb = neighbors[:, 3]
    south_ok = (south_nb != all_tiles).astype(jnp.int32)
    north_ok = (north_nb != all_tiles).astype(jnp.int32)
    south = jnp.where(south_ok > 0, jnp.clip(south_nb - block_base, 0, tile_count - 1), tile_count)
    north = jnp.where(north_ok > 0, jnp.clip(north_nb - block_base, 0, tile_count - 1), tile_count)
    indices = (south, north, west_at, east_at, west_ok, east_ok)

    fine_ends = jnp.stack(
        [
            fine_propagate(
                n, starts[n], diffusivity, velocity, obstacle, from_prev, from_next, indices,
                substep_scale,
            )
            for n in range(slice_count)
        ],
        axis=0,
    )
    restricting_x = 0.5 * jnp.repeat(coarse_x, 2, axis=2)
    coarse_of_starts = apply_coarse(starts, restricting_x, coarse_y)
    correction = fine_ends - prolong(coarse_of_starts)
    coarse_jump = restrict(correction)
    earlier_correction = passed_along(correction[-1], "tm", 1)
    tm_index = lax.axis_index("tm")
    tm_count = lax.axis_size("tm")
    first_coarse = restrict(starts[0])

    def prefix_over_tm(total, power_x, power_y):
        distances = []
        distance = 1
        while distance < tm_count:
            distances.append(distance)
            distance *= 2
        powers = {}
        for distance in distances:
            powers[distance] = (power_x, power_y)
            power_x = jnp.einsum("tij,tjk->tik", power_x, power_x, precision=exact_precision)
            power_y = jnp.einsum("tij,tjk->tik", power_y, power_y, precision=exact_precision)
        half = total.shape[0] // 2
        parts = [(slice(0, half), distances[:1] + distances[1:]),
                 (slice(half, None), distances[:1] + distances[1:][::-1])]
        values = [total[part] for part, _ in parts]
        for step in range(len(distances)):
            if step == 0:
                received = passed_along(total, "tm", distances[0])
                received = [received[part] for part, _ in parts]
            else:
                received = [passed_along(values[k], "tm", parts[k][1][step]) for k in range(2)]
            for k in range(2):
                part, order = parts[k]
                distance = order[step]
                mixed = apply_coarse(received[k], powers[distance][0][part], powers[distance][1][part])
                values[k] = values[k] + jnp.where(tm_index >= distance, mixed, 0.0)
        return jnp.concatenate(values, axis=0)

    if slice_count == 1:
        seed = jnp.where(tm_index == 0, coarse_of_starts[0], 0.0)
        jump = coarse_jump[0]
        total = jump + seed
        distances = []
        distance = 1
        while distance < tm_count:
            distances.append(distance)
            distance *= 2
        power_x = coarse_x
        power_y = coarse_y
        received = passed_along(jnp.stack([total, jump], axis=0), "tm", 1)
        jump_before = received[1]
        lagged = None
        for step, distance in enumerate(distances):
            if step > 0:
                power_x = jnp.einsum("tij,tjk->tik", power_x, power_x, precision=exact_precision)
                power_y = jnp.einsum("tij,tjk->tik", power_y, power_y, precision=exact_precision)
            last = step == len(distances) - 1
            if last:
                before = passed_along(total, "tm", 1) if step > 0 else received[0]
                before_far = passed_along(total, "tm", distance + 1)
            incoming = received[0] if step == 0 else passed_along(total, "tm", distance)
            if last:
                far_mixed = apply_coarse(before_far, power_x, power_y)
                lagged = before + jnp.where(tm_index - 1 >= distance, far_mixed, 0.0)
            mixed = apply_coarse(incoming, power_x, power_y)
            total = total + jnp.where(tm_index >= distance, mixed, 0.0)
        coarse_applied = (total - jump)[None]
        coarse_before = lagged - jump_before
    else:
        shifted_jump = jnp.concatenate(
            [passed_along(coarse_jump[-1:], "tm", 1), coarse_jump[:-1]], axis=0
        )
        head = jnp.where(tm_index == 0, first_coarse[None], shifted_jump[:1])
        local = jnp.concatenate([head, shifted_jump[1:]], axis=0)
        states = [local[0]]
        for n in range(1, slice_count):
            states.append(apply_coarse(states[-1], coarse_x, coarse_y) + local[n])
        power_x = coarse_x
        power_y = coarse_y
        for n in range(1, slice_count):
            power_x = jnp.einsum("tij,tjk->tik", power_x, coarse_x, precision=exact_precision)
            power_y = jnp.einsum("tij,tjk->tik", power_y, coarse_y, precision=exact_precision)
        total = prefix_over_tm(states[-1], power_x, power_y)
        earlier = jnp.where(tm_index > 0, passed_along(total, "tm", 1), 0.0)
        own_coarse = []
        for n in range(slice_count):
            earlier = apply_coarse(earlier, coarse_x, coarse_y)
            own_coarse.append(states[n] + earlier)
        coarse_applied = apply_coarse(jnp.stack(own_coarse, axis=0), coarse_x, coarse_y)
        coarse_before = passed_along(coarse_applied[-1], "tm", 1)
    slice_ends = prolong(coarse_applied) + correction
    previous = prolong(coarse_before) + earlier_correction
    first_step = jnp.where(
        lax.axis_index("tm") == 0, jnp.zeros_like(previous), previous - starts[0]
    )
    increment = jnp.concatenate([first_step[None], slice_ends[:-1] - starts[1:]], axis=0)
    return (slice_ends, increment)


def solution(mesh):
    placed = (
        P("tm", "space", None, None),
        P("space", None, None),
        P(None, "space", None, None),
        P("space", None, None),
        P(),
        P("space", None),
        P("space", None, None),
        P("space", None, None),
    )
    return jax.shard_map(
        on_device,
        mesh=mesh,
        in_specs=placed,
        out_specs=(P("tm", "space", None, None), P("tm", "space", None, None)),
        check_vma=False,
    )
```

```python
import functools

import jax
import jax.numpy as jnp
from jax import lax
from jax.experimental import pallas as pl
from jax.experimental.pallas import tpu as pltpu
from jax.sharding import PartitionSpec as P

SUB = 12
HALO = 16
PAD = 8


exact_precision = lax.Precision.HIGHEST


def spread(value, axis, source):
    kept = jnp.where(lax.axis_index(axis) == source, value, 0).astype(value.dtype)
    return lax.psum(kept, axis)


def passed_along(block, axis, distance):
    devices = range(lax.axis_size(axis))
    route = [(i - distance, i) for i in devices if i - distance in devices]
    return lax.ppermute(block, axis, route)


def restrict(values):
    return 0.5 * (values[..., 0::2, :] + values[..., 1::2, :])


def prolong(coarse_values):
    return jnp.repeat(coarse_values, 2, axis=-2)


def apply_coarse(coarse_values, matrix_x, matrix_y):
    mixed_x = jnp.einsum("tij,...tjk->...tik", matrix_x, coarse_values, precision=exact_precision)
    return jnp.einsum("...tik,tlk->...til", mixed_x, matrix_y, precision=exact_precision)


def fine_kernel(slice_at, south_ref, north_ref, west_at_ref, east_at_ref, west_ok_ref, east_ok_ref,
                scale_ref, u_ref, diffusivity_ref, velocity_ref, obstacle_ref, prev_ref, next_ref,
                coarse_ref, out_ref, jump_ref, state_ref, other_ref, field_ref):
    tiles = u_ref.shape[0]
    rows = u_ref.shape[1]
    lanes = u_ref.shape[2]
    total = rows + 2 * HALO
    layers = prev_ref.shape[0]
    for ref in (state_ref, other_ref):
        ref[tiles] = jnp.zeros(ref.shape[1:], jnp.float32)
        for i in range(tiles):
            ref[i, pl.ds(0, PAD), :] = jnp.zeros((PAD, lanes), jnp.float32)
            ref[i, pl.ds(PAD + total, PAD), :] = jnp.zeros((PAD, lanes), jnp.float32)
    for i in range(tiles):
        west_at = west_at_ref[i]
        east_at = east_at_ref[i]
        west_ok = west_ok_ref[i] > 0
        east_ok = east_ok_ref[i] > 0
        state_ref[i, pl.ds(PAD, HALO), :] = jnp.where(west_ok, prev_ref[slice_at, west_at], 0.0)
        state_ref[i, pl.ds(PAD + HALO, rows), :] = u_ref[i]
        state_ref[i, pl.ds(PAD + HALO + rows, HALO), :] = jnp.where(
            east_ok, next_ref[slice_at, east_at], 0.0
        )
        own = (
            diffusivity_ref[i],
            velocity_ref[0, i],
            velocity_ref[1, i],
            1.0 - obstacle_ref[i].astype(jnp.float32),
        )
        factor = (1.0, 0.5, 0.5, 1.0)
        for f in range(4):
            field_at = layers - 4 + f
            field_ref[f, i, pl.ds(0, HALO), :] = factor[f] * jnp.where(
                west_ok, prev_ref[field_at, west_at], 0.0
            )
            field_ref[f, i, pl.ds(HALO, rows), :] = factor[f] * own[f]
            field_ref[f, i, pl.ds(HALO + rows, HALO), :] = factor[f] * jnp.where(
                east_ok, next_ref[field_at, east_at], 0.0
            )

    chunk = 16
    lane = lax.broadcasted_iota(jnp.int32, (chunk, lanes), 1)
    first_lane = lane == 0
    last_lane = lane == lanes - 1

    def substep(strength, src_ref, dst_ref):
        for i in range(tiles):
            south_at = south_ref[i]
            north_at = north_ref[i]
            for start in range(0, total, chunk):
                rows_at = pl.ds(PAD + start, chunk)
                current = src_ref[i, rows_at, :]
                south_tile = src_ref[south_at, rows_at, :]
                north_tile = src_ref[north_at, rows_at, :]
                from_west = src_ref[i, pl.ds(PAD + start - 1, chunk), :]
                from_east = src_ref[i, pl.ds(PAD + start + 1, chunk), :]
                from_south = pltpu.roll(jnp.where(last_lane, south_tile, current), 1, 1)
                from_north = pltpu.roll(jnp.where(first_lane, north_tile, current), lanes - 1, 1)
                diffusivity = field_ref[0, i, pl.ds(start, chunk), :]
                half_speed_x = field_ref[1, i, pl.ds(start, chunk), :]
                half_speed_y = field_ref[2, i, pl.ds(start, chunk), :]
                open_cells = field_ref[3, i, pl.ds(start, chunk), :]
                laplace = from_west + from_east + from_south + from_north - 4.0 * current
                half_transport = half_speed_x * (from_east - from_west) + half_speed_y * (
                    from_north - from_south
                )
                dst_ref[i, rows_at, :] = open_cells * (
                    current + strength * diffusivity * laplace - half_transport
                )

    def substep_pair(p, carry):
        substep(scale_ref[2 * p], state_ref, other_ref)
        substep(scale_ref[2 * p + 1], other_ref, state_ref)
        return carry

    lax.fori_loop(0, SUB // 2, substep_pair, 0)
    final_ref = state_ref
    if SUB % 2:
        substep(scale_ref[SUB - 1], state_ref, other_ref)
        final_ref = other_ref
    half_rows = rows // 2
    for i in range(tiles):
        out_ref[i] = final_ref[i, pl.ds(PAD + HALO, rows), :]
        even = final_ref[i, pl.ds(PAD + HALO, half_rows, stride=2), :]
        odd = final_ref[i, pl.ds(PAD + HALO + 1, half_rows, stride=2), :]
        coarse = coarse_ref[i]
        jump_ref[i] = 0.5 * ((even - coarse) + (odd - coarse))


def fine_propagate(slice_at, u, diffusivity, velocity, obstacle, from_prev, from_next, coarse,
                   indices, scale):
    tiles, rows, lanes = u.shape
    total = rows + 2 * HALO
    vmem = pltpu.MemorySpace.VMEM
    smem = pltpu.MemorySpace.SMEM
    return pl.pallas_call(
        functools.partial(fine_kernel, slice_at),
        out_shape=(
            jax.ShapeDtypeStruct(u.shape, u.dtype),
            jax.ShapeDtypeStruct(coarse.shape, coarse.dtype),
        ),
        in_specs=[pl.BlockSpec(memory_space=smem)] * 7 + [pl.BlockSpec(memory_space=vmem)] * 7,
        out_specs=(pl.BlockSpec(memory_space=vmem), pl.BlockSpec(memory_space=vmem)),
        scratch_shapes=[
            pltpu.VMEM((tiles + 1, total + 2 * PAD, lanes), jnp.float32),
            pltpu.VMEM((tiles + 1, total + 2 * PAD, lanes), jnp.float32),
            pltpu.VMEM((4, tiles, total, lanes), jnp.float32),
        ],
        compiler_params=pltpu.CompilerParams(vmem_limit_bytes=48 * 1024 * 1024),
    )(*indices, scale, u, diffusivity, velocity, obstacle, from_prev, from_next, coarse)


def payload_kernel(starts_hbm, diffusivity_hbm, velocity_hbm, obstacle_hbm, low_ref, high_ref,
                   obstacle_rows, sems):
    slices = starts_hbm.shape[0]
    rows = starts_hbm.shape[2]
    copies = []
    for side, (out_ref, first) in enumerate(((low_ref, 0), (high_ref, rows - HALO))):
        part = pl.ds(first, HALO)
        sources = [starts_hbm.at[n, :, part, :] for n in range(slices)]
        sources += [
            diffusivity_hbm.at[:, part, :],
            velocity_hbm.at[0, :, part, :],
            velocity_hbm.at[1, :, part, :],
        ]
        for k, source in enumerate(sources):
            copies.append(pltpu.make_async_copy(source, out_ref.at[k], sems.at[side, k]))
        copies.append(
            pltpu.make_async_copy(
                obstacle_hbm.at[:, part, :], obstacle_rows.at[side], sems.at[side, len(sources)]
            )
        )
    for copy in copies:
        copy.start()
    for copy in copies:
        copy.wait()
    for side, out_ref in enumerate((low_ref, high_ref)):
        out_ref[slices + 3] = 1.0 - obstacle_rows[side].astype(jnp.float32)


def edge_payload(starts, diffusivity, velocity, obstacle):
    slices, tiles, rows, lanes = starts.shape
    shape = jax.ShapeDtypeStruct((slices + 4, tiles, HALO, lanes), jnp.float32)
    vmem = pltpu.MemorySpace.VMEM
    return pl.pallas_call(
        payload_kernel,
        out_shape=(shape, shape),
        in_specs=[pl.BlockSpec(memory_space=pl.ANY)] * 4,
        out_specs=(pl.BlockSpec(memory_space=vmem), pl.BlockSpec(memory_space=vmem)),
        scratch_shapes=[
            pltpu.VMEM((2, tiles, HALO, lanes), jnp.int32),
            pltpu.SemaphoreType.DMA((2, slices + 4)),
        ],
    )(starts, diffusivity, velocity, obstacle)


def on_device(
    starts, diffusivity, velocity, obstacle, substep_scale, neighbors, coarse_x, coarse_y
):
    slice_count = starts.shape[0]
    tile_count = starts.shape[1]
    rows = starts.shape[2]
    all_tiles = tile_count * lax.axis_size("space")
    block_base = lax.axis_index("space") * tile_count

    low_rows, high_rows = edge_payload(starts, diffusivity, velocity, obstacle)
    space_count = lax.axis_size("space")
    forward = [(i, i + 1) for i in range(space_count - 1)]
    backward = [(i + 1, i) for i in range(space_count - 1)]
    from_prev = lax.ppermute(high_rows, "space", forward)
    from_next = lax.ppermute(low_rows, "space", backward)
    west_nb = neighbors[:, 0]
    east_nb = neighbors[:, 1]
    west_ok = (west_nb != all_tiles).astype(jnp.int32)
    east_ok = (east_nb != all_tiles).astype(jnp.int32)
    west_at = jnp.clip(west_nb - (block_base - tile_count), 0, tile_count - 1) * west_ok
    east_at = jnp.clip(east_nb - (block_base + tile_count), 0, tile_count - 1) * east_ok

    south_nb = neighbors[:, 2]
    north_nb = neighbors[:, 3]
    south_ok = (south_nb != all_tiles).astype(jnp.int32)
    north_ok = (north_nb != all_tiles).astype(jnp.int32)
    south = jnp.where(south_ok > 0, jnp.clip(south_nb - block_base, 0, tile_count - 1), tile_count)
    north = jnp.where(north_ok > 0, jnp.clip(north_nb - block_base, 0, tile_count - 1), tile_count)
    indices = (south, north, west_at, east_at, west_ok, east_ok)

    restricting_x = 0.5 * jnp.repeat(coarse_x, 2, axis=2)
    coarse_of_starts = apply_coarse(starts, restricting_x, coarse_y)
    fine_results = [
        fine_propagate(
            n, starts[n], diffusivity, velocity, obstacle, from_prev, from_next,
            coarse_of_starts[n], indices, substep_scale,
        )
        for n in range(slice_count)
    ]
    fine_ends = jnp.stack([result[0] for result in fine_results], axis=0)
    coarse_jump = jnp.stack([result[1] for result in fine_results], axis=0)
    correction = fine_ends - prolong(coarse_of_starts)
    earlier_correction = passed_along(correction[-1], "tm", 1)
    tm_index = lax.axis_index("tm")
    tm_count = lax.axis_size("tm")
    first_coarse = restrict(starts[0])

    def prefix_over_tm(total, power_x, power_y):
        distances = []
        distance = 1
        while distance < tm_count:
            distances.append(distance)
            distance *= 2
        powers = {}
        for distance in distances:
            powers[distance] = (power_x, power_y)
            power_x = jnp.einsum("tij,tjk->tik", power_x, power_x, precision=exact_precision)
            power_y = jnp.einsum("tij,tjk->tik", power_y, power_y, precision=exact_precision)
        half = total.shape[0] // 2
        parts = [(slice(0, half), distances[:1] + distances[1:]),
                 (slice(half, None), distances[:1] + distances[1:][::-1])]
        values = [total[part] for part, _ in parts]
        for step in range(len(distances)):
            if step == 0:
                received = passed_along(total, "tm", distances[0])
                received = [received[part] for part, _ in parts]
            else:
                received = [passed_along(values[k], "tm", parts[k][1][step]) for k in range(2)]
            for k in range(2):
                part, order = parts[k]
                distance = order[step]
                mixed = apply_coarse(received[k], powers[distance][0][part], powers[distance][1][part])
                values[k] = values[k] + jnp.where(tm_index >= distance, mixed, 0.0)
        return jnp.concatenate(values, axis=0)

    if slice_count == 1:
        seed = jnp.where(tm_index == 0, coarse_of_starts[0], 0.0)
        reached = prefix_over_tm(coarse_jump[0] + seed, coarse_x, coarse_y)
        coarse_applied = (reached - coarse_jump[0])[None]
    else:
        shifted_jump = jnp.concatenate(
            [passed_along(coarse_jump[-1:], "tm", 1), coarse_jump[:-1]], axis=0
        )
        head = jnp.where(tm_index == 0, first_coarse[None], shifted_jump[:1])
        local = jnp.concatenate([head, shifted_jump[1:]], axis=0)
        states = [local[0]]
        for n in range(1, slice_count):
            states.append(apply_coarse(states[-1], coarse_x, coarse_y) + local[n])
        power_x = coarse_x
        power_y = coarse_y
        for n in range(1, slice_count):
            power_x = jnp.einsum("tij,tjk->tik", power_x, coarse_x, precision=exact_precision)
            power_y = jnp.einsum("tij,tjk->tik", power_y, coarse_y, precision=exact_precision)
        total = prefix_over_tm(states[-1], power_x, power_y)
        earlier = jnp.where(tm_index > 0, passed_along(total, "tm", 1), 0.0)
        own_coarse = []
        for n in range(slice_count):
            earlier = apply_coarse(earlier, coarse_x, coarse_y)
            own_coarse.append(states[n] + earlier)
        coarse_applied = apply_coarse(jnp.stack(own_coarse, axis=0), coarse_x, coarse_y)
    slice_ends = prolong(coarse_applied) + correction
    previous = prolong(passed_along(coarse_applied[-1], "tm", 1)) + earlier_correction
    first_step = jnp.where(
        lax.axis_index("tm") == 0, jnp.zeros_like(previous), previous - starts[0]
    )
    increment = jnp.concatenate([first_step[None], slice_ends[:-1] - starts[1:]], axis=0)
    return (slice_ends, increment)


def solution(mesh):
    placed = (
        P("tm", "space", None, None),
        P("space", None, None),
        P(None, "space", None, None),
        P("space", None, None),
        P(),
        P("space", None),
        P("space", None, None),
        P("space", None, None),
    )
    return jax.shard_map(
        on_device,
        mesh=mesh,
        in_specs=placed,
        out_specs=(P("tm", "space", None, None), P("tm", "space", None, None)),
        check_vma=False,
    )
```

```python
import functools

import jax
import jax.numpy as jnp
from jax import lax
from jax.experimental import pallas as pl
from jax.experimental.pallas import tpu as pltpu
from jax.sharding import PartitionSpec as P

SUB = 12
HALO = 16
PAD = 8


exact_precision = lax.Precision.HIGHEST


def spread(value, axis, source):
    kept = jnp.where(lax.axis_index(axis) == source, value, 0).astype(value.dtype)
    return lax.psum(kept, axis)


def passed_along(block, axis, distance):
    devices = range(lax.axis_size(axis))
    route = [(i - distance, i) for i in devices if i - distance in devices]
    return lax.ppermute(block, axis, route)


def restrict(values):
    return 0.5 * (values[..., 0::2, :] + values[..., 1::2, :])


def prolong(coarse_values):
    return jnp.repeat(coarse_values, 2, axis=-2)


def apply_coarse(coarse_values, matrix_x, matrix_y):
    mixed_x = jnp.einsum("tij,...tjk->...tik", matrix_x, coarse_values, precision=exact_precision)
    return jnp.einsum("...tik,tlk->...til", mixed_x, matrix_y, precision=exact_precision)


def fine_kernel(slice_at, south_ref, north_ref, west_at_ref, east_at_ref, west_ok_ref, east_ok_ref,
                scale_ref, u_ref, diffusivity_ref, velocity_ref, obstacle_ref, prev_ref, next_ref,
                coarse_ref, out_ref, jump_ref, state_ref, other_ref, field_ref):
    tiles = u_ref.shape[0]
    rows = u_ref.shape[1]
    lanes = u_ref.shape[2]
    total = rows + 2 * HALO
    layers = prev_ref.shape[0]
    for ref in (state_ref, other_ref):
        ref[tiles] = jnp.zeros(ref.shape[1:], jnp.float32)
        for i in range(tiles):
            ref[i, pl.ds(0, PAD), :] = jnp.zeros((PAD, lanes), jnp.float32)
            ref[i, pl.ds(PAD + total, PAD), :] = jnp.zeros((PAD, lanes), jnp.float32)
    for i in range(tiles):
        west_at = west_at_ref[i]
        east_at = east_at_ref[i]
        west_ok = west_ok_ref[i] > 0
        east_ok = east_ok_ref[i] > 0
        state_ref[i, pl.ds(PAD, HALO), :] = jnp.where(west_ok, prev_ref[slice_at, west_at], 0.0)
        state_ref[i, pl.ds(PAD + HALO, rows), :] = u_ref[i]
        state_ref[i, pl.ds(PAD + HALO + rows, HALO), :] = jnp.where(
            east_ok, next_ref[slice_at, east_at], 0.0
        )
        own = (
            diffusivity_ref[i],
            velocity_ref[0, i],
            velocity_ref[1, i],
            1.0 - obstacle_ref[i].astype(jnp.float32),
        )
        factor = (1.0, 0.5, 0.5, 1.0)
        for f in range(4):
            field_at = layers - 4 + f
            field_ref[f, i, pl.ds(0, HALO), :] = factor[f] * jnp.where(
                west_ok, prev_ref[field_at, west_at], 0.0
            )
            field_ref[f, i, pl.ds(HALO, rows), :] = factor[f] * own[f]
            field_ref[f, i, pl.ds(HALO + rows, HALO), :] = factor[f] * jnp.where(
                east_ok, next_ref[field_at, east_at], 0.0
            )

    chunk = 16
    lane = lax.broadcasted_iota(jnp.int32, (chunk, lanes), 1)
    first_lane = lane == 0
    last_lane = lane == lanes - 1

    def substep(strength, src_ref, dst_ref):
        for i in range(tiles):
            south_at = south_ref[i]
            north_at = north_ref[i]
            for start in range(0, total, chunk):
                rows_at = pl.ds(PAD + start, chunk)
                current = src_ref[i, rows_at, :]
                south_tile = src_ref[south_at, rows_at, :]
                north_tile = src_ref[north_at, rows_at, :]
                from_west = src_ref[i, pl.ds(PAD + start - 1, chunk), :]
                from_east = src_ref[i, pl.ds(PAD + start + 1, chunk), :]
                from_south = pltpu.roll(jnp.where(last_lane, south_tile, current), 1, 1)
                from_north = pltpu.roll(jnp.where(first_lane, north_tile, current), lanes - 1, 1)
                diffusivity = field_ref[0, i, pl.ds(start, chunk), :]
                half_speed_x = field_ref[1, i, pl.ds(start, chunk), :]
                half_speed_y = field_ref[2, i, pl.ds(start, chunk), :]
                open_cells = field_ref[3, i, pl.ds(start, chunk), :]
                laplace = from_west + from_east + from_south + from_north - 4.0 * current
                half_transport = half_speed_x * (from_east - from_west) + half_speed_y * (
                    from_north - from_south
                )
                dst_ref[i, rows_at, :] = open_cells * (
                    current + strength * diffusivity * laplace - half_transport
                )

    def substep_pair(p, carry):
        substep(scale_ref[2 * p], state_ref, other_ref)
        substep(scale_ref[2 * p + 1], other_ref, state_ref)
        return carry

    lax.fori_loop(0, SUB // 2, substep_pair, 0)
    final_ref = state_ref
    if SUB % 2:
        substep(scale_ref[SUB - 1], state_ref, other_ref)
        final_ref = other_ref
    half_rows = rows // 2
    for i in range(tiles):
        out_ref[i] = final_ref[i, pl.ds(PAD + HALO, rows), :]
        even = final_ref[i, pl.ds(PAD + HALO, half_rows, stride=2), :]
        odd = final_ref[i, pl.ds(PAD + HALO + 1, half_rows, stride=2), :]
        coarse = coarse_ref[i]
        jump_ref[i] = 0.5 * ((even - coarse) + (odd - coarse))


def fine_propagate(slice_at, u, diffusivity, velocity, obstacle, from_prev, from_next, coarse,
                   indices, scale):
    tiles, rows, lanes = u.shape
    total = rows + 2 * HALO
    vmem = pltpu.MemorySpace.VMEM
    smem = pltpu.MemorySpace.SMEM
    return pl.pallas_call(
        functools.partial(fine_kernel, slice_at),
        out_shape=(
            jax.ShapeDtypeStruct(u.shape, u.dtype),
            jax.ShapeDtypeStruct(coarse.shape, coarse.dtype),
        ),
        in_specs=[pl.BlockSpec(memory_space=smem)] * 7 + [pl.BlockSpec(memory_space=vmem)] * 7,
        out_specs=(pl.BlockSpec(memory_space=vmem), pl.BlockSpec(memory_space=vmem)),
        scratch_shapes=[
            pltpu.VMEM((tiles + 1, total + 2 * PAD, lanes), jnp.float32),
            pltpu.VMEM((tiles + 1, total + 2 * PAD, lanes), jnp.float32),
            pltpu.VMEM((4, tiles, total, lanes), jnp.float32),
        ],
        compiler_params=pltpu.CompilerParams(vmem_limit_bytes=48 * 1024 * 1024),
    )(*indices, scale, u, diffusivity, velocity, obstacle, from_prev, from_next, coarse)


def payload_kernel(starts_hbm, diffusivity_hbm, velocity_hbm, obstacle_hbm, low_ref, high_ref,
                   obstacle_rows, sems):
    slices = starts_hbm.shape[0]
    rows = starts_hbm.shape[2]
    copies = []
    for side, (out_ref, first) in enumerate(((low_ref, 0), (high_ref, rows - HALO))):
        part = pl.ds(first, HALO)
        sources = [starts_hbm.at[n, :, part, :] for n in range(slices)]
        sources += [
            diffusivity_hbm.at[:, part, :],
            velocity_hbm.at[0, :, part, :],
            velocity_hbm.at[1, :, part, :],
        ]
        for k, source in enumerate(sources):
            copies.append(pltpu.make_async_copy(source, out_ref.at[k], sems.at[side, k]))
        copies.append(
            pltpu.make_async_copy(
                obstacle_hbm.at[:, part, :], obstacle_rows.at[side], sems.at[side, len(sources)]
            )
        )
    for copy in copies:
        copy.start()
    for copy in copies:
        copy.wait()
    for side, out_ref in enumerate((low_ref, high_ref)):
        out_ref[slices + 3] = 1.0 - obstacle_rows[side].astype(jnp.float32)


def edge_payload(starts, diffusivity, velocity, obstacle):
    slices, tiles, rows, lanes = starts.shape
    shape = jax.ShapeDtypeStruct((slices + 4, tiles, HALO, lanes), jnp.float32)
    vmem = pltpu.MemorySpace.VMEM
    return pl.pallas_call(
        payload_kernel,
        out_shape=(shape, shape),
        in_specs=[pl.BlockSpec(memory_space=pl.ANY)] * 4,
        out_specs=(pl.BlockSpec(memory_space=vmem), pl.BlockSpec(memory_space=vmem)),
        scratch_shapes=[
            pltpu.VMEM((2, tiles, HALO, lanes), jnp.int32),
            pltpu.SemaphoreType.DMA((2, slices + 4)),
        ],
    )(starts, diffusivity, velocity, obstacle)


def on_device(
    starts, diffusivity, velocity, obstacle, substep_scale, neighbors, coarse_x, coarse_y
):
    slice_count = starts.shape[0]
    tile_count = starts.shape[1]
    rows = starts.shape[2]
    all_tiles = tile_count * lax.axis_size("space")
    block_base = lax.axis_index("space") * tile_count

    low_rows, high_rows = edge_payload(starts, diffusivity, velocity, obstacle)
    space_count = lax.axis_size("space")
    forward = [(i, i + 1) for i in range(space_count - 1)]
    backward = [(i + 1, i) for i in range(space_count - 1)]
    from_prev = lax.ppermute(high_rows, "space", forward)
    from_next = lax.ppermute(low_rows, "space", backward)
    west_nb = neighbors[:, 0]
    east_nb = neighbors[:, 1]
    west_ok = (west_nb != all_tiles).astype(jnp.int32)
    east_ok = (east_nb != all_tiles).astype(jnp.int32)
    west_at = jnp.clip(west_nb - (block_base - tile_count), 0, tile_count - 1) * west_ok
    east_at = jnp.clip(east_nb - (block_base + tile_count), 0, tile_count - 1) * east_ok

    south_nb = neighbors[:, 2]
    north_nb = neighbors[:, 3]
    south_ok = (south_nb != all_tiles).astype(jnp.int32)
    north_ok = (north_nb != all_tiles).astype(jnp.int32)
    south = jnp.where(south_ok > 0, jnp.clip(south_nb - block_base, 0, tile_count - 1), tile_count)
    north = jnp.where(north_ok > 0, jnp.clip(north_nb - block_base, 0, tile_count - 1), tile_count)
    indices = (south, north, west_at, east_at, west_ok, east_ok)

    restricting_x = 0.5 * jnp.repeat(coarse_x, 2, axis=2)
    coarse_of_starts = apply_coarse(starts, restricting_x, coarse_y)
    fine_results = [
        fine_propagate(
            n, starts[n], diffusivity, velocity, obstacle, from_prev, from_next,
            coarse_of_starts[n], indices, substep_scale,
        )
        for n in range(slice_count)
    ]
    fine_ends = jnp.stack([result[0] for result in fine_results], axis=0)
    coarse_jump = jnp.stack([result[1] for result in fine_results], axis=0)
    correction = fine_ends - prolong(coarse_of_starts)
    last_correction, coarse_jump = lax.optimization_barrier((correction[-1], coarse_jump))
    earlier_correction = passed_along(last_correction, "tm", 1)
    tm_index = lax.axis_index("tm")
    tm_count = lax.axis_size("tm")
    first_coarse = restrict(starts[0])

    def prefix_over_tm(total, power_x, power_y):
        distances = []
        distance = 1
        while distance < tm_count:
            distances.append(distance)
            distance *= 2
        powers = {}
        for distance in distances:
            powers[distance] = (power_x, power_y)
            power_x = jnp.einsum("tij,tjk->tik", power_x, power_x, precision=exact_precision)
            power_y = jnp.einsum("tij,tjk->tik", power_y, power_y, precision=exact_precision)
        half = total.shape[0] // 2
        parts = [(slice(0, half), distances[:1] + distances[1:]),
                 (slice(half, None), distances[:1] + distances[1:][::-1])]
        values = [total[part] for part, _ in parts]
        for step in range(len(distances)):
            if step == 0:
                received = passed_along(total, "tm", distances[0])
                received = [received[part] for part, _ in parts]
            else:
                received = [passed_along(values[k], "tm", parts[k][1][step]) for k in range(2)]
            for k in range(2):
                part, order = parts[k]
                distance = order[step]
                mixed = apply_coarse(received[k], powers[distance][0][part], powers[distance][1][part])
                values[k] = values[k] + jnp.where(tm_index >= distance, mixed, 0.0)
        return jnp.concatenate(values, axis=0)

    if slice_count == 1:
        seed = jnp.where(tm_index == 0, coarse_of_starts[0], 0.0)
        reached = prefix_over_tm(coarse_jump[0] + seed, coarse_x, coarse_y)
        coarse_applied = (reached - coarse_jump[0])[None]
    else:
        shifted_jump = jnp.concatenate(
            [passed_along(coarse_jump[-1:], "tm", 1), coarse_jump[:-1]], axis=0
        )
        head = jnp.where(tm_index == 0, first_coarse[None], shifted_jump[:1])
        local = jnp.concatenate([head, shifted_jump[1:]], axis=0)
        states = [local[0]]
        for n in range(1, slice_count):
            states.append(apply_coarse(states[-1], coarse_x, coarse_y) + local[n])
        power_x = coarse_x
        power_y = coarse_y
        for n in range(1, slice_count):
            power_x = jnp.einsum("tij,tjk->tik", power_x, coarse_x, precision=exact_precision)
            power_y = jnp.einsum("tij,tjk->tik", power_y, coarse_y, precision=exact_precision)
        total = prefix_over_tm(states[-1], power_x, power_y)
        earlier = jnp.where(tm_index > 0, passed_along(total, "tm", 1), 0.0)
        own_coarse = []
        for n in range(slice_count):
            earlier = apply_coarse(earlier, coarse_x, coarse_y)
            own_coarse.append(states[n] + earlier)
        coarse_applied = apply_coarse(jnp.stack(own_coarse, axis=0), coarse_x, coarse_y)
    slice_ends = prolong(coarse_applied) + correction
    previous = prolong(passed_along(coarse_applied[-1], "tm", 1)) + earlier_correction
    first_step = jnp.where(
        lax.axis_index("tm") == 0, jnp.zeros_like(previous), previous - starts[0]
    )
    increment = jnp.concatenate([first_step[None], slice_ends[:-1] - starts[1:]], axis=0)
    return (slice_ends, increment)


def solution(mesh):
    placed = (
        P("tm", "space", None, None),
        P("space", None, None),
        P(None, "space", None, None),
        P("space", None, None),
        P(),
        P("space", None),
        P("space", None, None),
        P("space", None, None),
    )
    return jax.shard_map(
        on_device,
        mesh=mesh,
        in_specs=placed,
        out_specs=(P("tm", "space", None, None), P("tm", "space", None, None)),
        check_vma=False,
    )
```

```python
import functools

import jax
import jax.numpy as jnp
from jax import lax
from jax.experimental import pallas as pl
from jax.experimental.pallas import tpu as pltpu
from jax.sharding import PartitionSpec as P

SUB = 12
HALO = 16
PAD = 8


exact_precision = lax.Precision.HIGHEST


def spread(value, axis, source):
    kept = jnp.where(lax.axis_index(axis) == source, value, 0).astype(value.dtype)
    return lax.psum(kept, axis)


def passed_along(block, axis, distance):
    devices = range(lax.axis_size(axis))
    route = [(i - distance, i) for i in devices if i - distance in devices]
    return lax.ppermute(block, axis, route)


def restrict(values):
    return 0.5 * (values[..., 0::2, :] + values[..., 1::2, :])


def prolong(coarse_values):
    return jnp.repeat(coarse_values, 2, axis=-2)


def apply_coarse(coarse_values, matrix_x, matrix_y):
    mixed_x = jnp.einsum("tij,...tjk->...tik", matrix_x, coarse_values, precision=exact_precision)
    return jnp.einsum("...tik,tlk->...til", mixed_x, matrix_y, precision=exact_precision)


def fine_kernel(slice_at, south_ref, north_ref, west_at_ref, east_at_ref, west_ok_ref, east_ok_ref,
                scale_ref, u_ref, diffusivity_ref, velocity_ref, obstacle_ref, prev_ref, next_ref,
                coarse_ref, out_ref, jump_ref, state_ref, other_ref, field_ref):
    tiles = u_ref.shape[0]
    rows = u_ref.shape[1]
    lanes = u_ref.shape[2]
    total = rows + 2 * HALO
    layers = prev_ref.shape[0]
    for ref in (state_ref, other_ref):
        ref[tiles] = jnp.zeros(ref.shape[1:], jnp.float32)
        for i in range(tiles):
            ref[i, pl.ds(0, PAD), :] = jnp.zeros((PAD, lanes), jnp.float32)
            ref[i, pl.ds(PAD + total, PAD), :] = jnp.zeros((PAD, lanes), jnp.float32)
    for i in range(tiles):
        west_at = west_at_ref[i]
        east_at = east_at_ref[i]
        west_ok = west_ok_ref[i] > 0
        east_ok = east_ok_ref[i] > 0
        state_ref[i, pl.ds(PAD, HALO), :] = jnp.where(west_ok, prev_ref[slice_at, west_at], 0.0)
        state_ref[i, pl.ds(PAD + HALO, rows), :] = u_ref[i]
        state_ref[i, pl.ds(PAD + HALO + rows, HALO), :] = jnp.where(
            east_ok, next_ref[slice_at, east_at], 0.0
        )
        own = (
            diffusivity_ref[i],
            velocity_ref[0, i],
            velocity_ref[1, i],
            1.0 - obstacle_ref[i].astype(jnp.float32),
        )
        factor = (1.0, 0.5, 0.5, 1.0)
        for f in range(4):
            field_at = layers - 4 + f
            field_ref[f, i, pl.ds(0, HALO), :] = factor[f] * jnp.where(
                west_ok, prev_ref[field_at, west_at], 0.0
            )
            field_ref[f, i, pl.ds(HALO, rows), :] = factor[f] * own[f]
            field_ref[f, i, pl.ds(HALO + rows, HALO), :] = factor[f] * jnp.where(
                east_ok, next_ref[field_at, east_at], 0.0
            )

    chunk = 16
    lane = lax.broadcasted_iota(jnp.int32, (chunk, lanes), 1)
    first_lane = lane == 0
    last_lane = lane == lanes - 1

    def substep(strength, src_ref, dst_ref):
        for i in range(tiles):
            south_at = south_ref[i]
            north_at = north_ref[i]
            for start in range(0, total, chunk):
                rows_at = pl.ds(PAD + start, chunk)
                current = src_ref[i, rows_at, :]
                south_tile = src_ref[south_at, rows_at, :]
                north_tile = src_ref[north_at, rows_at, :]
                from_west = src_ref[i, pl.ds(PAD + start - 1, chunk), :]
                from_east = src_ref[i, pl.ds(PAD + start + 1, chunk), :]
                from_south = pltpu.roll(jnp.where(last_lane, south_tile, current), 1, 1)
                from_north = pltpu.roll(jnp.where(first_lane, north_tile, current), lanes - 1, 1)
                diffusivity = field_ref[0, i, pl.ds(start, chunk), :]
                half_speed_x = field_ref[1, i, pl.ds(start, chunk), :]
                half_speed_y = field_ref[2, i, pl.ds(start, chunk), :]
                open_cells = field_ref[3, i, pl.ds(start, chunk), :]
                laplace = from_west + from_east + from_south + from_north - 4.0 * current
                half_transport = half_speed_x * (from_east - from_west) + half_speed_y * (
                    from_north - from_south
                )
                dst_ref[i, rows_at, :] = open_cells * (
                    current + strength * diffusivity * laplace - half_transport
                )

    def substep_pair(p, carry):
        substep(scale_ref[2 * p], state_ref, other_ref)
        substep(scale_ref[2 * p + 1], other_ref, state_ref)
        return carry

    lax.fori_loop(0, SUB // 2, substep_pair, 0)
    final_ref = state_ref
    if SUB % 2:
        substep(scale_ref[SUB - 1], state_ref, other_ref)
        final_ref = other_ref
    half_rows = rows // 2
    for i in range(tiles):
        out_ref[i] = final_ref[i, pl.ds(PAD + HALO, rows), :]
        even = final_ref[i, pl.ds(PAD + HALO, half_rows, stride=2), :]
        odd = final_ref[i, pl.ds(PAD + HALO + 1, half_rows, stride=2), :]
        coarse = coarse_ref[i]
        jump_ref[i] = 0.5 * ((even - coarse) + (odd - coarse))


def fine_propagate(slice_at, u, diffusivity, velocity, obstacle, from_prev, from_next, coarse,
                   indices, scale):
    tiles, rows, lanes = u.shape
    total = rows + 2 * HALO
    vmem = pltpu.MemorySpace.VMEM
    smem = pltpu.MemorySpace.SMEM
    return pl.pallas_call(
        functools.partial(fine_kernel, slice_at),
        out_shape=(
            jax.ShapeDtypeStruct(u.shape, u.dtype),
            jax.ShapeDtypeStruct(coarse.shape, coarse.dtype),
        ),
        in_specs=[pl.BlockSpec(memory_space=smem)] * 7 + [pl.BlockSpec(memory_space=vmem)] * 7,
        out_specs=(pl.BlockSpec(memory_space=vmem), pl.BlockSpec(memory_space=vmem)),
        scratch_shapes=[
            pltpu.VMEM((tiles + 1, total + 2 * PAD, lanes), jnp.float32),
            pltpu.VMEM((tiles + 1, total + 2 * PAD, lanes), jnp.float32),
            pltpu.VMEM((4, tiles, total, lanes), jnp.float32),
        ],
        compiler_params=pltpu.CompilerParams(vmem_limit_bytes=48 * 1024 * 1024),
    )(*indices, scale, u, diffusivity, velocity, obstacle, from_prev, from_next, coarse)


def payload_kernel(starts_hbm, diffusivity_hbm, velocity_hbm, obstacle_hbm, low_ref, high_ref,
                   obstacle_rows, sems):
    slices = starts_hbm.shape[0]
    rows = starts_hbm.shape[2]
    copies = []
    for side, (out_ref, first) in enumerate(((low_ref, 0), (high_ref, rows - HALO))):
        part = pl.ds(first, HALO)
        sources = [starts_hbm.at[n, :, part, :] for n in range(slices)]
        sources += [
            diffusivity_hbm.at[:, part, :],
            velocity_hbm.at[0, :, part, :],
            velocity_hbm.at[1, :, part, :],
        ]
        for k, source in enumerate(sources):
            copies.append(pltpu.make_async_copy(source, out_ref.at[k], sems.at[side, k]))
        copies.append(
            pltpu.make_async_copy(
                obstacle_hbm.at[:, part, :], obstacle_rows.at[side], sems.at[side, len(sources)]
            )
        )
    for copy in copies:
        copy.start()
    for copy in copies:
        copy.wait()
    for side, out_ref in enumerate((low_ref, high_ref)):
        out_ref[slices + 3] = 1.0 - obstacle_rows[side].astype(jnp.float32)


def edge_payload(starts, diffusivity, velocity, obstacle):
    slices, tiles, rows, lanes = starts.shape
    shape = jax.ShapeDtypeStruct((slices + 4, tiles, HALO, lanes), jnp.float32)
    vmem = pltpu.MemorySpace.VMEM
    return pl.pallas_call(
        payload_kernel,
        out_shape=(shape, shape),
        in_specs=[pl.BlockSpec(memory_space=pl.ANY)] * 4,
        out_specs=(pl.BlockSpec(memory_space=vmem), pl.BlockSpec(memory_space=vmem)),
        scratch_shapes=[
            pltpu.VMEM((2, tiles, HALO, lanes), jnp.int32),
            pltpu.SemaphoreType.DMA((2, slices + 4)),
        ],
    )(starts, diffusivity, velocity, obstacle)


def on_device(
    starts, diffusivity, velocity, obstacle, substep_scale, neighbors, coarse_x, coarse_y
):
    slice_count = starts.shape[0]
    tile_count = starts.shape[1]
    rows = starts.shape[2]
    all_tiles = tile_count * lax.axis_size("space")
    block_base = lax.axis_index("space") * tile_count

    low_rows, high_rows = edge_payload(starts, diffusivity, velocity, obstacle)
    space_count = lax.axis_size("space")
    forward = [(i, i + 1) for i in range(space_count - 1)]
    backward = [(i + 1, i) for i in range(space_count - 1)]
    from_prev = lax.ppermute(high_rows, "space", forward)
    from_next = lax.ppermute(low_rows, "space", backward)
    west_nb = neighbors[:, 0]
    east_nb = neighbors[:, 1]
    west_ok = (west_nb != all_tiles).astype(jnp.int32)
    east_ok = (east_nb != all_tiles).astype(jnp.int32)
    west_at = jnp.clip(west_nb - (block_base - tile_count), 0, tile_count - 1) * west_ok
    east_at = jnp.clip(east_nb - (block_base + tile_count), 0, tile_count - 1) * east_ok

    south_nb = neighbors[:, 2]
    north_nb = neighbors[:, 3]
    south_ok = (south_nb != all_tiles).astype(jnp.int32)
    north_ok = (north_nb != all_tiles).astype(jnp.int32)
    south = jnp.where(south_ok > 0, jnp.clip(south_nb - block_base, 0, tile_count - 1), tile_count)
    north = jnp.where(north_ok > 0, jnp.clip(north_nb - block_base, 0, tile_count - 1), tile_count)
    indices = (south, north, west_at, east_at, west_ok, east_ok)

    restricting_x = 0.5 * jnp.repeat(coarse_x, 2, axis=2)
    coarse_of_starts = apply_coarse(starts, restricting_x, coarse_y)
    fine_results = [
        fine_propagate(
            n, starts[n], diffusivity, velocity, obstacle, from_prev, from_next,
            coarse_of_starts[n], indices, substep_scale,
        )
        for n in range(slice_count)
    ]
    fine_ends = jnp.stack([result[0] for result in fine_results], axis=0)
    coarse_jump = jnp.stack([result[1] for result in fine_results], axis=0)
    correction = fine_ends - prolong(coarse_of_starts)
    last_correction, coarse_jump = lax.optimization_barrier((correction[-1], coarse_jump))
    earlier_correction = passed_along(last_correction, "tm", 1)
    tm_index = lax.axis_index("tm")
    tm_count = lax.axis_size("tm")
    first_coarse = restrict(starts[0])

    def prefix_over_tm(total, power_x, power_y):
        distances = []
        distance = 1
        while distance < tm_count:
            distances.append(distance)
            distance *= 2
        powers = {}
        for distance in distances:
            powers[distance] = (power_x, power_y)
            power_x = jnp.einsum("tij,tjk->tik", power_x, power_x, precision=exact_precision)
            power_y = jnp.einsum("tij,tjk->tik", power_y, power_y, precision=exact_precision)
        parts = [(slice(0, None), distances)]
        values = [total[part] for part, _ in parts]
        for step in range(len(distances)):
            if step == 0:
                received = passed_along(total, "tm", distances[0])
                received = [received[part] for part, _ in parts]
            else:
                received = [passed_along(values[k], "tm", parts[k][1][step]) for k in range(len(parts))]
            for k in range(len(parts)):
                part, order = parts[k]
                distance = order[step]
                mixed = apply_coarse(received[k], powers[distance][0][part], powers[distance][1][part])
                values[k] = values[k] + jnp.where(tm_index >= distance, mixed, 0.0)
        return jnp.concatenate(values, axis=0)

    if slice_count == 1:
        seed = jnp.where(tm_index == 0, coarse_of_starts[0], 0.0)
        reached = prefix_over_tm(coarse_jump[0] + seed, coarse_x, coarse_y)
        coarse_applied = (reached - coarse_jump[0])[None]
    else:
        shifted_jump = jnp.concatenate(
            [passed_along(coarse_jump[-1:], "tm", 1), coarse_jump[:-1]], axis=0
        )
        head = jnp.where(tm_index == 0, first_coarse[None], shifted_jump[:1])
        local = jnp.concatenate([head, shifted_jump[1:]], axis=0)
        states = [local[0]]
        for n in range(1, slice_count):
            states.append(apply_coarse(states[-1], coarse_x, coarse_y) + local[n])
        power_x = coarse_x
        power_y = coarse_y
        for n in range(1, slice_count):
            power_x = jnp.einsum("tij,tjk->tik", power_x, coarse_x, precision=exact_precision)
            power_y = jnp.einsum("tij,tjk->tik", power_y, coarse_y, precision=exact_precision)
        total = prefix_over_tm(states[-1], power_x, power_y)
        earlier = jnp.where(tm_index > 0, passed_along(total, "tm", 1), 0.0)
        own_coarse = []
        for n in range(slice_count):
            earlier = apply_coarse(earlier, coarse_x, coarse_y)
            own_coarse.append(states[n] + earlier)
        coarse_applied = apply_coarse(jnp.stack(own_coarse, axis=0), coarse_x, coarse_y)
    slice_ends = prolong(coarse_applied) + correction
    previous = prolong(passed_along(coarse_applied[-1], "tm", 1)) + earlier_correction
    first_step = jnp.where(
        lax.axis_index("tm") == 0, jnp.zeros_like(previous), previous - starts[0]
    )
    increment = jnp.concatenate([first_step[None], slice_ends[:-1] - starts[1:]], axis=0)
    return (slice_ends, increment)


def solution(mesh):
    placed = (
        P("tm", "space", None, None),
        P("space", None, None),
        P(None, "space", None, None),
        P("space", None, None),
        P(),
        P("space", None),
        P("space", None, None),
        P("space", None, None),
    )
    return jax.shard_map(
        on_device,
        mesh=mesh,
        in_specs=placed,
        out_specs=(P("tm", "space", None, None), P("tm", "space", None, None)),
        check_vma=False,
    )
```

```python
import functools

import jax
import jax.numpy as jnp
from jax import lax
from jax.experimental import pallas as pl
from jax.experimental.pallas import tpu as pltpu
from jax.sharding import PartitionSpec as P

SUB = 12
HALO = 16
PAD = 8


exact_precision = lax.Precision.HIGHEST


def spread(value, axis, source):
    kept = jnp.where(lax.axis_index(axis) == source, value, 0).astype(value.dtype)
    return lax.psum(kept, axis)


def passed_along(block, axis, distance):
    devices = range(lax.axis_size(axis))
    route = [(i - distance, i) for i in devices if i - distance in devices]
    return lax.ppermute(block, axis, route)


def restrict(values):
    return 0.5 * (values[..., 0::2, :] + values[..., 1::2, :])


def prolong(coarse_values):
    return jnp.repeat(coarse_values, 2, axis=-2)


def apply_coarse(coarse_values, matrix_x, matrix_y):
    mixed_x = jnp.einsum("tij,...tjk->...tik", matrix_x, coarse_values, precision=exact_precision)
    return jnp.einsum("...tik,tlk->...til", mixed_x, matrix_y, precision=exact_precision)


def fine_kernel(slice_at, south_ref, north_ref, west_at_ref, east_at_ref, west_ok_ref, east_ok_ref,
                scale_ref, u_ref, diffusivity_ref, velocity_ref, obstacle_ref, prev_ref, next_ref,
                coarse_ref, out_ref, jump_ref, state_ref, other_ref, field_ref):
    tiles = u_ref.shape[0]
    rows = u_ref.shape[1]
    lanes = u_ref.shape[2]
    total = rows + 2 * HALO
    layers = prev_ref.shape[0]
    for ref in (state_ref, other_ref):
        ref[tiles] = jnp.zeros(ref.shape[1:], jnp.float32)
        for i in range(tiles):
            ref[i, pl.ds(0, PAD), :] = jnp.zeros((PAD, lanes), jnp.float32)
            ref[i, pl.ds(PAD + total, PAD), :] = jnp.zeros((PAD, lanes), jnp.float32)
    for i in range(tiles):
        west_at = west_at_ref[i]
        east_at = east_at_ref[i]
        west_ok = west_ok_ref[i] > 0
        east_ok = east_ok_ref[i] > 0
        state_ref[i, pl.ds(PAD, HALO), :] = jnp.where(west_ok, prev_ref[slice_at, west_at], 0.0)
        state_ref[i, pl.ds(PAD + HALO, rows), :] = u_ref[i]
        state_ref[i, pl.ds(PAD + HALO + rows, HALO), :] = jnp.where(
            east_ok, next_ref[slice_at, east_at], 0.0
        )
        own = (
            diffusivity_ref[i],
            velocity_ref[0, i],
            velocity_ref[1, i],
            1.0 - obstacle_ref[i].astype(jnp.float32),
        )
        factor = (1.0, 0.5, 0.5, 1.0)
        for f in range(4):
            field_at = layers - 4 + f
            field_ref[f, i, pl.ds(0, HALO), :] = factor[f] * jnp.where(
                west_ok, prev_ref[field_at, west_at], 0.0
            )
            field_ref[f, i, pl.ds(HALO, rows), :] = factor[f] * own[f]
            field_ref[f, i, pl.ds(HALO + rows, HALO), :] = factor[f] * jnp.where(
                east_ok, next_ref[field_at, east_at], 0.0
            )

    chunk = 16
    lane = lax.broadcasted_iota(jnp.int32, (chunk, lanes), 1)
    first_lane = lane == 0
    last_lane = lane == lanes - 1

    def substep(strength, src_ref, dst_ref):
        for i in range(tiles):
            south_at = south_ref[i]
            north_at = north_ref[i]
            for start in range(0, total, chunk):
                rows_at = pl.ds(PAD + start, chunk)
                current = src_ref[i, rows_at, :]
                south_tile = src_ref[south_at, rows_at, :]
                north_tile = src_ref[north_at, rows_at, :]
                from_west = src_ref[i, pl.ds(PAD + start - 1, chunk), :]
                from_east = src_ref[i, pl.ds(PAD + start + 1, chunk), :]
                from_south = pltpu.roll(jnp.where(last_lane, south_tile, current), 1, 1)
                from_north = pltpu.roll(jnp.where(first_lane, north_tile, current), lanes - 1, 1)
                diffusivity = field_ref[0, i, pl.ds(start, chunk), :]
                half_speed_x = field_ref[1, i, pl.ds(start, chunk), :]
                half_speed_y = field_ref[2, i, pl.ds(start, chunk), :]
                open_cells = field_ref[3, i, pl.ds(start, chunk), :]
                laplace = from_west + from_east + from_south + from_north - 4.0 * current
                half_transport = half_speed_x * (from_east - from_west) + half_speed_y * (
                    from_north - from_south
                )
                dst_ref[i, rows_at, :] = open_cells * (
                    current + strength * diffusivity * laplace - half_transport
                )

    def substep_pair(p, carry):
        substep(scale_ref[2 * p], state_ref, other_ref)
        substep(scale_ref[2 * p + 1], other_ref, state_ref)
        return carry

    lax.fori_loop(0, SUB // 2, substep_pair, 0)
    final_ref = state_ref
    if SUB % 2:
        substep(scale_ref[SUB - 1], state_ref, other_ref)
        final_ref = other_ref
    half_rows = rows // 2
    for i in range(tiles):
        out_ref[i] = final_ref[i, pl.ds(PAD + HALO, rows), :]
        even = final_ref[i, pl.ds(PAD + HALO, half_rows, stride=2), :]
        odd = final_ref[i, pl.ds(PAD + HALO + 1, half_rows, stride=2), :]
        coarse = coarse_ref[i]
        jump_ref[i] = 0.5 * ((even - coarse) + (odd - coarse))


def fine_propagate(slice_at, u, diffusivity, velocity, obstacle, from_prev, from_next, coarse,
                   indices, scale):
    tiles, rows, lanes = u.shape
    total = rows + 2 * HALO
    vmem = pltpu.MemorySpace.VMEM
    smem = pltpu.MemorySpace.SMEM
    return pl.pallas_call(
        functools.partial(fine_kernel, slice_at),
        out_shape=(
            jax.ShapeDtypeStruct(u.shape, u.dtype),
            jax.ShapeDtypeStruct(coarse.shape, coarse.dtype),
        ),
        in_specs=[pl.BlockSpec(memory_space=smem)] * 7 + [pl.BlockSpec(memory_space=vmem)] * 7,
        out_specs=(pl.BlockSpec(memory_space=vmem), pl.BlockSpec(memory_space=vmem)),
        scratch_shapes=[
            pltpu.VMEM((tiles + 1, total + 2 * PAD, lanes), jnp.float32),
            pltpu.VMEM((tiles + 1, total + 2 * PAD, lanes), jnp.float32),
            pltpu.VMEM((4, tiles, total, lanes), jnp.float32),
        ],
        compiler_params=pltpu.CompilerParams(vmem_limit_bytes=48 * 1024 * 1024),
    )(*indices, scale, u, diffusivity, velocity, obstacle, from_prev, from_next, coarse)


def payload_kernel(starts_hbm, diffusivity_hbm, velocity_hbm, obstacle_hbm, low_ref, high_ref,
                   obstacle_rows, sems):
    slices = starts_hbm.shape[0]
    rows = starts_hbm.shape[2]
    copies = []
    for side, (out_ref, first) in enumerate(((low_ref, 0), (high_ref, rows - HALO))):
        part = pl.ds(first, HALO)
        sources = [starts_hbm.at[n, :, part, :] for n in range(slices)]
        sources += [
            diffusivity_hbm.at[:, part, :],
            velocity_hbm.at[0, :, part, :],
            velocity_hbm.at[1, :, part, :],
        ]
        for k, source in enumerate(sources):
            copies.append(pltpu.make_async_copy(source, out_ref.at[k], sems.at[side, k]))
        copies.append(
            pltpu.make_async_copy(
                obstacle_hbm.at[:, part, :], obstacle_rows.at[side], sems.at[side, len(sources)]
            )
        )
    for copy in copies:
        copy.start()
    for copy in copies:
        copy.wait()
    for side, out_ref in enumerate((low_ref, high_ref)):
        out_ref[slices + 3] = 1.0 - obstacle_rows[side].astype(jnp.float32)


def edge_payload(starts, diffusivity, velocity, obstacle):
    slices, tiles, rows, lanes = starts.shape
    shape = jax.ShapeDtypeStruct((slices + 4, tiles, HALO, lanes), jnp.float32)
    vmem = pltpu.MemorySpace.VMEM
    return pl.pallas_call(
        payload_kernel,
        out_shape=(shape, shape),
        in_specs=[pl.BlockSpec(memory_space=pl.ANY)] * 4,
        out_specs=(pl.BlockSpec(memory_space=vmem), pl.BlockSpec(memory_space=vmem)),
        scratch_shapes=[
            pltpu.VMEM((2, tiles, HALO, lanes), jnp.int32),
            pltpu.SemaphoreType.DMA((2, slices + 4)),
        ],
    )(starts, diffusivity, velocity, obstacle)


def on_device(
    starts, diffusivity, velocity, obstacle, substep_scale, neighbors, coarse_x, coarse_y
):
    slice_count = starts.shape[0]
    tile_count = starts.shape[1]
    rows = starts.shape[2]
    all_tiles = tile_count * lax.axis_size("space")
    block_base = lax.axis_index("space") * tile_count

    low_rows, high_rows = edge_payload(starts, diffusivity, velocity, obstacle)
    space_count = lax.axis_size("space")
    forward = [(i, i + 1) for i in range(space_count - 1)]
    backward = [(i + 1, i) for i in range(space_count - 1)]
    from_prev = lax.ppermute(high_rows, "space", forward)
    from_next = lax.ppermute(low_rows, "space", backward)
    west_nb = neighbors[:, 0]
    east_nb = neighbors[:, 1]
    west_ok = (west_nb != all_tiles).astype(jnp.int32)
    east_ok = (east_nb != all_tiles).astype(jnp.int32)
    west_at = jnp.clip(west_nb - (block_base - tile_count), 0, tile_count - 1) * west_ok
    east_at = jnp.clip(east_nb - (block_base + tile_count), 0, tile_count - 1) * east_ok

    south_nb = neighbors[:, 2]
    north_nb = neighbors[:, 3]
    south_ok = (south_nb != all_tiles).astype(jnp.int32)
    north_ok = (north_nb != all_tiles).astype(jnp.int32)
    south = jnp.where(south_ok > 0, jnp.clip(south_nb - block_base, 0, tile_count - 1), tile_count)
    north = jnp.where(north_ok > 0, jnp.clip(north_nb - block_base, 0, tile_count - 1), tile_count)
    indices = (south, north, west_at, east_at, west_ok, east_ok)

    restricting_x = 0.5 * jnp.repeat(coarse_x, 2, axis=2)
    coarse_of_starts = apply_coarse(starts, restricting_x, coarse_y)
    fine_results = [
        fine_propagate(
            n, starts[n], diffusivity, velocity, obstacle, from_prev, from_next,
            coarse_of_starts[n], indices, substep_scale,
        )
        for n in range(slice_count)
    ]
    fine_ends = jnp.stack([result[0] for result in fine_results], axis=0)
    coarse_jump = jnp.stack([result[1] for result in fine_results], axis=0)
    correction = fine_ends - prolong(coarse_of_starts)
    last_correction, coarse_jump = lax.optimization_barrier((correction[-1], coarse_jump))
    earlier_correction = passed_along(last_correction, "tm", 1)
    tm_index = lax.axis_index("tm")
    tm_count = lax.axis_size("tm")
    first_coarse = restrict(starts[0])

    def prefix_over_tm(total, power_x, power_y):
        distances = []
        distance = 1
        while distance < tm_count:
            distances.append(distance)
            distance *= 2
        powers = {}
        for distance in distances:
            powers[distance] = (power_x, power_y)
            power_x = jnp.einsum("tij,tjk->tik", power_x, power_x, precision=exact_precision)
            power_y = jnp.einsum("tij,tjk->tik", power_y, power_y, precision=exact_precision)
        half = total.shape[0] // 2
        parts = [(slice(0, half), distances),
                 (slice(half, None), distances[1:] + distances[:1])]
        values = [total[part] for part, _ in parts]
        for step in range(len(distances)):
            received = [passed_along(values[k], "tm", parts[k][1][step]) for k in range(2)]
            for k in range(2):
                part, order = parts[k]
                distance = order[step]
                mixed = apply_coarse(received[k], powers[distance][0][part], powers[distance][1][part])
                values[k] = values[k] + jnp.where(tm_index >= distance, mixed, 0.0)
        return jnp.concatenate(values, axis=0)

    if slice_count == 1:
        seed = jnp.where(tm_index == 0, coarse_of_starts[0], 0.0)
        reached = prefix_over_tm(coarse_jump[0] + seed, coarse_x, coarse_y)
        coarse_applied = (reached - coarse_jump[0])[None]
    else:
        shifted_jump = jnp.concatenate(
            [passed_along(coarse_jump[-1:], "tm", 1), coarse_jump[:-1]], axis=0
        )
        head = jnp.where(tm_index == 0, first_coarse[None], shifted_jump[:1])
        local = jnp.concatenate([head, shifted_jump[1:]], axis=0)
        states = [local[0]]
        for n in range(1, slice_count):
            states.append(apply_coarse(states[-1], coarse_x, coarse_y) + local[n])
        power_x = coarse_x
        power_y = coarse_y
        for n in range(1, slice_count):
            power_x = jnp.einsum("tij,tjk->tik", power_x, coarse_x, precision=exact_precision)
            power_y = jnp.einsum("tij,tjk->tik", power_y, coarse_y, precision=exact_precision)
        total = prefix_over_tm(states[-1], power_x, power_y)
        earlier = jnp.where(tm_index > 0, passed_along(total, "tm", 1), 0.0)
        own_coarse = []
        for n in range(slice_count):
            earlier = apply_coarse(earlier, coarse_x, coarse_y)
            own_coarse.append(states[n] + earlier)
        coarse_applied = apply_coarse(jnp.stack(own_coarse, axis=0), coarse_x, coarse_y)
    slice_ends = prolong(coarse_applied) + correction
    previous = prolong(passed_along(coarse_applied[-1], "tm", 1)) + earlier_correction
    first_step = jnp.where(
        lax.axis_index("tm") == 0, jnp.zeros_like(previous), previous - starts[0]
    )
    increment = jnp.concatenate([first_step[None], slice_ends[:-1] - starts[1:]], axis=0)
    return (slice_ends, increment)


def solution(mesh):
    placed = (
        P("tm", "space", None, None),
        P("space", None, None),
        P(None, "space", None, None),
        P("space", None, None),
        P(),
        P("space", None),
        P("space", None, None),
        P("space", None, None),
    )
    return jax.shard_map(
        on_device,
        mesh=mesh,
        in_specs=placed,
        out_specs=(P("tm", "space", None, None), P("tm", "space", None, None)),
        check_vma=False,
    )
```
